32 devices in a mesh: groups: 2 (over y), pool: 4 (over z), col: 2 (over x), side: 2 (over core).
Axes of the slice: x: 2, y: 2, z: 4, core: 2. Of those that a mesh axis runs over, the one named last changes fastest.
Arguments:
- tokens: bfloat16 [64, 8192], P(('groups', 'col', 'side'), 'pool'), parts along dimension 0, may hold values from -35 to 35
- attn_gain: float32 [8192], P('pool'), may hold values from 0.25 to 1.75
- w_qkv: bfloat16 [8192, 8, 1280], P('pool', ('col', 'side')), may hold values from -0.0625 to 0.0625
- w_out: bfloat16 [8192, 8192], P(('col', 'side'), 'pool'), may hold values from -0.25 to 0.25
- ffn_gain: float32 [8192], P('pool'), may hold values from 0.25 to 1.75
- w_gate: bfloat16 [8192, 14336], P('pool', ('col', 'side')), may hold values from -0.0625 to 0.0625
- w_up: bfloat16 [8192, 14336], P('pool', ('col', 'side')), may hold values from -0.0625 to 0.0625
- w_down: bfloat16 [14336, 8192], P(('col', 'side'), 'pool'), may hold values from -0.046875 to 0.046875
- kv_cache: bfloat16 [64, 256, 2, 8, 128], P(('groups', 'pool'), None, None, ('col', 'side')), parts along dimension 0, may hold values from -240 to 240
- lengths: int32 [64], P('groups'), parts along dimension 0, may hold values from 1 to 256, 4096 in all
- request_slot: int32 [64], P('groups'), parts along dimension 0, may hold values from 0 to 31, each once
- row_request: int32 [64], P('groups'), parts along dimension 0, may hold values from 0 to 31, each once
Outputs:
- layer_out: float32 [64, 8192], P(('groups', 'col', 'side'), 'pool'), parts along dimension 0
The draws below stay inside these ranges and needn't reach their ends.
There are 2 independent parts, one for each index of `groups`. The reference program is written for one: setup_inputs(seed, part) draws one part's arguments, and reference() takes and returns one part's arrays. A program takes and returns all parts, laid end to end along the dimension named above; an argument that names none is the same for every part. Nothing has to cross between parts.
Inputs may be any that keep to these rules, and one draw needn't show every extreme that they name: `lengths`: tokens in the cache of each request; over one part they sum to 4096 and one request has exactly 256. A permutation: the cache of request r is kv_cache[request_slot[r]]. A permutation: row j of tokens is request row_request[j].
All inputs are finite; a program needn't handle non-finite values.
Results may differ from the reference program's by a relative error of at most 0.009.
The reference program's roundings to bfloat16 on the way count: a program that leaves them out, or rounds other values in their place, can miss the bound.
Values may be sent and summed in bfloat16 or wider, within the bound.
No kernel may reach another device: no remote copies, remote signals or barrier semaphores. Data moves between devices by JAX's collectives and lax.ppermute only.
A program may use at most 192 MiB of HBM per device.

```python
import math
import jax
import jax.numpy as jnp
import numpy as np
from jax import lax

D = 8192
H = 64
KVH = 8
HD = 128
FF = 14336
MAXLEN = 256
QPG = 8
QKVW = 1280
R = 32
N_POOL = 4


def draw_tokens(key, part):
    base_key, row_key, col_key = jax.random.split(key, 3)
    row_scale = jnp.exp(jax.random.uniform(row_key, (R, 1), jnp.float32, math.log(0.3), math.log(3.0)))
    col_scale = 10.0 ** (0.5 * jnp.arange(D, dtype=jnp.float32) / D - 0.25)
    col_scale = col_scale[None, :] * jnp.exp(jax.random.uniform(col_key, (1, D), jnp.float32, math.log(0.6), math.log(1.6)))
    base_draw = jnp.clip(jax.random.normal(base_key, (R, D), jnp.float32), -4.0, 4.0)
    return (base_draw * row_scale * col_scale).astype(jnp.bfloat16)


def draw_kv_cache(key, part):
    base_key = jax.random.fold_in(key, 0)
    base_draw = jnp.clip(jax.random.normal(base_key, (R, MAXLEN, 2, KVH, HD), jnp.float32), -4.0, 4.0)
    return base_draw.astype(jnp.bfloat16)


def block_scale(rng, shape, cuts, smallest, largest):
    level, own = 1.0, jax.random.fold_in(rng, 6)
    for position, blocks in cuts:
        steps = jnp.exp(jax.random.uniform(jax.random.fold_in(own, position), (blocks,), jnp.float32, smallest / len(cuts), largest / len(cuts)))
        level = level * jnp.repeat(steps, shape[position] // blocks).reshape([-1 if axis == position else 1 for axis in range(len(shape))])
    return level


def split_up(amount, total, limit, skew):
    loads = [(1 << 20) // math.isqrt(standing ** skew) + 1 for standing in range(2, amount + 1)]
    rest, counts = total - limit - (amount - 1), [1] * (amount - 1)
    while rest > 0:
        movable = [i for i in range(amount - 1) if counts[i] < limit]
        pool, budget = sum([loads[i] for i in movable]), rest
        for i in movable:
            extra = min(limit - counts[i], max(1, budget * loads[i] // pool), rest)
            counts[i] = counts[i] + extra
            rest = rest - extra
    return np.array([limit] + counts)


def ragged(rng, number_of, total, limit, skew):
    if number_of == 2:
        one = jax.random.randint(rng, (), max(1, total - limit), min(limit, total - 1) + 1)
        return jnp.stack([one, total - one])
    sizes = jnp.asarray(split_up(number_of, total, limit, skew), jnp.int32)
    twos = (number_of - 1) // 2
    source_of, receiver = sizes[1:1 + 2 * twos:2], sizes[2:2 + 2 * twos:2]
    slack = jnp.minimum(source_of - 1, limit - receiver)
    shifted = jax.random.randint(jax.random.fold_in(rng, 1), (twos,), 0, 1 << 20) % (slack + 1)
    sizes = sizes.at[1:1 + 2 * twos:2].set(source_of - shifted).at[2:2 + 2 * twos:2].set(receiver + shifted)
    return sizes[jax.random.permutation(jax.random.fold_in(rng, 2), number_of)]


def scatter_about(stream_key, dims, deviation, most, cuts=(), kind=jnp.bfloat16):
    factor_of = block_scale(stream_key, dims, cuts, -0.22, 0.18) if cuts else 1.0
    entries = jax.random.normal(stream_key, dims, jnp.float32) * deviation * factor_of
    return jnp.minimum(jnp.maximum(entries, -most), most).astype(kind)


def setup_inputs(seed: int = 0, part: int = 0) -> dict:
    key_list = jax.random.split(jax.random.key(seed), 13)
    part_splits = jax.random.split(jax.random.fold_in(key_list[12], part), 13)
    return {
        "tokens": draw_tokens(jax.random.fold_in(jax.random.fold_in(key_list[12], part), 71), part),
        "attn_gain": jnp.clip(1.0 + 0.15 * jax.random.normal(key_list[1], (D,), jnp.float32), 0.25, 1.75),
        "w_qkv": scatter_about(key_list[2], (D, KVH, QKVW), D ** -0.5, 0.0625, ((0, 4), (1, 4))),
        "w_out": scatter_about(key_list[3], (H * HD, D), (H * HD // 16) ** -0.5, 0.25, ((0, 4), (1, 4))),
        "ffn_gain": jnp.clip(1.0 + 0.15 * jax.random.normal(key_list[4], (D,), jnp.float32), 0.25, 1.75),
        "w_gate": scatter_about(key_list[5], (D, FF), D ** -0.5, 0.0625, ((0, 4), (1, 4))),
        "w_up": scatter_about(key_list[6], (D, FF), D ** -0.5, 0.0625, ((0, 4), (1, 4))),
        "w_down": scatter_about(key_list[7], (FF, D), FF ** -0.5, 0.046875, ((0, 4), (1, 4))),
        "kv_cache": draw_kv_cache(jax.random.fold_in(jax.random.fold_in(key_list[12], part), 71), part),
        "lengths": ragged(part_splits[9], R, R * MAXLEN // 2, MAXLEN, 2).astype(jnp.int32),
        "request_slot": jax.random.permutation(part_splits[10], R).astype(jnp.int32),
        "row_request": jax.random.permutation(part_splits[11], R).astype(jnp.int32),
    }


epsilon = 1e-05
rope_base = 500000.0

def rotate(heads_in, positions):
    half_width = heads_in.shape[-1] // 2
    frequency = 1.0 / rope_base ** (jnp.arange(half_width, dtype=jnp.float32) * 2.0 / heads_in.shape[-1])
    angles = positions.astype(jnp.float32)[:, None] * frequency[None, :]
    cosine_part = jnp.cos(angles)[:, None, :]
    sine_part = jnp.sin(angles)[:, None, :]
    first_half = heads_in[..., :half_width]
    second_half = heads_in[..., half_width:]
    return jnp.concatenate([first_half * cosine_part - second_half * sine_part, second_half * cosine_part + first_half * sine_part], axis=-1)

def rope_rows(qkv_sum, positions, per_group, head_dim):
    row_count = qkv_sum.shape[0]
    shaped = qkv_sum.reshape(row_count, -1, per_group + 2, head_dim)
    group_count = shaped.shape[1]
    turned = rotate(shaped[:, :, :per_group + 1].reshape(row_count, group_count * (per_group + 1), head_dim), positions)
    turned = turned.reshape(row_count, group_count, per_group + 1, head_dim)
    return jnp.concatenate([turned, shaped[:, :, per_group + 1:]], axis=2).reshape(row_count, -1).astype(jnp.bfloat16)

def attend(qkv_rot, kv_block, seen_count, per_group, head_dim):
    slot_count = qkv_rot.shape[0]
    cache_keys = kv_block[:, :, 0].astype(jnp.float32)
    values_all = kv_block[:, :, 1].astype(jnp.float32)
    shaped = qkv_rot.reshape(slot_count, cache_keys.shape[2], per_group + 2, head_dim).astype(jnp.float32)
    queries = shaped[:, :, :per_group]
    own_key = shaped[:, :, per_group]
    own_value = shaped[:, :, per_group + 1]
    score_scale = 1.0 / math.sqrt(head_dim)
    scores = jnp.einsum('sgqd,stgd->sgqt', queries, cache_keys, precision=lax.Precision.HIGHEST) * score_scale
    own_score = jnp.einsum('sgqd,sgd->sgq', queries, own_key, precision=lax.Precision.HIGHEST) * score_scale
    live_mask = (jnp.arange(cache_keys.shape[1], dtype=jnp.int32)[None, :] < seen_count[:, None])[:, None, None, :]
    peak_score = jnp.maximum(lax.optimization_barrier(jnp.max(jnp.where(live_mask, scores, -jnp.inf), axis=-1)), own_score)
    weights = jnp.where(live_mask, jnp.exp(scores - peak_score[..., None]), 0.0)
    own_weight = jnp.exp(own_score - peak_score)
    denominator = lax.optimization_barrier(jnp.sum(weights, axis=-1)) + own_weight
    prob_weights = (weights / denominator[..., None]).astype(jnp.bfloat16).astype(jnp.float32)
    own_prob = (own_weight / denominator).astype(jnp.bfloat16).astype(jnp.float32)
    mixture = jnp.einsum('sgqt,stgd->sgqd', prob_weights, values_all, precision=lax.Precision.HIGHEST)
    mixture = mixture + own_prob[..., None] * own_value[:, :, None, :]
    return mixture.reshape(slot_count, -1).astype(jnp.bfloat16)

def normalize(residual, gain):
    squares = lax.optimization_barrier(jnp.sum(residual * residual, axis=1, keepdims=True))
    return (residual * lax.rsqrt(squares / D + epsilon) * gain[None, :]).astype(jnp.bfloat16)

def reference(tokens, attn_gain, w_qkv, w_out, ffn_gain, w_gate, w_up, w_down, kv_cache, lengths, request_slot, row_request):
    rows_total = tokens.shape[0]
    slot_of_row = jnp.take(request_slot, row_request).astype(jnp.int32)
    row_of_slot = jnp.argsort(slot_of_row).astype(jnp.int32)
    length_of_row = jnp.take(lengths, row_request).astype(jnp.int32)
    length_of_slot = jnp.take(length_of_row, row_of_slot)
    residual = tokens.astype(jnp.float32)
    attn_normed = normalize(residual, attn_gain)
    qkv_sum = jnp.dot(attn_normed, w_qkv.reshape(D, -1), preferred_element_type=jnp.float32)
    qkv_rot = rope_rows(qkv_sum, length_of_row, QPG, HD)
    attended = attend(jnp.take(qkv_rot, row_of_slot, axis=0), kv_cache, length_of_slot, QPG, HD)
    attended = jnp.take(attended, slot_of_row, axis=0)
    resid_mid = residual + jnp.dot(attended, w_out, preferred_element_type=jnp.float32)
    ffn_normed = normalize(resid_mid, ffn_gain)
    blocks = ffn_normed.reshape(rows_total, N_POOL, D // N_POOL).transpose(1, 0, 2)
    gate_blocks = w_gate.reshape(N_POOL, D // N_POOL, FF)
    up_blocks = w_up.reshape(N_POOL, D // N_POOL, FF)

    def add_block(carry, pieces):
        gate_sum, up_sum = carry
        rows_block, gate_piece, up_piece = pieces
        gate_term = jnp.dot(rows_block, gate_piece, preferred_element_type=jnp.float32).astype(jnp.bfloat16)
        up_term = jnp.dot(rows_block, up_piece, preferred_element_type=jnp.float32).astype(jnp.bfloat16)
        gate_term, up_term = lax.optimization_barrier((gate_term, up_term))
        return ((gate_sum + gate_term.astype(jnp.float32), up_sum + up_term.astype(jnp.float32)), None)
    zero_block = jnp.zeros((rows_total, FF), jnp.float32)
    (gate_total, up_total), _ = lax.scan(add_block, (zero_block, zero_block), (blocks, gate_blocks, up_blocks))
    hidden = (jax.nn.silu(gate_total) * up_total).astype(jnp.bfloat16)
    return resid_mid + jnp.dot(hidden, w_down, preferred_element_type=jnp.float32)
```

```python
import math

import jax
import jax.numpy as jnp
from jax import lax
from jax.sharding import PartitionSpec as P

D = 8192
H = 64
KVH = 8
HD = 128


epsilon = 1e-05
rope_base = 500000.0
CS = ("col", "side")


def rotate(heads_in, positions):
    half_width = heads_in.shape[-1] // 2
    frequency = 1.0 / rope_base ** (
        jnp.arange(half_width, dtype=jnp.float32) * 2.0 / heads_in.shape[-1]
    )
    angles = positions.astype(jnp.float32)[:, None] * frequency[None, :]
    cosine_part = jnp.cos(angles)[:, None, :]
    sine_part = jnp.sin(angles)[:, None, :]
    first_half = heads_in[..., :half_width]
    second_half = heads_in[..., half_width:]
    return jnp.concatenate(
        [
            first_half * cosine_part - second_half * sine_part,
            second_half * cosine_part + first_half * sine_part,
        ],
        axis=-1,
    )


def rope_rows(qkv_sum, positions, per_group, head_dim):
    row_count = qkv_sum.shape[0]
    shaped = qkv_sum.reshape(row_count, -1, per_group + 2, head_dim)
    group_count = shaped.shape[1]
    turned = rotate(
        shaped[:, :, : per_group + 1].reshape(row_count, group_count * (per_group + 1), head_dim),
        positions,
    )
    turned = turned.reshape(row_count, group_count, per_group + 1, head_dim)
    return (
        jnp.concatenate([turned, shaped[:, :, per_group + 1 :]], axis=2)
        .reshape(row_count, -1)
        .astype(jnp.bfloat16)
    )


def attend(qkv_rot, kv_block, seen_count, per_group, head_dim):
    slot_count = qkv_rot.shape[0]
    cache_keys = kv_block[:, :, 0]
    values_all = kv_block[:, :, 1]
    shaped = qkv_rot.reshape(slot_count, cache_keys.shape[2], per_group + 2, head_dim)
    queries = shaped[:, :, :per_group]
    own_key = shaped[:, :, per_group]
    own_value = shaped[:, :, per_group + 1]
    score_scale = 1.0 / math.sqrt(head_dim)
    scores = (
        jnp.einsum("sgqd,stgd->sgqt", queries, cache_keys, preferred_element_type=jnp.float32)
        * score_scale
    )
    own_score = (
        jnp.einsum("sgqd,sgd->sgq", queries, own_key, preferred_element_type=jnp.float32)
        * score_scale
    )
    live_mask = (jnp.arange(cache_keys.shape[1], dtype=jnp.int32)[None, :] < seen_count[:, None])[
        :, None, None, :
    ]
    peak_score = jnp.maximum(jnp.max(jnp.where(live_mask, scores, -jnp.inf), axis=-1), own_score)
    weights = jnp.where(live_mask, jnp.exp(scores - peak_score[..., None]), 0.0)
    own_weight = jnp.exp(own_score - peak_score)
    denominator = jnp.sum(weights, axis=-1) + own_weight
    prob_weights = (weights / denominator[..., None]).astype(jnp.bfloat16)
    own_prob = (own_weight / denominator).astype(jnp.bfloat16)
    mixture = jnp.einsum(
        "sgqt,stgd->sgqd", prob_weights, values_all, preferred_element_type=jnp.float32
    )
    mixture = (
        mixture
        + own_prob.astype(jnp.float32)[..., None] * own_value.astype(jnp.float32)[:, :, None, :]
    )
    return mixture.reshape(slot_count, -1).astype(jnp.bfloat16)


def shift_pairs(n, k):
    return [(i, (i + k) % n) for i in range(n)]


def gather_blocks(x, axis, n):
    idx = lax.axis_index(axis)
    got = [x] + [lax.ppermute(x, axis, shift_pairs(n, k)) for k in range(1, n)]
    stacked = jnp.stack(got)
    return jnp.take(stacked, (idx - jnp.arange(n)) % n, axis=0)


def scatter_sum(blocks, axis, n):
    idx = lax.axis_index(axis)
    total = jnp.take(blocks, idx, axis=0).astype(jnp.float32)
    for k in range(1, n):
        piece = jnp.take(blocks, (idx + k) % n, axis=0)
        total = total + lax.ppermute(piece, axis, shift_pairs(n, k)).astype(jnp.float32)
    return total


def all_sum(x, axis, n):
    total = x
    for k in range(1, n):
        total = total + lax.ppermute(x, axis, shift_pairs(n, k))
    return total


def local(
    tokens,
    attn_gain,
    w_qkv,
    w_out,
    ffn_gain,
    w_gate,
    w_up,
    w_down,
    kv_cache,
    lengths,
    request_slot,
    row_request,
):
    n_pool = lax.axis_size("pool")
    n_cs = lax.axis_size(CS)
    pool_index = lax.axis_index("pool")
    per_owner = kv_cache.shape[0]
    per_group = H // KVH
    rows_here = tokens.shape[0]
    rows_total = rows_here * n_cs
    my_start = pool_index * per_owner
    slot_of_row = jnp.take(request_slot, row_request)
    row_of_slot = jnp.zeros_like(slot_of_row).at[slot_of_row].set(
        jnp.arange(rows_total, dtype=slot_of_row.dtype)
    )
    length_of_row = jnp.take(lengths, row_request)
    length_of_slot = jnp.take(length_of_row, row_of_slot)

    residual = tokens.astype(jnp.float32)
    squares = all_sum(jnp.sum(residual * residual, axis=1), "pool", n_pool)
    normed = (residual * lax.rsqrt(squares / D + epsilon)[:, None] * attn_gain[None, :]).astype(
        jnp.bfloat16
    )
    normed_all = gather_blocks(normed, CS, n_cs).reshape(rows_total, -1)
    by_slot = jnp.take(normed_all, row_of_slot, axis=0)
    qkv_part = jnp.dot(by_slot, w_qkv.reshape(w_qkv.shape[0], -1), preferred_element_type=jnp.float32)
    summed = scatter_sum(qkv_part.reshape(n_pool, per_owner, -1), "pool", n_pool)
    positions = lax.dynamic_slice_in_dim(length_of_slot, my_start, per_owner, 0)
    rotated = rope_rows(summed, positions, per_group, HD)
    attended = attend(rotated, kv_cache, positions, per_group, HD)
    gathered = gather_blocks(attended, "pool", n_pool).reshape(rows_total, -1)
    by_row = jnp.take(gathered, slot_of_row, axis=0)
    out_part = jnp.dot(by_row, w_out, preferred_element_type=jnp.float32)
    residual = residual + scatter_sum(out_part.reshape(n_cs, rows_here, -1), CS, n_cs)

    squares_mid = all_sum(jnp.sum(residual * residual, axis=1), "pool", n_pool)
    ffn_normed = (
        residual * lax.rsqrt(squares_mid / D + epsilon)[:, None] * ffn_gain[None, :]
    ).astype(jnp.bfloat16)
    ffn_all = gather_blocks(ffn_normed, CS, n_cs).reshape(rows_total, -1)
    gate_part = jnp.dot(ffn_all, w_gate, preferred_element_type=jnp.float32).astype(jnp.bfloat16)
    up_part = jnp.dot(ffn_all, w_up, preferred_element_type=jnp.float32).astype(jnp.bfloat16)
    hidden_cols = w_gate.shape[1]
    chunk = hidden_cols // n_pool
    gate_blocks = gate_part.reshape(rows_total, n_pool, chunk).transpose(1, 0, 2)
    up_blocks = up_part.reshape(rows_total, n_pool, chunk).transpose(1, 0, 2)
    both = scatter_sum(jnp.concatenate([gate_blocks, up_blocks], axis=2), "pool", n_pool)
    gate_total = both[:, :chunk]
    up_total = both[:, chunk:]
    hidden = (jax.nn.silu(gate_total) * up_total).astype(jnp.bfloat16)
    hidden_all = gather_blocks(hidden, "pool", n_pool).transpose(1, 0, 2).reshape(rows_total, -1)
    down_part = jnp.dot(hidden_all, w_down, preferred_element_type=jnp.float32)
    return residual + scatter_sum(down_part.reshape(n_cs, rows_here, -1), CS, n_cs)


def solution(mesh):
    return jax.shard_map(
        local,
        mesh=mesh,
        in_specs=(
            P(("groups", "col", "side"), "pool"),
            P("pool"),
            P("pool", ("col", "side"), None),
            P(("col", "side"), "pool"),
            P("pool"),
            P("pool", ("col", "side")),
            P("pool", ("col", "side")),
            P(("col", "side"), "pool"),
            P(("groups", "pool"), None, None, ("col", "side"), None),
            P("groups"),
            P("groups"),
            P("groups"),
        ),
        out_specs=P(("groups", "col", "side"), "pool"),
        check_vma=False,
    )
```

```python
import math

import jax
import jax.numpy as jnp
from jax import lax
from jax.sharding import PartitionSpec as P

D = 8192
H = 64
KVH = 8
HD = 128


epsilon = 1e-05
rope_base = 500000.0
CS = ("col", "side")


def rotate(heads_in, positions):
    half_width = heads_in.shape[-1] // 2
    frequency = 1.0 / rope_base ** (
        jnp.arange(half_width, dtype=jnp.float32) * 2.0 / heads_in.shape[-1]
    )
    angles = positions.astype(jnp.float32)[:, None] * frequency[None, :]
    cosine_part = jnp.cos(angles)[:, None, :]
    sine_part = jnp.sin(angles)[:, None, :]
    first_half = heads_in[..., :half_width]
    second_half = heads_in[..., half_width:]
    return jnp.concatenate(
        [
            first_half * cosine_part - second_half * sine_part,
            second_half * cosine_part + first_half * sine_part,
        ],
        axis=-1,
    )


def rope_rows(qkv_sum, positions, per_group, head_dim):
    row_count = qkv_sum.shape[0]
    shaped = qkv_sum.reshape(row_count, -1, per_group + 2, head_dim)
    group_count = shaped.shape[1]
    turned = rotate(
        shaped[:, :, : per_group + 1].reshape(row_count, group_count * (per_group + 1), head_dim),
        positions,
    )
    turned = turned.reshape(row_count, group_count, per_group + 1, head_dim)
    return (
        jnp.concatenate([turned, shaped[:, :, per_group + 1 :]], axis=2)
        .reshape(row_count, -1)
        .astype(jnp.bfloat16)
    )


def attend(qkv_rot, kv_block, seen_count, per_group, head_dim):
    slot_count = qkv_rot.shape[0]
    cache_keys = kv_block[:, :, 0]
    values_all = kv_block[:, :, 1]
    shaped = qkv_rot.reshape(slot_count, cache_keys.shape[2], per_group + 2, head_dim)
    queries = shaped[:, :, :per_group]
    own_key = shaped[:, :, per_group]
    own_value = shaped[:, :, per_group + 1]
    score_scale = 1.0 / math.sqrt(head_dim)
    scores = (
        jnp.einsum("sgqd,stgd->sgqt", queries, cache_keys, preferred_element_type=jnp.float32)
        * score_scale
    )
    own_score = (
        jnp.einsum("sgqd,sgd->sgq", queries, own_key, preferred_element_type=jnp.float32)
        * score_scale
    )
    live_mask = (jnp.arange(cache_keys.shape[1], dtype=jnp.int32)[None, :] < seen_count[:, None])[
        :, None, None, :
    ]
    peak_score = jnp.maximum(jnp.max(jnp.where(live_mask, scores, -jnp.inf), axis=-1), own_score)
    weights = jnp.where(live_mask, jnp.exp(scores - peak_score[..., None]), 0.0)
    own_weight = jnp.exp(own_score - peak_score)
    denominator = jnp.sum(weights, axis=-1) + own_weight
    prob_weights = (weights / denominator[..., None]).astype(jnp.bfloat16)
    own_prob = (own_weight / denominator).astype(jnp.bfloat16)
    mixture = jnp.einsum(
        "sgqt,stgd->sgqd", prob_weights, values_all, preferred_element_type=jnp.float32
    )
    mixture = (
        mixture
        + own_prob.astype(jnp.float32)[..., None] * own_value.astype(jnp.float32)[:, :, None, :]
    )
    return mixture.reshape(slot_count, -1).astype(jnp.bfloat16)


def shift_pairs(n, k):
    return [(i, (i + k) % n) for i in range(n)]


def gather_blocks(x, axis, n):
    idx = lax.axis_index(axis)
    got = [x] + [lax.ppermute(x, axis, shift_pairs(n, k)) for k in range(1, n)]
    stacked = jnp.stack(got)
    return jnp.take(stacked, (idx - jnp.arange(n)) % n, axis=0)


def scatter_sum(blocks, axis, n):
    idx = lax.axis_index(axis)
    total = jnp.take(blocks, idx, axis=0).astype(jnp.float32)
    for k in range(1, n):
        piece = jnp.take(blocks, (idx + k) % n, axis=0)
        total = total + lax.ppermute(piece, axis, shift_pairs(n, k)).astype(jnp.float32)
    return total


def all_sum(x, axis, n):
    total = x
    for k in range(1, n):
        total = total + lax.ppermute(x, axis, shift_pairs(n, k))
    return total


def local(
    tokens,
    attn_gain,
    w_qkv,
    w_out,
    ffn_gain,
    w_gate,
    w_up,
    w_down,
    kv_cache,
    lengths,
    request_slot,
    row_request,
):
    n_pool = lax.axis_size("pool")
    n_cs = lax.axis_size(CS)
    pool_index = lax.axis_index("pool")
    per_owner = kv_cache.shape[0]
    per_group = H // KVH
    rows_here = tokens.shape[0]
    rows_total = rows_here * n_cs
    my_start = pool_index * per_owner
    slot_of_row = jnp.take(request_slot, row_request)
    row_of_slot = jnp.zeros_like(slot_of_row).at[slot_of_row].set(
        jnp.arange(rows_total, dtype=slot_of_row.dtype)
    )
    length_of_row = jnp.take(lengths, row_request)
    length_of_slot = jnp.take(length_of_row, row_of_slot)

    residual = tokens.astype(jnp.float32)
    squares = all_sum(jnp.sum(residual * residual, axis=1), "pool", n_pool)
    normed = (residual * lax.rsqrt(squares / D + epsilon)[:, None] * attn_gain[None, :]).astype(
        jnp.bfloat16
    )
    normed_all = gather_blocks(normed, CS, n_cs).reshape(rows_total, -1)
    by_slot = jnp.take(normed_all, row_of_slot, axis=0)
    qkv_part = jnp.einsum(
        "rf,fgc->rgc", by_slot, w_qkv, preferred_element_type=jnp.float32
    ).reshape(rows_total, -1)
    summed = scatter_sum(qkv_part.reshape(n_pool, per_owner, -1), "pool", n_pool)
    positions = lax.dynamic_slice_in_dim(length_of_slot, my_start, per_owner, 0)
    rotated = rope_rows(summed, positions, per_group, HD)
    attended = attend(rotated, kv_cache, positions, per_group, HD)
    gathered = gather_blocks(attended, "pool", n_pool).reshape(rows_total, -1)
    by_row = jnp.take(gathered, slot_of_row, axis=0)
    out_part = jnp.dot(by_row, w_out, preferred_element_type=jnp.float32)
    residual = residual + scatter_sum(out_part.reshape(n_cs, rows_here, -1), CS, n_cs)

    squares_mid = all_sum(jnp.sum(residual * residual, axis=1), "pool", n_pool)
    ffn_normed = (
        residual * lax.rsqrt(squares_mid / D + epsilon)[:, None] * ffn_gain[None, :]
    ).astype(jnp.bfloat16)
    ffn_all = gather_blocks(ffn_normed, CS, n_cs).reshape(rows_total, -1)
    gate_part = jnp.dot(ffn_all, w_gate, preferred_element_type=jnp.float32).astype(jnp.bfloat16)
    up_part = jnp.dot(ffn_all, w_up, preferred_element_type=jnp.float32).astype(jnp.bfloat16)
    hidden_cols = w_gate.shape[1]
    chunk = hidden_cols // n_pool
    gate_blocks = gate_part.reshape(rows_total, n_pool, chunk).transpose(1, 0, 2)
    up_blocks = up_part.reshape(rows_total, n_pool, chunk).transpose(1, 0, 2)
    both = scatter_sum(jnp.concatenate([gate_blocks, up_blocks], axis=2), "pool", n_pool)
    gate_total = both[:, :chunk]
    up_total = both[:, chunk:]
    hidden = (jax.nn.silu(gate_total) * up_total).astype(jnp.bfloat16)
    hidden_all = gather_blocks(hidden, "pool", n_pool).transpose(1, 0, 2).reshape(rows_total, -1)
    down_part = jnp.dot(hidden_all, w_down, preferred_element_type=jnp.float32)
    return residual + scatter_sum(down_part.reshape(n_cs, rows_here, -1), CS, n_cs)


def solution(mesh):
    return jax.shard_map(
        local,
        mesh=mesh,
        in_specs=(
            P(("groups", "col", "side"), "pool"),
            P("pool"),
            P("pool", ("col", "side"), None),
            P(("col", "side"), "pool"),
            P("pool"),
            P("pool", ("col", "side")),
            P("pool", ("col", "side")),
            P(("col", "side"), "pool"),
            P(("groups", "pool"), None, None, ("col", "side"), None),
            P("groups"),
            P("groups"),
            P("groups"),
        ),
        out_specs=P(("groups", "col", "side"), "pool"),
        check_vma=False,
    )
```

```python
import math

import jax
import jax.numpy as jnp
from jax import lax
from jax.sharding import PartitionSpec as P

D = 8192
H = 64
KVH = 8
HD = 128


epsilon = 1e-05
rope_base = 500000.0
CS = ("col", "side")


def rotate(heads_in, positions):
    half_width = heads_in.shape[-1] // 2
    frequency = 1.0 / rope_base ** (
        jnp.arange(half_width, dtype=jnp.float32) * 2.0 / heads_in.shape[-1]
    )
    angles = positions.astype(jnp.float32)[:, None] * frequency[None, :]
    cosine_part = jnp.cos(angles)[:, None, :]
    sine_part = jnp.sin(angles)[:, None, :]
    first_half = heads_in[..., :half_width]
    second_half = heads_in[..., half_width:]
    return jnp.concatenate(
        [
            first_half * cosine_part - second_half * sine_part,
            second_half * cosine_part + first_half * sine_part,
        ],
        axis=-1,
    )


def rope_rows(qkv_sum, positions, per_group, head_dim):
    row_count = qkv_sum.shape[0]
    shaped = qkv_sum.reshape(row_count, -1, per_group + 2, head_dim)
    group_count = shaped.shape[1]
    turned = rotate(
        shaped[:, :, : per_group + 1].reshape(row_count, group_count * (per_group + 1), head_dim),
        positions,
    )
    turned = turned.reshape(row_count, group_count, per_group + 1, head_dim)
    return (
        jnp.concatenate([turned, shaped[:, :, per_group + 1 :]], axis=2)
        .reshape(row_count, -1)
        .astype(jnp.bfloat16)
    )


def attend(qkv_rot, kv_block, seen_count, per_group, head_dim):
    slot_count = qkv_rot.shape[0]
    cache_keys = kv_block[:, :, 0]
    values_all = kv_block[:, :, 1]
    shaped = qkv_rot.reshape(slot_count, cache_keys.shape[2], per_group + 2, head_dim)
    queries = shaped[:, :, :per_group]
    own_key = shaped[:, :, per_group]
    own_value = shaped[:, :, per_group + 1]
    score_scale = 1.0 / math.sqrt(head_dim)
    scores = (
        jnp.einsum("sgqd,stgd->sgqt", queries, cache_keys, preferred_element_type=jnp.float32)
        * score_scale
    )
    own_score = (
        jnp.einsum("sgqd,sgd->sgq", queries, own_key, preferred_element_type=jnp.float32)
        * score_scale
    )
    live_mask = (jnp.arange(cache_keys.shape[1], dtype=jnp.int32)[None, :] < seen_count[:, None])[
        :, None, None, :
    ]
    peak_score = jnp.maximum(jnp.max(jnp.where(live_mask, scores, -jnp.inf), axis=-1), own_score)
    weights = jnp.where(live_mask, jnp.exp(scores - peak_score[..., None]), 0.0)
    own_weight = jnp.exp(own_score - peak_score)
    denominator = jnp.sum(weights, axis=-1) + own_weight
    prob_weights = (weights / denominator[..., None]).astype(jnp.bfloat16)
    own_prob = (own_weight / denominator).astype(jnp.bfloat16)
    mixture = jnp.einsum(
        "sgqt,stgd->sgqd", prob_weights, values_all, preferred_element_type=jnp.float32
    )
    mixture = (
        mixture
        + own_prob.astype(jnp.float32)[..., None] * own_value.astype(jnp.float32)[:, :, None, :]
    )
    return mixture.reshape(slot_count, -1).astype(jnp.bfloat16)


def shift_pairs(n, k):
    return [(i, (i + k) % n) for i in range(n)]


def gather_blocks(x, axis, n):
    idx = lax.axis_index(axis)
    got = [x] + [lax.ppermute(x, axis, shift_pairs(n, k)) for k in range(1, n)]
    stacked = jnp.stack(got)
    return jnp.take(stacked, (idx - jnp.arange(n)) % n, axis=0)


def scatter_sum(blocks, axis, n):
    idx = lax.axis_index(axis)
    total = jnp.take(blocks, idx, axis=0).astype(jnp.float32)
    for k in range(1, n):
        piece = jnp.take(blocks, (idx + k) % n, axis=0)
        total = total + lax.ppermute(piece, axis, shift_pairs(n, k)).astype(jnp.float32)
    return total


def all_sum(x, axis, n):
    total = x
    for k in range(1, n):
        total = total + lax.ppermute(x, axis, shift_pairs(n, k))
    return total


def scatter_matmul(x, weights, axis, n):
    idx = lax.axis_index(axis)
    chunk = weights[0].shape[1] // n

    def block(j):
        parts = [
            jnp.dot(
                x,
                lax.dynamic_slice_in_dim(w, j * chunk, chunk, 1),
                preferred_element_type=jnp.float32,
            ).astype(jnp.bfloat16)
            for w in weights
        ]
        return jnp.concatenate(parts, axis=1)

    total = None
    for k in range(1, n):
        got = lax.ppermute(block((idx + k) % n), axis, shift_pairs(n, k)).astype(jnp.float32)
        total = got if total is None else total + got
    own = block(idx).astype(jnp.float32)
    return own if total is None else own + total


def gather_matmul(x, w, axis, n):
    idx = lax.axis_index(axis)
    chunk = x.shape[1]
    acc = jnp.dot(
        x, lax.dynamic_slice_in_dim(w, idx * chunk, chunk, 0), preferred_element_type=jnp.float32
    )
    for k in range(1, n):
        got = lax.ppermute(x, axis, shift_pairs(n, k))
        rows = lax.dynamic_slice_in_dim(w, ((idx - k) % n) * chunk, chunk, 0)
        acc = acc + jnp.dot(got, rows, preferred_element_type=jnp.float32)
    return acc


def local(
    tokens,
    attn_gain,
    w_qkv,
    w_out,
    ffn_gain,
    w_gate,
    w_up,
    w_down,
    kv_cache,
    lengths,
    request_slot,
    row_request,
):
    n_pool = lax.axis_size("pool")
    n_cs = lax.axis_size(CS)
    pool_index = lax.axis_index("pool")
    per_owner = kv_cache.shape[0]
    per_group = H // KVH
    rows_here = tokens.shape[0]
    rows_total = rows_here * n_cs
    my_start = pool_index * per_owner
    slot_of_row = jnp.take(request_slot, row_request)
    row_of_slot = jnp.zeros_like(slot_of_row).at[slot_of_row].set(
        jnp.arange(rows_total, dtype=slot_of_row.dtype)
    )
    length_of_row = jnp.take(lengths, row_request)
    length_of_slot = jnp.take(length_of_row, row_of_slot)

    residual = tokens.astype(jnp.float32)
    squares = all_sum(jnp.sum(residual * residual, axis=1), "pool", n_pool)
    normed = (residual * lax.rsqrt(squares / D + epsilon)[:, None] * attn_gain[None, :]).astype(
        jnp.bfloat16
    )
    normed_all = gather_blocks(normed, CS, n_cs).reshape(rows_total, -1)
    by_slot = jnp.take(normed_all, row_of_slot, axis=0)
    qkv_part = jnp.einsum(
        "rf,fgc->rgc", by_slot, w_qkv, preferred_element_type=jnp.float32
    ).reshape(rows_total, -1)
    summed = scatter_sum(qkv_part.reshape(n_pool, per_owner, -1), "pool", n_pool)
    positions = lax.dynamic_slice_in_dim(length_of_slot, my_start, per_owner, 0)
    rotated = rope_rows(summed, positions, per_group, HD)
    attended = attend(rotated, kv_cache, positions, per_group, HD)
    gathered = gather_blocks(attended, "pool", n_pool).reshape(rows_total, -1)
    by_row = jnp.take(gathered, slot_of_row, axis=0)
    out_part = jnp.dot(by_row, w_out, preferred_element_type=jnp.float32)
    residual = residual + scatter_sum(out_part.reshape(n_cs, rows_here, -1), CS, n_cs)

    squares_mid = all_sum(jnp.sum(residual * residual, axis=1), "pool", n_pool)
    ffn_normed = (
        residual * lax.rsqrt(squares_mid / D + epsilon)[:, None] * ffn_gain[None, :]
    ).astype(jnp.bfloat16)
    ffn_all = gather_blocks(ffn_normed, CS, n_cs).reshape(rows_total, -1)
    both = scatter_matmul(ffn_all, (w_gate, w_up), "pool", n_pool)
    chunk = w_gate.shape[1] // n_pool
    gate_total = both[:, :chunk]
    up_total = both[:, chunk:]
    hidden = (jax.nn.silu(gate_total) * up_total).astype(jnp.bfloat16)
    down_part = gather_matmul(hidden, w_down, "pool", n_pool)
    return residual + scatter_sum(down_part.reshape(n_cs, rows_here, -1), CS, n_cs)


def solution(mesh):
    return jax.shard_map(
        local,
        mesh=mesh,
        in_specs=(
            P(("groups", "col", "side"), "pool"),
            P("pool"),
            P("pool", ("col", "side"), None),
            P(("col", "side"), "pool"),
            P("pool"),
            P("pool", ("col", "side")),
            P("pool", ("col", "side")),
            P(("col", "side"), "pool"),
            P(("groups", "pool"), None, None, ("col", "side"), None),
            P("groups"),
            P("groups"),
            P("groups"),
        ),
        out_specs=P(("groups", "col", "side"), "pool"),
        check_vma=False,
    )
```

```python
import math

import jax
import jax.numpy as jnp
from jax import lax
from jax.sharding import PartitionSpec as P

D = 8192
H = 64
KVH = 8
HD = 128


epsilon = 1e-05
rope_base = 500000.0
CS = ("col", "side")


def rotate(heads_in, positions):
    half_width = heads_in.shape[-1] // 2
    frequency = 1.0 / rope_base ** (
        jnp.arange(half_width, dtype=jnp.float32) * 2.0 / heads_in.shape[-1]
    )
    angles = positions.astype(jnp.float32)[:, None] * frequency[None, :]
    cosine_part = jnp.cos(angles)[:, None, :]
    sine_part = jnp.sin(angles)[:, None, :]
    first_half = heads_in[..., :half_width]
    second_half = heads_in[..., half_width:]
    return jnp.concatenate(
        [
            first_half * cosine_part - second_half * sine_part,
            second_half * cosine_part + first_half * sine_part,
        ],
        axis=-1,
    )


def rope_rows(qkv_sum, positions, per_group, head_dim):
    row_count = qkv_sum.shape[0]
    shaped = qkv_sum.reshape(row_count, -1, per_group + 2, head_dim)
    group_count = shaped.shape[1]
    turned = rotate(
        shaped[:, :, : per_group + 1].reshape(row_count, group_count * (per_group + 1), head_dim),
        positions,
    )
    turned = turned.reshape(row_count, group_count, per_group + 1, head_dim)
    return (
        jnp.concatenate([turned, shaped[:, :, per_group + 1 :]], axis=2)
        .reshape(row_count, -1)
        .astype(jnp.bfloat16)
    )


def attend(qkv_rot, kv_block, seen_count, per_group, head_dim):
    slot_count = qkv_rot.shape[0]
    cache_keys = kv_block[:, :, 0]
    values_all = kv_block[:, :, 1]
    shaped = qkv_rot.reshape(slot_count, cache_keys.shape[2], per_group + 2, head_dim)
    queries = shaped[:, :, :per_group]
    own_key = shaped[:, :, per_group]
    own_value = shaped[:, :, per_group + 1]
    score_scale = 1.0 / math.sqrt(head_dim)
    scores = (
        jnp.einsum("sgqd,stgd->sgqt", queries, cache_keys, preferred_element_type=jnp.float32)
        * score_scale
    )
    own_score = (
        jnp.einsum("sgqd,sgd->sgq", queries, own_key, preferred_element_type=jnp.float32)
        * score_scale
    )
    live_mask = (jnp.arange(cache_keys.shape[1], dtype=jnp.int32)[None, :] < seen_count[:, None])[
        :, None, None, :
    ]
    peak_score = jnp.maximum(jnp.max(jnp.where(live_mask, scores, -jnp.inf), axis=-1), own_score)
    weights = jnp.where(live_mask, jnp.exp(scores - peak_score[..., None]), 0.0)
    own_weight = jnp.exp(own_score - peak_score)
    denominator = jnp.sum(weights, axis=-1) + own_weight
    prob_weights = (weights / denominator[..., None]).astype(jnp.bfloat16)
    own_prob = (own_weight / denominator).astype(jnp.bfloat16)
    mixture = jnp.einsum(
        "sgqt,stgd->sgqd", prob_weights, values_all, preferred_element_type=jnp.float32
    )
    mixture = (
        mixture
        + own_prob.astype(jnp.float32)[..., None] * own_value.astype(jnp.float32)[:, :, None, :]
    )
    return mixture.reshape(slot_count, -1).astype(jnp.bfloat16)


def shift_pairs(n, k):
    return [(i, (i + k) % n) for i in range(n)]


def gather_blocks(x, axis, n):
    idx = lax.axis_index(axis)
    got = [x] + [lax.ppermute(x, axis, shift_pairs(n, k)) for k in range(1, n)]
    stacked = jnp.stack(got)
    return jnp.take(stacked, (idx - jnp.arange(n)) % n, axis=0)


def scatter_sum(blocks, axis, n):
    idx = lax.axis_index(axis)
    total = jnp.take(blocks, idx, axis=0).astype(jnp.float32)
    for k in range(1, n):
        piece = jnp.take(blocks, (idx + k) % n, axis=0)
        total = total + lax.ppermute(piece, axis, shift_pairs(n, k)).astype(jnp.float32)
    return total


def all_sum(x, axis, n):
    total = x
    for k in range(1, n):
        total = total + lax.ppermute(x, axis, shift_pairs(n, k))
    return total


def gather_matmul(x, w, axis, n):
    idx = lax.axis_index(axis)
    chunk = x.shape[1]
    acc = jnp.dot(
        x, lax.dynamic_slice_in_dim(w, idx * chunk, chunk, 0), preferred_element_type=jnp.float32
    )
    for k in range(1, n):
        got = lax.ppermute(x, axis, shift_pairs(n, k))
        rows = lax.dynamic_slice_in_dim(w, ((idx - k) % n) * chunk, chunk, 0)
        acc = acc + jnp.dot(got, rows, preferred_element_type=jnp.float32)
    return acc


def local(
    tokens,
    attn_gain,
    w_qkv,
    w_out,
    ffn_gain,
    w_gate,
    w_up,
    w_down,
    kv_cache,
    lengths,
    request_slot,
    row_request,
):
    n_pool = lax.axis_size("pool")
    n_cs = lax.axis_size(CS)
    pool_index = lax.axis_index("pool")
    per_owner = kv_cache.shape[0]
    per_group = H // KVH
    rows_here = tokens.shape[0]
    rows_total = rows_here * n_cs
    my_start = pool_index * per_owner
    slot_of_row = jnp.take(request_slot, row_request)
    row_of_slot = jnp.zeros_like(slot_of_row).at[slot_of_row].set(
        jnp.arange(rows_total, dtype=slot_of_row.dtype)
    )
    length_of_row = jnp.take(lengths, row_request)
    length_of_slot = jnp.take(length_of_row, row_of_slot)

    residual = tokens.astype(jnp.float32)
    squares = all_sum(jnp.sum(residual * residual, axis=1), "pool", n_pool)
    normed = (residual * lax.rsqrt(squares / D + epsilon)[:, None] * attn_gain[None, :]).astype(
        jnp.bfloat16
    )
    normed_all = gather_blocks(normed, CS, n_cs).reshape(rows_total, -1)
    by_slot = jnp.take(normed_all, row_of_slot, axis=0)
    qkv_part = jnp.einsum(
        "rf,fgc->rgc", by_slot, w_qkv, preferred_element_type=jnp.float32
    ).reshape(rows_total, -1)
    summed = scatter_sum(qkv_part.reshape(n_pool, per_owner, -1), "pool", n_pool)
    positions = lax.dynamic_slice_in_dim(length_of_slot, my_start, per_owner, 0)
    rotated = rope_rows(summed, positions, per_group, HD)
    attended = attend(rotated, kv_cache, positions, per_group, HD)
    gathered = gather_blocks(attended, "pool", n_pool).reshape(rows_total, -1)
    by_row = jnp.take(gathered, slot_of_row, axis=0)
    out_part = jnp.dot(by_row, w_out, preferred_element_type=jnp.float32)
    residual = residual + scatter_sum(out_part.reshape(n_cs, rows_here, -1), CS, n_cs)

    squares_mid = all_sum(jnp.sum(residual * residual, axis=1), "pool", n_pool)
    ffn_normed = (
        residual * lax.rsqrt(squares_mid / D + epsilon)[:, None] * ffn_gain[None, :]
    ).astype(jnp.bfloat16)
    ffn_all = gather_blocks(ffn_normed, CS, n_cs).reshape(rows_total, -1)
    chunk = w_gate.shape[1] // n_pool
    gate_part = jnp.dot(ffn_all, w_gate, preferred_element_type=jnp.float32).astype(jnp.bfloat16)
    up_part = jnp.dot(ffn_all, w_up, preferred_element_type=jnp.float32).astype(jnp.bfloat16)
    gate_blocks = gate_part.reshape(rows_total, n_pool, chunk).transpose(1, 0, 2)
    up_blocks = up_part.reshape(rows_total, n_pool, chunk).transpose(1, 0, 2)
    both = scatter_sum(jnp.concatenate([gate_blocks, up_blocks], axis=2), "pool", n_pool)
    gate_total = both[:, :chunk]
    up_total = both[:, chunk:]
    hidden = (jax.nn.silu(gate_total) * up_total).astype(jnp.bfloat16)
    down_part = gather_matmul(hidden, w_down, "pool", n_pool)
    return residual + scatter_sum(down_part.reshape(n_cs, rows_here, -1), CS, n_cs)


def solution(mesh):
    return jax.shard_map(
        local,
        mesh=mesh,
        in_specs=(
            P(("groups", "col", "side"), "pool"),
            P("pool"),
            P("pool", ("col", "side"), None),
            P(("col", "side"), "pool"),
            P("pool"),
            P("pool", ("col", "side")),
            P("pool", ("col", "side")),
            P(("col", "side"), "pool"),
            P(("groups", "pool"), None, None, ("col", "side"), None),
            P("groups"),
            P("groups"),
            P("groups"),
        ),
        out_specs=P(("groups", "col", "side"), "pool"),
        check_vma=False,
    )
```

```python
import math

import jax
import jax.numpy as jnp
from jax import lax
from jax.sharding import PartitionSpec as P

D = 8192
H = 64
KVH = 8
HD = 128


epsilon = 1e-05
rope_base = 500000.0
CS = ("col", "side")


def rotate(heads_in, positions):
    half_width = heads_in.shape[-1] // 2
    frequency = 1.0 / rope_base ** (
        jnp.arange(half_width, dtype=jnp.float32) * 2.0 / heads_in.shape[-1]
    )
    angles = positions.astype(jnp.float32)[:, None] * frequency[None, :]
    cosine_part = jnp.cos(angles)[:, None, :]
    sine_part = jnp.sin(angles)[:, None, :]
    first_half = heads_in[..., :half_width]
    second_half = heads_in[..., half_width:]
    return jnp.concatenate(
        [
            first_half * cosine_part - second_half * sine_part,
            second_half * cosine_part + first_half * sine_part,
        ],
        axis=-1,
    )


def rope_rows(qkv_sum, positions, per_group, head_dim):
    row_count = qkv_sum.shape[0]
    shaped = qkv_sum.reshape(row_count, -1, per_group + 2, head_dim)
    group_count = shaped.shape[1]
    turned = rotate(
        shaped[:, :, : per_group + 1].reshape(row_count, group_count * (per_group + 1), head_dim),
        positions,
    )
    turned = turned.reshape(row_count, group_count, per_group + 1, head_dim)
    return (
        jnp.concatenate([turned, shaped[:, :, per_group + 1 :]], axis=2)
        .reshape(row_count, -1)
        .astype(jnp.bfloat16)
    )


def attend(qkv_rot, kv_block, seen_count, per_group, head_dim):
    slot_count = qkv_rot.shape[0]
    cache_keys = kv_block[:, :, 0]
    values_all = kv_block[:, :, 1]
    shaped = qkv_rot.reshape(slot_count, cache_keys.shape[2], per_group + 2, head_dim)
    queries = shaped[:, :, :per_group]
    own_key = shaped[:, :, per_group]
    own_value = shaped[:, :, per_group + 1]
    score_scale = 1.0 / math.sqrt(head_dim)
    scores = (
        jnp.einsum("sgqd,stgd->sgqt", queries, cache_keys, preferred_element_type=jnp.float32)
        * score_scale
    )
    own_score = (
        jnp.einsum("sgqd,sgd->sgq", queries, own_key, preferred_element_type=jnp.float32)
        * score_scale
    )
    live_mask = (jnp.arange(cache_keys.shape[1], dtype=jnp.int32)[None, :] < seen_count[:, None])[
        :, None, None, :
    ]
    peak_score = jnp.maximum(jnp.max(jnp.where(live_mask, scores, -jnp.inf), axis=-1), own_score)
    weights = jnp.where(live_mask, jnp.exp(scores - peak_score[..., None]), 0.0)
    own_weight = jnp.exp(own_score - peak_score)
    denominator = jnp.sum(weights, axis=-1) + own_weight
    prob_weights = (weights / denominator[..., None]).astype(jnp.bfloat16)
    own_prob = (own_weight / denominator).astype(jnp.bfloat16)
    mixture = jnp.einsum(
        "sgqt,stgd->sgqd", prob_weights, values_all, preferred_element_type=jnp.float32
    )
    mixture = (
        mixture
        + own_prob.astype(jnp.float32)[..., None] * own_value.astype(jnp.float32)[:, :, None, :]
    )
    return mixture.reshape(slot_count, -1).astype(jnp.bfloat16)


def shift_pairs(n, k):
    return [(i, (i + k) % n) for i in range(n)]


def gather_rows(x, axis, n, want):
    idx = lax.axis_index(axis)
    per = x.shape[0]
    got = [x] + [lax.ppermute(x, axis, shift_pairs(n, k)) for k in range(1, n)]
    stacked = jnp.concatenate(got, axis=0)
    arrival = ((idx - want // per) % n) * per + want % per
    return jnp.take(stacked, arrival, axis=0)


def pick(keys, wanted, values):
    hit = keys[None, :] == wanted[:, None]
    return jnp.sum(jnp.where(hit, values[None, :], 0), axis=1)


def scatter_sum(blocks, axis, n):
    idx = lax.axis_index(axis)
    total = jnp.take(blocks, idx, axis=0).astype(jnp.float32)
    for k in range(1, n):
        piece = jnp.take(blocks, (idx + k) % n, axis=0)
        total = total + lax.ppermute(piece, axis, shift_pairs(n, k)).astype(jnp.float32)
    return total


def all_sum(x, axis, n):
    total = x
    for k in range(1, n):
        total = total + lax.ppermute(x, axis, shift_pairs(n, k))
    return total


def gather_matmul(x, w, axis, n):
    idx = lax.axis_index(axis)
    chunk = x.shape[1]
    acc = jnp.dot(
        x, lax.dynamic_slice_in_dim(w, idx * chunk, chunk, 0), preferred_element_type=jnp.float32
    )
    for k in range(1, n):
        got = lax.ppermute(x, axis, shift_pairs(n, k))
        rows = lax.dynamic_slice_in_dim(w, ((idx - k) % n) * chunk, chunk, 0)
        acc = acc + jnp.dot(got, rows, preferred_element_type=jnp.float32)
    return acc


def local(
    tokens,
    attn_gain,
    w_qkv,
    w_out,
    ffn_gain,
    w_gate,
    w_up,
    w_down,
    kv_cache,
    lengths,
    request_slot,
    row_request,
):
    n_pool = lax.axis_size("pool")
    n_cs = lax.axis_size(CS)
    pool_index = lax.axis_index("pool")
    per_owner = kv_cache.shape[0]
    per_group = H // KVH
    rows_here = tokens.shape[0]
    rows_total = rows_here * n_cs
    my_start = pool_index * per_owner
    every = jnp.arange(rows_total, dtype=row_request.dtype)
    slot_of_row = pick(every, row_request, request_slot)
    row_of_slot = pick(slot_of_row, every, every)
    positions = pick(request_slot, my_start + jnp.arange(per_owner, dtype=row_request.dtype), lengths)

    residual = tokens.astype(jnp.float32)
    squares = all_sum(jnp.sum(residual * residual, axis=1), "pool", n_pool)
    normed = (residual * lax.rsqrt(squares / D + epsilon)[:, None] * attn_gain[None, :]).astype(
        jnp.bfloat16
    )
    by_slot = gather_rows(normed, CS, n_cs, row_of_slot)
    qkv_part = jnp.einsum(
        "rf,fgc->rgc", by_slot, w_qkv, preferred_element_type=jnp.float32
    ).reshape(rows_total, -1)
    summed = scatter_sum(qkv_part.reshape(n_pool, per_owner, -1), "pool", n_pool)
    rotated = rope_rows(summed, positions, per_group, HD)
    attended = attend(rotated, kv_cache, positions, per_group, HD)
    by_row = gather_rows(attended, "pool", n_pool, slot_of_row)
    out_part = jnp.dot(by_row, w_out, preferred_element_type=jnp.float32)
    residual = residual + scatter_sum(out_part.reshape(n_cs, rows_here, -1), CS, n_cs)

    squares_mid = all_sum(jnp.sum(residual * residual, axis=1), "pool", n_pool)
    ffn_normed = (
        residual * lax.rsqrt(squares_mid / D + epsilon)[:, None] * ffn_gain[None, :]
    ).astype(jnp.bfloat16)
    ffn_all = gather_rows(ffn_normed, CS, n_cs, every)
    chunk = w_gate.shape[1] // n_pool
    gate_part = jnp.dot(ffn_all, w_gate, preferred_element_type=jnp.float32).astype(jnp.bfloat16)
    up_part = jnp.dot(ffn_all, w_up, preferred_element_type=jnp.float32).astype(jnp.bfloat16)
    gate_blocks = gate_part.reshape(rows_total, n_pool, chunk).transpose(1, 0, 2)
    up_blocks = up_part.reshape(rows_total, n_pool, chunk).transpose(1, 0, 2)
    both = scatter_sum(jnp.concatenate([gate_blocks, up_blocks], axis=2), "pool", n_pool)
    gate_total = both[:, :chunk]
    up_total = both[:, chunk:]
    hidden = (jax.nn.silu(gate_total) * up_total).astype(jnp.bfloat16)
    down_part = gather_matmul(hidden, w_down, "pool", n_pool)
    return residual + scatter_sum(down_part.reshape(n_cs, rows_here, -1), CS, n_cs)


def solution(mesh):
    return jax.shard_map(
        local,
        mesh=mesh,
        in_specs=(
            P(("groups", "col", "side"), "pool"),
            P("pool"),
            P("pool", ("col", "side"), None),
            P(("col", "side"), "pool"),
            P("pool"),
            P("pool", ("col", "side")),
            P("pool", ("col", "side")),
            P(("col", "side"), "pool"),
            P(("groups", "pool"), None, None, ("col", "side"), None),
            P("groups"),
            P("groups"),
            P("groups"),
        ),
        out_specs=P(("groups", "col", "side"), "pool"),
        check_vma=False,
    )
```

```python
import math

import jax
import jax.numpy as jnp
from jax import lax
from jax.sharding import PartitionSpec as P

D = 8192
H = 64
KVH = 8
HD = 128


epsilon = 1e-05
rope_base = 500000.0
CS = ("col", "side")


def rotate(heads_in, positions):
    half_width = heads_in.shape[-1] // 2
    frequency = 1.0 / rope_base ** (
        jnp.arange(half_width, dtype=jnp.float32) * 2.0 / heads_in.shape[-1]
    )
    angles = positions.astype(jnp.float32)[:, None] * frequency[None, :]
    cosine_part = jnp.cos(angles)[:, None, :]
    sine_part = jnp.sin(angles)[:, None, :]
    first_half = heads_in[..., :half_width]
    second_half = heads_in[..., half_width:]
    return jnp.concatenate(
        [
            first_half * cosine_part - second_half * sine_part,
            second_half * cosine_part + first_half * sine_part,
        ],
        axis=-1,
    )


def rope_rows(qkv_sum, positions, per_group, head_dim):
    row_count = qkv_sum.shape[0]
    shaped = qkv_sum.reshape(row_count, -1, per_group + 2, head_dim)
    group_count = shaped.shape[1]
    turned = rotate(
        shaped[:, :, : per_group + 1].reshape(row_count, group_count * (per_group + 1), head_dim),
        positions,
    )
    turned = turned.reshape(row_count, group_count, per_group + 1, head_dim)
    return (
        jnp.concatenate([turned, shaped[:, :, per_group + 1 :]], axis=2)
        .reshape(row_count, -1)
        .astype(jnp.bfloat16)
    )


def attend(qkv_rot, kv_block, seen_count, per_group, head_dim):
    slot_count = qkv_rot.shape[0]
    cache_keys = kv_block[:, :, 0]
    values_all = kv_block[:, :, 1]
    shaped = qkv_rot.reshape(slot_count, cache_keys.shape[2], per_group + 2, head_dim)
    queries = shaped[:, :, :per_group]
    own_key = shaped[:, :, per_group]
    own_value = shaped[:, :, per_group + 1]
    score_scale = 1.0 / math.sqrt(head_dim)
    scores = (
        jnp.einsum("sgqd,stgd->sgqt", queries, cache_keys, preferred_element_type=jnp.float32)
        * score_scale
    )
    own_score = (
        jnp.einsum("sgqd,sgd->sgq", queries, own_key, preferred_element_type=jnp.float32)
        * score_scale
    )
    live_mask = (jnp.arange(cache_keys.shape[1], dtype=jnp.int32)[None, :] < seen_count[:, None])[
        :, None, None, :
    ]
    peak_score = jnp.maximum(jnp.max(jnp.where(live_mask, scores, -jnp.inf), axis=-1), own_score)
    weights = jnp.where(live_mask, jnp.exp(scores - peak_score[..., None]), 0.0)
    own_weight = jnp.exp(own_score - peak_score)
    denominator = jnp.sum(weights, axis=-1) + own_weight
    prob_weights = (weights / denominator[..., None]).astype(jnp.bfloat16)
    own_prob = (own_weight / denominator).astype(jnp.bfloat16)
    mixture = jnp.einsum(
        "sgqt,stgd->sgqd", prob_weights, values_all, preferred_element_type=jnp.float32
    )
    mixture = (
        mixture
        + own_prob.astype(jnp.float32)[..., None] * own_value.astype(jnp.float32)[:, :, None, :]
    )
    return mixture.reshape(slot_count, -1).astype(jnp.bfloat16)


def shift_pairs(n, k):
    return [(i, (i + k) % n) for i in range(n)]


def gather_rows(x, axis, n, want):
    idx = lax.axis_index(axis)
    per = x.shape[0]
    got = [x] + [lax.ppermute(x, axis, shift_pairs(n, k)) for k in range(1, n)]
    stacked = jnp.concatenate(got, axis=0)
    arrival = ((idx - want // per) % n) * per + want % per
    return jnp.take(stacked, arrival, axis=0)


def pick(keys, wanted, values):
    hit = keys[None, :] == wanted[:, None]
    return jnp.sum(jnp.where(hit, values[None, :], 0), axis=1)


def scatter_sum(blocks, axis, n):
    idx = lax.axis_index(axis)
    total = jnp.take(blocks, idx, axis=0).astype(jnp.float32)
    for k in range(1, n):
        piece = jnp.take(blocks, (idx + k) % n, axis=0)
        total = total + lax.ppermute(piece, axis, shift_pairs(n, k)).astype(jnp.float32)
    return total


def all_sum(x, axis, n):
    total = x
    for k in range(1, n):
        total = total + lax.ppermute(x, axis, shift_pairs(n, k))
    return total


def gather_matmul(x, w, axis, n):
    idx = lax.axis_index(axis)
    chunk = x.shape[1]
    acc = jnp.dot(
        x, lax.dynamic_slice_in_dim(w, idx * chunk, chunk, 0), preferred_element_type=jnp.float32
    )
    for k in range(1, n):
        got = lax.ppermute(x, axis, shift_pairs(n, k))
        rows = lax.dynamic_slice_in_dim(w, ((idx - k) % n) * chunk, chunk, 0)
        acc = acc + jnp.dot(got, rows, preferred_element_type=jnp.float32)
    return acc


def local(
    tokens,
    attn_gain,
    w_qkv,
    w_out,
    ffn_gain,
    w_gate,
    w_up,
    w_down,
    kv_cache,
    lengths,
    request_slot,
    row_request,
):
    n_pool = lax.axis_size("pool")
    n_cs = lax.axis_size(CS)
    pool_index = lax.axis_index("pool")
    per_owner = kv_cache.shape[0]
    per_group = H // KVH
    rows_here = tokens.shape[0]
    rows_total = rows_here * n_cs
    my_start = pool_index * per_owner
    every = jnp.arange(rows_total, dtype=row_request.dtype)
    slot_of_row = pick(every, row_request, request_slot)
    row_of_slot = pick(slot_of_row, every, every)
    positions = pick(request_slot, my_start + jnp.arange(per_owner, dtype=row_request.dtype), lengths)

    residual = tokens.astype(jnp.float32)
    squares = all_sum(jnp.sum(residual * residual, axis=1), "pool", n_pool)
    normed = (residual * lax.rsqrt(squares / D + epsilon)[:, None] * attn_gain[None, :]).astype(
        jnp.bfloat16
    )
    by_slot = gather_rows(normed, CS, n_cs, row_of_slot)
    qkv_part = jnp.einsum(
        "rf,fgc->rgc", by_slot, w_qkv, preferred_element_type=jnp.float32
    ).reshape(rows_total, -1)
    qkv_part, kv_cache = lax.optimization_barrier((qkv_part, kv_cache))
    summed = scatter_sum(qkv_part.reshape(n_pool, per_owner, -1), "pool", n_pool)
    rotated = rope_rows(summed, positions, per_group, HD)
    attended = attend(rotated, kv_cache, positions, per_group, HD)
    by_row = gather_rows(attended, "pool", n_pool, slot_of_row)
    out_part = jnp.dot(by_row, w_out, preferred_element_type=jnp.float32)
    residual = residual + scatter_sum(out_part.reshape(n_cs, rows_here, -1), CS, n_cs)

    squares_mid = all_sum(jnp.sum(residual * residual, axis=1), "pool", n_pool)
    ffn_normed = (
        residual * lax.rsqrt(squares_mid / D + epsilon)[:, None] * ffn_gain[None, :]
    ).astype(jnp.bfloat16)
    ffn_all = gather_rows(ffn_normed, CS, n_cs, every)
    chunk = w_gate.shape[1] // n_pool
    gate_part = jnp.dot(ffn_all, w_gate, preferred_element_type=jnp.float32).astype(jnp.bfloat16)
    up_part = jnp.dot(ffn_all, w_up, preferred_element_type=jnp.float32).astype(jnp.bfloat16)
    gate_blocks = gate_part.reshape(rows_total, n_pool, chunk).transpose(1, 0, 2)
    up_blocks = up_part.reshape(rows_total, n_pool, chunk).transpose(1, 0, 2)
    both = scatter_sum(jnp.concatenate([gate_blocks, up_blocks], axis=2), "pool", n_pool)
    gate_total = both[:, :chunk]
    up_total = both[:, chunk:]
    hidden = (jax.nn.silu(gate_total) * up_total).astype(jnp.bfloat16)
    down_part = gather_matmul(hidden, w_down, "pool", n_pool)
    return residual + scatter_sum(down_part.reshape(n_cs, rows_here, -1), CS, n_cs)


def solution(mesh):
    return jax.shard_map(
        local,
        mesh=mesh,
        in_specs=(
            P(("groups", "col", "side"), "pool"),
            P("pool"),
            P("pool", ("col", "side"), None),
            P(("col", "side"), "pool"),
            P("pool"),
            P("pool", ("col", "side")),
            P("pool", ("col", "side")),
            P(("col", "side"), "pool"),
            P(("groups", "pool"), None, None, ("col", "side"), None),
            P("groups"),
            P("groups"),
            P("groups"),
        ),
        out_specs=P(("groups", "col", "side"), "pool"),
        check_vma=False,
    )
```

```python
import math

import jax
import jax.numpy as jnp
from jax import lax
from jax.sharding import PartitionSpec as P

D = 8192
H = 64
KVH = 8
HD = 128


epsilon = 1e-05
rope_base = 500000.0
CS = ("col", "side")


def rotate(heads_in, positions):
    half_width = heads_in.shape[-1] // 2
    frequency = 1.0 / rope_base ** (
        jnp.arange(half_width, dtype=jnp.float32) * 2.0 / heads_in.shape[-1]
    )
    angles = positions.astype(jnp.float32)[:, None] * frequency[None, :]
    cosine_part = jnp.cos(angles)[:, None, :]
    sine_part = jnp.sin(angles)[:, None, :]
    first_half = heads_in[..., :half_width]
    second_half = heads_in[..., half_width:]
    return jnp.concatenate(
        [
            first_half * cosine_part - second_half * sine_part,
            second_half * cosine_part + first_half * sine_part,
        ],
        axis=-1,
    )


def rope_rows(qkv_sum, positions, per_group, head_dim):
    row_count = qkv_sum.shape[0]
    shaped = qkv_sum.reshape(row_count, -1, per_group + 2, head_dim)
    group_count = shaped.shape[1]
    turned = rotate(
        shaped[:, :, : per_group + 1].reshape(row_count, group_count * (per_group + 1), head_dim),
        positions,
    )
    turned = turned.reshape(row_count, group_count, per_group + 1, head_dim)
    return (
        jnp.concatenate([turned, shaped[:, :, per_group + 1 :]], axis=2)
        .reshape(row_count, -1)
        .astype(jnp.bfloat16)
    )


def attend(qkv_rot, kv_block, seen_count, per_group, head_dim):
    slot_count = qkv_rot.shape[0]
    cache_keys = kv_block[:, :, 0]
    values_all = kv_block[:, :, 1]
    shaped = qkv_rot.reshape(slot_count, cache_keys.shape[2], per_group + 2, head_dim)
    queries = shaped[:, :, :per_group]
    own_key = shaped[:, :, per_group]
    own_value = shaped[:, :, per_group + 1]
    score_scale = 1.0 / math.sqrt(head_dim)
    scores = (
        jnp.einsum("sgqd,stgd->sgqt", queries, cache_keys, preferred_element_type=jnp.float32)
        * score_scale
    )
    own_score = (
        jnp.einsum("sgqd,sgd->sgq", queries, own_key, preferred_element_type=jnp.float32)
        * score_scale
    )
    live_mask = (jnp.arange(cache_keys.shape[1], dtype=jnp.int32)[None, :] < seen_count[:, None])[
        :, None, None, :
    ]
    peak_score = jnp.maximum(jnp.max(jnp.where(live_mask, scores, -jnp.inf), axis=-1), own_score)
    weights = jnp.where(live_mask, jnp.exp(scores - peak_score[..., None]), 0.0)
    own_weight = jnp.exp(own_score - peak_score)
    denominator = jnp.sum(weights, axis=-1) + own_weight
    prob_weights = (weights / denominator[..., None]).astype(jnp.bfloat16)
    own_prob = (own_weight / denominator).astype(jnp.bfloat16)
    mixture = jnp.einsum(
        "sgqt,stgd->sgqd", prob_weights, values_all, preferred_element_type=jnp.float32
    )
    mixture = (
        mixture
        + own_prob.astype(jnp.float32)[..., None] * own_value.astype(jnp.float32)[:, :, None, :]
    )
    return mixture.reshape(slot_count, -1).astype(jnp.bfloat16)


def shift_pairs(n, k):
    return [(i, (i + k) % n) for i in range(n)]


def gather_rows(x, axis, n, want):
    idx = lax.axis_index(axis)
    per = x.shape[0]
    got = [x] + [lax.ppermute(x, axis, shift_pairs(n, k)) for k in range(1, n)]
    stacked = jnp.concatenate(got, axis=0)
    arrival = ((idx - want // per) % n) * per + want % per
    return jnp.take(stacked, arrival, axis=0)


def pick(keys, wanted, values):
    hit = keys[None, :] == wanted[:, None]
    return jnp.sum(jnp.where(hit, values[None, :], 0), axis=1)


def scatter_sum(blocks, axis, n):
    idx = lax.axis_index(axis)
    total = jnp.take(blocks, idx, axis=0).astype(jnp.float32)
    for k in range(1, n):
        piece = jnp.take(blocks, (idx + k) % n, axis=0)
        total = total + lax.ppermute(piece, axis, shift_pairs(n, k)).astype(jnp.float32)
    return total


def all_sum(x, axis, n):
    total = x
    for k in range(1, n):
        total = total + lax.ppermute(x, axis, shift_pairs(n, k))
    return total


def gather_matmul(x, w, axis, n):
    idx = lax.axis_index(axis)
    chunk = x.shape[1]
    acc = jnp.dot(
        x, lax.dynamic_slice_in_dim(w, idx * chunk, chunk, 0), preferred_element_type=jnp.float32
    )
    for k in range(1, n):
        got = lax.ppermute(x, axis, shift_pairs(n, k))
        rows = lax.dynamic_slice_in_dim(w, ((idx - k) % n) * chunk, chunk, 0)
        acc = acc + jnp.dot(got, rows, preferred_element_type=jnp.float32)
    return acc


def staged_matmul(x, w, axis, n):
    idx = lax.axis_index(axis)
    size = w.shape[0] // n
    turned = jnp.roll(x, -idx * size, axis=1)
    acc = None
    for k in range(n):
        rows = lax.dynamic_slice_in_dim(w, ((idx + k) % n) * size, size, 0)
        part = jnp.dot(turned[:, k * size : (k + 1) * size], rows, preferred_element_type=jnp.float32)
        acc = part if acc is None else acc + part
    return acc


def local(
    tokens,
    attn_gain,
    w_qkv,
    w_out,
    ffn_gain,
    w_gate,
    w_up,
    w_down,
    kv_cache,
    lengths,
    request_slot,
    row_request,
):
    n_pool = lax.axis_size("pool")
    n_cs = lax.axis_size(CS)
    pool_index = lax.axis_index("pool")
    per_owner = kv_cache.shape[0]
    per_group = H // KVH
    rows_here = tokens.shape[0]
    rows_total = rows_here * n_cs
    my_start = pool_index * per_owner
    every = jnp.arange(rows_total, dtype=row_request.dtype)
    slot_of_row = pick(every, row_request, request_slot)
    row_of_slot = pick(slot_of_row, every, every)
    positions = pick(request_slot, my_start + jnp.arange(per_owner, dtype=row_request.dtype), lengths)

    residual = tokens.astype(jnp.float32)
    squares = all_sum(jnp.sum(residual * residual, axis=1), "pool", n_pool)
    normed = (residual * lax.rsqrt(squares / D + epsilon)[:, None] * attn_gain[None, :]).astype(
        jnp.bfloat16
    )
    by_slot = gather_rows(normed, CS, n_cs, row_of_slot)
    qkv_part = jnp.einsum(
        "rf,fgc->rgc", by_slot, w_qkv, preferred_element_type=jnp.float32
    ).reshape(rows_total, -1)
    qkv_part, kv_cache = lax.optimization_barrier((qkv_part, kv_cache))
    summed = scatter_sum(qkv_part.reshape(n_pool, per_owner, -1), "pool", n_pool)
    rotated = rope_rows(summed, positions, per_group, HD)
    attended = attend(rotated, kv_cache, positions, per_group, HD)
    by_row = gather_rows(attended, "pool", n_pool, slot_of_row)
    out_part = staged_matmul(by_row, w_out, "pool", n_pool)
    residual = residual + scatter_sum(out_part.reshape(n_cs, rows_here, -1), CS, n_cs)

    squares_mid = all_sum(jnp.sum(residual * residual, axis=1), "pool", n_pool)
    ffn_normed = (
        residual * lax.rsqrt(squares_mid / D + epsilon)[:, None] * ffn_gain[None, :]
    ).astype(jnp.bfloat16)
    ffn_all = gather_rows(ffn_normed, CS, n_cs, every)
    chunk = w_gate.shape[1] // n_pool
    gate_part = staged_matmul(ffn_all, w_gate, "pool", n_pool).astype(jnp.bfloat16)
    up_part = staged_matmul(ffn_all, w_up, "pool", n_pool).astype(jnp.bfloat16)
    gate_blocks = gate_part.reshape(rows_total, n_pool, chunk).transpose(1, 0, 2)
    up_blocks = up_part.reshape(rows_total, n_pool, chunk).transpose(1, 0, 2)
    both = scatter_sum(jnp.concatenate([gate_blocks, up_blocks], axis=2), "pool", n_pool)
    gate_total = both[:, :chunk]
    up_total = both[:, chunk:]
    hidden = (jax.nn.silu(gate_total) * up_total).astype(jnp.bfloat16)
    down_part = gather_matmul(hidden, w_down, "pool", n_pool)
    return residual + scatter_sum(down_part.reshape(n_cs, rows_here, -1), CS, n_cs)


def solution(mesh):
    return jax.shard_map(
        local,
        mesh=mesh,
        in_specs=(
            P(("groups", "col", "side"), "pool"),
            P("pool"),
            P("pool", ("col", "side"), None),
            P(("col", "side"), "pool"),
            P("pool"),
            P("pool", ("col", "side")),
            P("pool", ("col", "side")),
            P(("col", "side"), "pool"),
            P(("groups", "pool"), None, None, ("col", "side"), None),
            P("groups"),
            P("groups"),
            P("groups"),
        ),
        out_specs=P(("groups", "col", "side"), "pool"),
        check_vma=False,
    )
```

```python
import math

import jax
import jax.numpy as jnp
from jax import lax
from jax.sharding import PartitionSpec as P

D = 8192
H = 64
KVH = 8
HD = 128


epsilon = 1e-05
rope_base = 500000.0
CS = ("col", "side")


def rotate(heads_in, positions):
    half_width = heads_in.shape[-1] // 2
    frequency = 1.0 / rope_base ** (
        jnp.arange(half_width, dtype=jnp.float32) * 2.0 / heads_in.shape[-1]
    )
    angles = positions.astype(jnp.float32)[:, None] * frequency[None, :]
    cosine_part = jnp.cos(angles)[:, None, :]
    sine_part = jnp.sin(angles)[:, None, :]
    first_half = heads_in[..., :half_width]
    second_half = heads_in[..., half_width:]
    return jnp.concatenate(
        [
            first_half * cosine_part - second_half * sine_part,
            second_half * cosine_part + first_half * sine_part,
        ],
        axis=-1,
    )


def rope_rows(qkv_sum, positions, per_group, head_dim):
    row_count = qkv_sum.shape[0]
    shaped = qkv_sum.reshape(row_count, -1, per_group + 2, head_dim)
    group_count = shaped.shape[1]
    turned = rotate(
        shaped[:, :, : per_group + 1].reshape(row_count, group_count * (per_group + 1), head_dim),
        positions,
    )
    turned = turned.reshape(row_count, group_count, per_group + 1, head_dim)
    return (
        jnp.concatenate([turned, shaped[:, :, per_group + 1 :]], axis=2)
        .reshape(row_count, -1)
        .astype(jnp.bfloat16)
    )


def attend(qkv_rot, kv_block, seen_count, per_group, head_dim):
    slot_count = qkv_rot.shape[0]
    cache_keys = kv_block[:, :, 0]
    values_all = kv_block[:, :, 1]
    shaped = qkv_rot.reshape(slot_count, cache_keys.shape[2], per_group + 2, head_dim)
    queries = shaped[:, :, :per_group]
    own_key = shaped[:, :, per_group]
    own_value = shaped[:, :, per_group + 1]
    score_scale = 1.0 / math.sqrt(head_dim)
    scores = (
        jnp.einsum("sgqd,stgd->sgqt", queries, cache_keys, preferred_element_type=jnp.float32)
        * score_scale
    )
    own_score = (
        jnp.einsum("sgqd,sgd->sgq", queries, own_key, preferred_element_type=jnp.float32)
        * score_scale
    )
    live_mask = (jnp.arange(cache_keys.shape[1], dtype=jnp.int32)[None, :] < seen_count[:, None])[
        :, None, None, :
    ]
    peak_score = jnp.maximum(jnp.max(jnp.where(live_mask, scores, -jnp.inf), axis=-1), own_score)
    weights = jnp.where(live_mask, jnp.exp(scores - peak_score[..., None]), 0.0)
    own_weight = jnp.exp(own_score - peak_score)
    denominator = jnp.sum(weights, axis=-1) + own_weight
    prob_weights = (weights / denominator[..., None]).astype(jnp.bfloat16)
    own_prob = (own_weight / denominator).astype(jnp.bfloat16)
    mixture = jnp.einsum(
        "sgqt,stgd->sgqd", prob_weights, values_all, preferred_element_type=jnp.float32
    )
    mixture = (
        mixture
        + own_prob.astype(jnp.float32)[..., None] * own_value.astype(jnp.float32)[:, :, None, :]
    )
    return mixture.reshape(slot_count, -1).astype(jnp.bfloat16)


def shift_pairs(n, k):
    return [(i, (i + k) % n) for i in range(n)]


def gather_rows(x, axis, n, want):
    idx = lax.axis_index(axis)
    per = x.shape[0]
    got = [x] + [lax.ppermute(x, axis, shift_pairs(n, k)) for k in range(1, n)]
    stacked = jnp.concatenate(got, axis=0)
    arrival = ((idx - want // per) % n) * per + want % per
    return jnp.take(stacked, arrival, axis=0)


def pick(keys, wanted, values):
    hit = keys[None, :] == wanted[:, None]
    return jnp.sum(jnp.where(hit, values[None, :], 0), axis=1)


def scatter_sum(blocks, axis, n):
    idx = lax.axis_index(axis)
    total = jnp.take(blocks, idx, axis=0).astype(jnp.float32)
    for k in range(1, n):
        piece = jnp.take(blocks, (idx + k) % n, axis=0)
        total = total + lax.ppermute(piece, axis, shift_pairs(n, k)).astype(jnp.float32)
    return total


def scatter_sum_cs(blocks):
    n_col = lax.axis_size("col")
    n_side = lax.axis_size("side")
    shaped = blocks.reshape((n_col, n_side) + blocks.shape[1:])
    per_col = scatter_sum(jnp.swapaxes(shaped, 0, 1), "side", n_side)
    return scatter_sum(per_col, "col", n_col)


def all_sum(x, axis, n):
    total = x
    for k in range(1, n):
        total = total + lax.ppermute(x, axis, shift_pairs(n, k))
    return total


def gather_matmul(x, w, axis, n):
    idx = lax.axis_index(axis)
    chunk = x.shape[1]
    acc = jnp.dot(
        x, lax.dynamic_slice_in_dim(w, idx * chunk, chunk, 0), preferred_element_type=jnp.float32
    )
    for k in range(1, n):
        got = lax.ppermute(x, axis, shift_pairs(n, k))
        rows = lax.dynamic_slice_in_dim(w, ((idx - k) % n) * chunk, chunk, 0)
        acc = acc + jnp.dot(got, rows, preferred_element_type=jnp.float32)
    return acc


def local(
    tokens,
    attn_gain,
    w_qkv,
    w_out,
    ffn_gain,
    w_gate,
    w_up,
    w_down,
    kv_cache,
    lengths,
    request_slot,
    row_request,
):
    n_pool = lax.axis_size("pool")
    n_cs = lax.axis_size(CS)
    pool_index = lax.axis_index("pool")
    per_owner = kv_cache.shape[0]
    per_group = H // KVH
    rows_here = tokens.shape[0]
    rows_total = rows_here * n_cs
    my_start = pool_index * per_owner
    every = jnp.arange(rows_total, dtype=row_request.dtype)
    slot_of_row = pick(every, row_request, request_slot)
    row_of_slot = pick(slot_of_row, every, every)
    positions = pick(request_slot, my_start + jnp.arange(per_owner, dtype=row_request.dtype), lengths)

    residual = tokens.astype(jnp.float32)
    squares = all_sum(jnp.sum(residual * residual, axis=1), "pool", n_pool)
    normed = (residual * lax.rsqrt(squares / D + epsilon)[:, None] * attn_gain[None, :]).astype(
        jnp.bfloat16
    )
    by_slot = gather_rows(normed, CS, n_cs, row_of_slot)
    qkv_part = jnp.einsum(
        "rf,fgc->rgc", by_slot, w_qkv, preferred_element_type=jnp.float32
    ).reshape(rows_total, -1)
    qkv_part, kv_cache = lax.optimization_barrier((qkv_part, kv_cache))
    summed = scatter_sum(qkv_part.reshape(n_pool, per_owner, -1), "pool", n_pool)
    rotated = rope_rows(summed, positions, per_group, HD)
    attended = attend(rotated, kv_cache, positions, per_group, HD)
    by_row = gather_rows(attended, "pool", n_pool, slot_of_row)
    out_part = jnp.dot(by_row, w_out, preferred_element_type=jnp.float32)
    residual = residual + scatter_sum_cs(out_part.reshape(n_cs, rows_here, -1))

    squares_mid = all_sum(jnp.sum(residual * residual, axis=1), "pool", n_pool)
    ffn_normed = (
        residual * lax.rsqrt(squares_mid / D + epsilon)[:, None] * ffn_gain[None, :]
    ).astype(jnp.bfloat16)
    ffn_all = gather_rows(ffn_normed, CS, n_cs, every)
    chunk = w_gate.shape[1] // n_pool
    gate_part = jnp.dot(ffn_all, w_gate, preferred_element_type=jnp.float32).astype(jnp.bfloat16)
    up_part = jnp.dot(ffn_all, w_up, preferred_element_type=jnp.float32).astype(jnp.bfloat16)
    gate_blocks = gate_part.reshape(rows_total, n_pool, chunk).transpose(1, 0, 2)
    up_blocks = up_part.reshape(rows_total, n_pool, chunk).transpose(1, 0, 2)
    both = scatter_sum(jnp.concatenate([gate_blocks, up_blocks], axis=2), "pool", n_pool)
    gate_total = both[:, :chunk]
    up_total = both[:, chunk:]
    hidden = (jax.nn.silu(gate_total) * up_total).astype(jnp.bfloat16)
    down_part = gather_matmul(hidden, w_down, "pool", n_pool)
    return residual + scatter_sum_cs(down_part.reshape(n_cs, rows_here, -1))


def solution(mesh):
    return jax.shard_map(
        local,
        mesh=mesh,
        in_specs=(
            P(("groups", "col", "side"), "pool"),
            P("pool"),
            P("pool", ("col", "side"), None),
            P(("col", "side"), "pool"),
            P("pool"),
            P("pool", ("col", "side")),
            P("pool", ("col", "side")),
            P(("col", "side"), "pool"),
            P(("groups", "pool"), None, None, ("col", "side"), None),
            P("groups"),
            P("groups"),
            P("groups"),
        ),
        out_specs=P(("groups", "col", "side"), "pool"),
        check_vma=False,
    )
```

```python
import math

import jax
import jax.numpy as jnp
from jax import lax
from jax.sharding import PartitionSpec as P

D = 8192
H = 64
KVH = 8
HD = 128


epsilon = 1e-05
rope_base = 500000.0
CS = ("col", "side")


def rotate(heads_in, positions):
    half_width = heads_in.shape[-1] // 2
    frequency = 1.0 / rope_base ** (
        jnp.arange(half_width, dtype=jnp.float32) * 2.0 / heads_in.shape[-1]
    )
    angles = positions.astype(jnp.float32)[:, None] * frequency[None, :]
    cosine_part = jnp.cos(angles)[:, None, :]
    sine_part = jnp.sin(angles)[:, None, :]
    first_half = heads_in[..., :half_width]
    second_half = heads_in[..., half_width:]
    return jnp.concatenate(
        [
            first_half * cosine_part - second_half * sine_part,
            second_half * cosine_part + first_half * sine_part,
        ],
        axis=-1,
    )


def rope_rows(qkv_sum, positions, per_group, head_dim):
    row_count = qkv_sum.shape[0]
    shaped = qkv_sum.reshape(row_count, -1, per_group + 2, head_dim)
    group_count = shaped.shape[1]
    turned = rotate(
        shaped[:, :, : per_group + 1].reshape(row_count, group_count * (per_group + 1), head_dim),
        positions,
    )
    turned = turned.reshape(row_count, group_count, per_group + 1, head_dim)
    return (
        jnp.concatenate([turned, shaped[:, :, per_group + 1 :]], axis=2)
        .reshape(row_count, -1)
        .astype(jnp.bfloat16)
    )


def attend(qkv_rot, kv_block, seen_count, per_group, head_dim):
    slot_count = qkv_rot.shape[0]
    cache_keys = kv_block[:, :, 0]
    values_all = kv_block[:, :, 1]
    shaped = qkv_rot.reshape(slot_count, cache_keys.shape[2], per_group + 2, head_dim)
    queries = shaped[:, :, :per_group]
    own_key = shaped[:, :, per_group]
    own_value = shaped[:, :, per_group + 1]
    score_scale = 1.0 / math.sqrt(head_dim)
    scores = (
        jnp.einsum("sgqd,stgd->sgqt", queries, cache_keys, preferred_element_type=jnp.float32)
        * score_scale
    )
    own_score = (
        jnp.einsum("sgqd,sgd->sgq", queries, own_key, preferred_element_type=jnp.float32)
        * score_scale
    )
    live_mask = (jnp.arange(cache_keys.shape[1], dtype=jnp.int32)[None, :] < seen_count[:, None])[
        :, None, None, :
    ]
    peak_score = jnp.maximum(jnp.max(jnp.where(live_mask, scores, -jnp.inf), axis=-1), own_score)
    weights = jnp.where(live_mask, jnp.exp(scores - peak_score[..., None]), 0.0)
    own_weight = jnp.exp(own_score - peak_score)
    denominator = jnp.sum(weights, axis=-1) + own_weight
    prob_weights = (weights / denominator[..., None]).astype(jnp.bfloat16)
    own_prob = (own_weight / denominator).astype(jnp.bfloat16)
    mixture = jnp.einsum(
        "sgqt,stgd->sgqd", prob_weights, values_all, preferred_element_type=jnp.float32
    )
    mixture = (
        mixture
        + own_prob.astype(jnp.float32)[..., None] * own_value.astype(jnp.float32)[:, :, None, :]
    )
    return mixture.reshape(slot_count, -1).astype(jnp.bfloat16)


def shift_pairs(n, k):
    return [(i, (i + k) % n) for i in range(n)]


def gather_rows(x, axis, n, want):
    idx = lax.axis_index(axis)
    per = x.shape[0]
    got = [x] + [lax.ppermute(x, axis, shift_pairs(n, k)) for k in range(1, n)]
    stacked = jnp.concatenate(got, axis=0)
    arrival = ((idx - want // per) % n) * per + want % per
    return jnp.take(stacked, arrival, axis=0)


def pick(keys, wanted, values):
    hit = keys[None, :] == wanted[:, None]
    return jnp.sum(jnp.where(hit, values[None, :], 0), axis=1)


def scatter_sum(blocks, axis, n):
    idx = lax.axis_index(axis)
    total = jnp.take(blocks, idx, axis=0).astype(jnp.float32)
    for k in range(1, n):
        piece = jnp.take(blocks, (idx + k) % n, axis=0)
        total = total + lax.ppermute(piece, axis, shift_pairs(n, k)).astype(jnp.float32)
    return total


def scatter_sum_cs(blocks):
    n_col = lax.axis_size("col")
    n_side = lax.axis_size("side")
    shaped = blocks.reshape((n_col, n_side) + blocks.shape[1:])
    per_col = scatter_sum(jnp.swapaxes(shaped, 0, 1), "side", n_side)
    return scatter_sum(per_col, "col", n_col)


def all_sum(x, axis, n):
    total = x
    for k in range(1, n):
        total = total + lax.ppermute(x, axis, shift_pairs(n, k))
    return total


def scatter_matmul(x, weights, axis, n):
    idx = lax.axis_index(axis)
    chunk = weights[0].shape[1] // n

    def block(j):
        parts = [
            jnp.dot(
                x,
                lax.dynamic_slice_in_dim(w, j * chunk, chunk, 1),
                preferred_element_type=jnp.float32,
            ).astype(jnp.bfloat16)
            for w in weights
        ]
        return jnp.concatenate(parts, axis=1)

    total = None
    for k in range(1, n):
        got = lax.ppermute(block((idx + k) % n), axis, shift_pairs(n, k)).astype(jnp.float32)
        total = got if total is None else total + got
    own = block(idx).astype(jnp.float32)
    return own if total is None else own + total


def gather_matmul(x, w, axis, n):
    idx = lax.axis_index(axis)
    chunk = x.shape[1]
    acc = jnp.dot(
        x, lax.dynamic_slice_in_dim(w, idx * chunk, chunk, 0), preferred_element_type=jnp.float32
    )
    for k in range(1, n):
        got = lax.ppermute(x, axis, shift_pairs(n, k))
        rows = lax.dynamic_slice_in_dim(w, ((idx - k) % n) * chunk, chunk, 0)
        acc = acc + jnp.dot(got, rows, preferred_element_type=jnp.float32)
    return acc


def local(
    tokens,
    attn_gain,
    w_qkv,
    w_out,
    ffn_gain,
    w_gate,
    w_up,
    w_down,
    kv_cache,
    lengths,
    request_slot,
    row_request,
):
    n_pool = lax.axis_size("pool")
    n_cs = lax.axis_size(CS)
    pool_index = lax.axis_index("pool")
    per_owner = kv_cache.shape[0]
    per_group = H // KVH
    rows_here = tokens.shape[0]
    rows_total = rows_here * n_cs
    my_start = pool_index * per_owner
    every = jnp.arange(rows_total, dtype=row_request.dtype)
    slot_of_row = pick(every, row_request, request_slot)
    row_of_slot = pick(slot_of_row, every, every)
    positions = pick(request_slot, my_start + jnp.arange(per_owner, dtype=row_request.dtype), lengths)

    residual = tokens.astype(jnp.float32)
    squares = all_sum(jnp.sum(residual * residual, axis=1), "pool", n_pool)
    normed = (residual * lax.rsqrt(squares / D + epsilon)[:, None] * attn_gain[None, :]).astype(
        jnp.bfloat16
    )
    by_slot = gather_rows(normed, CS, n_cs, row_of_slot)
    qkv_part = jnp.einsum(
        "rf,fgc->rgc", by_slot, w_qkv, preferred_element_type=jnp.float32
    ).reshape(rows_total, -1)
    qkv_part, kv_cache = lax.optimization_barrier((qkv_part, kv_cache))
    summed = scatter_sum(qkv_part.reshape(n_pool, per_owner, -1), "pool", n_pool)
    rotated = rope_rows(summed, positions, per_group, HD)
    attended = attend(rotated, kv_cache, positions, per_group, HD)
    by_row = gather_rows(attended, "pool", n_pool, slot_of_row)
    out_part = jnp.dot(by_row, w_out, preferred_element_type=jnp.float32)
    residual = residual + scatter_sum_cs(out_part.reshape(n_cs, rows_here, -1))

    squares_mid = all_sum(jnp.sum(residual * residual, axis=1), "pool", n_pool)
    ffn_normed = (
        residual * lax.rsqrt(squares_mid / D + epsilon)[:, None] * ffn_gain[None, :]
    ).astype(jnp.bfloat16)
    ffn_all = gather_rows(ffn_normed, CS, n_cs, every)
    both = scatter_matmul(ffn_all, (w_gate, w_up), "pool", n_pool)
    chunk = w_gate.shape[1] // n_pool
    gate_total = both[:, :chunk]
    up_total = both[:, chunk:]
    hidden = (jax.nn.silu(gate_total) * up_total).astype(jnp.bfloat16)
    down_part = gather_matmul(hidden, w_down, "pool", n_pool)
    return residual + scatter_sum_cs(down_part.reshape(n_cs, rows_here, -1))


def solution(mesh):
    return jax.shard_map(
        local,
        mesh=mesh,
        in_specs=(
            P(("groups", "col", "side"), "pool"),
            P("pool"),
            P("pool", ("col", "side"), None),
            P(("col", "side"), "pool"),
            P("pool"),
            P("pool", ("col", "side")),
            P("pool", ("col", "side")),
            P(("col", "side"), "pool"),
            P(("groups", "pool"), None, None, ("col", "side"), None),
            P("groups"),
            P("groups"),
            P("groups"),
        ),
        out_specs=P(("groups", "col", "side"), "pool"),
        check_vma=False,
    )
```

```python
import math

import jax
import jax.numpy as jnp
from jax import lax
from jax.sharding import PartitionSpec as P

D = 8192
H = 64
KVH = 8
HD = 128


epsilon = 1e-05
rope_base = 500000.0
CS = ("col", "side")


def rotate(heads_in, positions):
    half_width = heads_in.shape[-1] // 2
    frequency = 1.0 / rope_base ** (
        jnp.arange(half_width, dtype=jnp.float32) * 2.0 / heads_in.shape[-1]
    )
    angles = positions.astype(jnp.float32)[:, None] * frequency[None, :]
    cosine_part = jnp.cos(angles)[:, None, :]
    sine_part = jnp.sin(angles)[:, None, :]
    first_half = heads_in[..., :half_width]
    second_half = heads_in[..., half_width:]
    return jnp.concatenate(
        [
            first_half * cosine_part - second_half * sine_part,
            second_half * cosine_part + first_half * sine_part,
        ],
        axis=-1,
    )


def rope_rows(qkv_sum, positions, per_group, head_dim):
    row_count = qkv_sum.shape[0]
    shaped = qkv_sum.reshape(row_count, -1, per_group + 2, head_dim)
    group_count = shaped.shape[1]
    turned = rotate(
        shaped[:, :, : per_group + 1].reshape(row_count, group_count * (per_group + 1), head_dim),
        positions,
    )
    turned = turned.reshape(row_count, group_count, per_group + 1, head_dim)
    return (
        jnp.concatenate([turned, shaped[:, :, per_group + 1 :]], axis=2)
        .reshape(row_count, -1)
        .astype(jnp.bfloat16)
    )


def attend(qkv_rot, kv_block, seen_count, per_group, head_dim):
    slot_count = qkv_rot.shape[0]
    cache_keys = kv_block[:, :, 0]
    values_all = kv_block[:, :, 1]
    shaped = qkv_rot.reshape(slot_count, cache_keys.shape[2], per_group + 2, head_dim)
    queries = shaped[:, :, :per_group]
    own_key = shaped[:, :, per_group]
    own_value = shaped[:, :, per_group + 1]
    score_scale = 1.0 / math.sqrt(head_dim)
    scores = (
        jnp.einsum("sgqd,stgd->sgqt", queries, cache_keys, preferred_element_type=jnp.float32)
        * score_scale
    )
    own_score = (
        jnp.einsum("sgqd,sgd->sgq", queries, own_key, preferred_element_type=jnp.float32)
        * score_scale
    )
    live_mask = (jnp.arange(cache_keys.shape[1], dtype=jnp.int32)[None, :] < seen_count[:, None])[
        :, None, None, :
    ]
    peak_score = jnp.maximum(jnp.max(jnp.where(live_mask, scores, -jnp.inf), axis=-1), own_score)
    weights = jnp.where(live_mask, jnp.exp(scores - peak_score[..., None]), 0.0)
    own_weight = jnp.exp(own_score - peak_score)
    denominator = jnp.sum(weights, axis=-1) + own_weight
    prob_weights = (weights / denominator[..., None]).astype(jnp.bfloat16)
    own_prob = (own_weight / denominator).astype(jnp.bfloat16)
    mixture = jnp.einsum(
        "sgqt,stgd->sgqd", prob_weights, values_all, preferred_element_type=jnp.float32
    )
    mixture = (
        mixture
        + own_prob.astype(jnp.float32)[..., None] * own_value.astype(jnp.float32)[:, :, None, :]
    )
    return mixture.reshape(slot_count, -1).astype(jnp.bfloat16)


def shift_pairs(n, k):
    return [(i, (i + k) % n) for i in range(n)]


def gather_rows(x, axis, n, want):
    idx = lax.axis_index(axis)
    per = x.shape[0]
    got = [x] + [lax.ppermute(x, axis, shift_pairs(n, k)) for k in range(1, n)]
    stacked = jnp.concatenate(got, axis=0)
    arrival = ((idx - want // per) % n) * per + want % per
    return jnp.take(stacked, arrival, axis=0)


def pick(keys, wanted, values):
    hit = keys[None, :] == wanted[:, None]
    return jnp.sum(jnp.where(hit, values[None, :], 0), axis=1)


def scatter_sum(blocks, axis, n):
    idx = lax.axis_index(axis)
    total = jnp.take(blocks, idx, axis=0).astype(jnp.float32)
    for k in range(1, n):
        piece = jnp.take(blocks, (idx + k) % n, axis=0)
        total = total + lax.ppermute(piece, axis, shift_pairs(n, k)).astype(jnp.float32)
    return total


def scatter_sum_cs(blocks):
    n_col = lax.axis_size("col")
    n_side = lax.axis_size("side")
    shaped = blocks.reshape((n_col, n_side) + blocks.shape[1:])
    per_col = scatter_sum(jnp.swapaxes(shaped, 0, 1), "side", n_side)
    return scatter_sum(per_col, "col", n_col)


def all_sum(x, axis, n):
    total = x
    for k in range(1, n):
        total = total + lax.ppermute(x, axis, shift_pairs(n, k))
    return total


def scatter_matmul(x, weights, axis, n):
    idx = lax.axis_index(axis)
    chunk = weights[0].shape[1] // n

    def block(j):
        parts = [
            jnp.dot(
                x,
                lax.dynamic_slice_in_dim(w, j * chunk, chunk, 1),
                preferred_element_type=jnp.float32,
            ).astype(jnp.bfloat16)
            for w in weights
        ]
        return jnp.concatenate(parts, axis=1)

    total = None
    for k in range(1, n):
        got = lax.ppermute(block((idx + k) % n), axis, shift_pairs(n, k)).astype(jnp.float32)
        total = got if total is None else total + got
    own = block(idx).astype(jnp.float32)
    return own if total is None else own + total


def gather_matmul(x, w, axis, n):
    idx = lax.axis_index(axis)
    chunk = x.shape[1]
    acc = jnp.dot(
        x, lax.dynamic_slice_in_dim(w, idx * chunk, chunk, 0), preferred_element_type=jnp.float32
    )
    for k in range(1, n):
        got = lax.ppermute(x, axis, shift_pairs(n, k))
        rows = lax.dynamic_slice_in_dim(w, ((idx - k) % n) * chunk, chunk, 0)
        acc = acc + jnp.dot(got, rows, preferred_element_type=jnp.float32)
    return acc


def local(
    tokens,
    attn_gain,
    w_qkv,
    w_out,
    ffn_gain,
    w_gate,
    w_up,
    w_down,
    kv_cache,
    lengths,
    request_slot,
    row_request,
):
    n_pool = lax.axis_size("pool")
    n_cs = lax.axis_size(CS)
    pool_index = lax.axis_index("pool")
    per_owner = kv_cache.shape[0]
    per_group = H // KVH
    rows_here = tokens.shape[0]
    rows_total = rows_here * n_cs
    my_start = pool_index * per_owner
    every = jnp.arange(rows_total, dtype=row_request.dtype)
    slot_of_row = pick(every, row_request, request_slot)
    row_of_slot = pick(slot_of_row, every, every)
    positions = pick(request_slot, my_start + jnp.arange(per_owner, dtype=row_request.dtype), lengths)

    residual = tokens.astype(jnp.float32)
    squares = all_sum(jnp.sum(residual * residual, axis=1), "pool", n_pool)
    normed = (residual * lax.rsqrt(squares / D + epsilon)[:, None] * attn_gain[None, :]).astype(
        jnp.bfloat16
    )
    by_slot = gather_rows(normed, CS, n_cs, row_of_slot)
    cut = w_qkv.shape[2] // 2
    sums = []
    for cols in (slice(0, cut), slice(cut, w_qkv.shape[2])):
        qkv_part = jnp.einsum(
            "rf,fgc->rgc", by_slot, w_qkv[:, :, cols], preferred_element_type=jnp.float32
        )
        if not sums:
            qkv_part, kv_cache = lax.optimization_barrier((qkv_part, kv_cache))
        sums.append(
            scatter_sum(qkv_part.reshape((n_pool, per_owner) + qkv_part.shape[1:]), "pool", n_pool)
        )
    summed = jnp.concatenate(sums, axis=2).reshape(per_owner, -1)
    rotated = rope_rows(summed, positions, per_group, HD)
    attended = attend(rotated, kv_cache, positions, per_group, HD)
    by_row = gather_rows(attended, "pool", n_pool, slot_of_row)
    out_part = jnp.dot(by_row, w_out, preferred_element_type=jnp.float32)
    residual = residual + scatter_sum_cs(out_part.reshape(n_cs, rows_here, -1))

    squares_mid = all_sum(jnp.sum(residual * residual, axis=1), "pool", n_pool)
    ffn_normed = (
        residual * lax.rsqrt(squares_mid / D + epsilon)[:, None] * ffn_gain[None, :]
    ).astype(jnp.bfloat16)
    ffn_all = gather_rows(ffn_normed, CS, n_cs, every)
    both = scatter_matmul(ffn_all, (w_gate, w_up), "pool", n_pool)
    chunk = w_gate.shape[1] // n_pool
    gate_total = both[:, :chunk]
    up_total = both[:, chunk:]
    hidden = (jax.nn.silu(gate_total) * up_total).astype(jnp.bfloat16)
    down_part = gather_matmul(hidden, w_down, "pool", n_pool)
    return residual + scatter_sum_cs(down_part.reshape(n_cs, rows_here, -1))


def solution(mesh):
    return jax.shard_map(
        local,
        mesh=mesh,
        in_specs=(
            P(("groups", "col", "side"), "pool"),
            P("pool"),
            P("pool", ("col", "side"), None),
            P(("col", "side"), "pool"),
            P("pool"),
            P("pool", ("col", "side")),
            P("pool", ("col", "side")),
            P(("col", "side"), "pool"),
            P(("groups", "pool"), None, None, ("col", "side"), None),
            P("groups"),
            P("groups"),
            P("groups"),
        ),
        out_specs=P(("groups", "col", "side"), "pool"),
        check_vma=False,
    )
```

```python
import math

import jax
import jax.numpy as jnp
from jax import lax
from jax.sharding import PartitionSpec as P

D = 8192
H = 64
KVH = 8
HD = 128


epsilon = 1e-05
rope_base = 500000.0
CS = ("col", "side")


def rotate(heads_in, positions):
    half_width = heads_in.shape[-1] // 2
    frequency = 1.0 / rope_base ** (
        jnp.arange(half_width, dtype=jnp.float32) * 2.0 / heads_in.shape[-1]
    )
    angles = positions.astype(jnp.float32)[:, None] * frequency[None, :]
    cosine_part = jnp.cos(angles)[:, None, :]
    sine_part = jnp.sin(angles)[:, None, :]
    first_half = heads_in[..., :half_width]
    second_half = heads_in[..., half_width:]
    return jnp.concatenate(
        [
            first_half * cosine_part - second_half * sine_part,
            second_half * cosine_part + first_half * sine_part,
        ],
        axis=-1,
    )


def rope_rows(qkv_sum, positions, per_group, head_dim):
    row_count = qkv_sum.shape[0]
    shaped = qkv_sum.reshape(row_count, -1, per_group + 2, head_dim)
    group_count = shaped.shape[1]
    turned = rotate(
        shaped[:, :, : per_group + 1].reshape(row_count, group_count * (per_group + 1), head_dim),
        positions,
    )
    turned = turned.reshape(row_count, group_count, per_group + 1, head_dim)
    return (
        jnp.concatenate([turned, shaped[:, :, per_group + 1 :]], axis=2)
        .reshape(row_count, -1)
        .astype(jnp.bfloat16)
    )


def attend(qkv_rot, kv_block, seen_count, per_group, head_dim):
    slot_count = qkv_rot.shape[0]
    cache_keys = kv_block[:, :, 0]
    values_all = kv_block[:, :, 1]
    shaped = qkv_rot.reshape(slot_count, cache_keys.shape[2], per_group + 2, head_dim)
    queries = shaped[:, :, :per_group]
    own_key = shaped[:, :, per_group]
    own_value = shaped[:, :, per_group + 1]
    score_scale = 1.0 / math.sqrt(head_dim)
    scores = (
        jnp.einsum("sgqd,stgd->sgqt", queries, cache_keys, preferred_element_type=jnp.float32)
        * score_scale
    )
    own_score = (
        jnp.einsum("sgqd,sgd->sgq", queries, own_key, preferred_element_type=jnp.float32)
        * score_scale
    )
    live_mask = (jnp.arange(cache_keys.shape[1], dtype=jnp.int32)[None, :] < seen_count[:, None])[
        :, None, None, :
    ]
    peak_score = jnp.maximum(jnp.max(jnp.where(live_mask, scores, -jnp.inf), axis=-1), own_score)
    weights = jnp.where(live_mask, jnp.exp(scores - peak_score[..., None]), 0.0)
    own_weight = jnp.exp(own_score - peak_score)
    denominator = jnp.sum(weights, axis=-1) + own_weight
    prob_weights = (weights / denominator[..., None]).astype(jnp.bfloat16)
    own_prob = (own_weight / denominator).astype(jnp.bfloat16)
    mixture = jnp.einsum(
        "sgqt,stgd->sgqd", prob_weights, values_all, preferred_element_type=jnp.float32
    )
    mixture = (
        mixture
        + own_prob.astype(jnp.float32)[..., None] * own_value.astype(jnp.float32)[:, :, None, :]
    )
    return mixture.reshape(slot_count, -1).astype(jnp.bfloat16)


def shift_pairs(n, k):
    return [(i, (i + k) % n) for i in range(n)]


def gather_rows(x, axis, n, want):
    idx = lax.axis_index(axis)
    per = x.shape[0]
    got = [x] + [lax.ppermute(x, axis, shift_pairs(n, k)) for k in range(1, n)]
    stacked = jnp.concatenate(got, axis=0)
    arrival = ((idx - want // per) % n) * per + want % per
    return jnp.take(stacked, arrival, axis=0)


def pick(keys, wanted, values):
    hit = keys[None, :] == wanted[:, None]
    return jnp.sum(jnp.where(hit, values[None, :], 0), axis=1)


def scatter_sum(blocks, axis, n):
    idx = lax.axis_index(axis)
    total = jnp.take(blocks, idx, axis=0).astype(jnp.float32)
    for k in range(1, n):
        piece = jnp.take(blocks, (idx + k) % n, axis=0)
        total = total + lax.ppermute(piece, axis, shift_pairs(n, k)).astype(jnp.float32)
    return total


def scatter_sum_cs(blocks):
    n_col = lax.axis_size("col")
    n_side = lax.axis_size("side")
    shaped = blocks.reshape((n_col, n_side) + blocks.shape[1:])
    per_col = scatter_sum(jnp.swapaxes(shaped, 0, 1), "side", n_side)
    return scatter_sum(per_col, "col", n_col)


def all_sum_cs(parts):
    n_col = lax.axis_size("col")
    n_side = lax.axis_size("side")
    side = lax.axis_index("side")
    mine = scatter_sum(parts.reshape((n_side, -1) + parts.shape[1:]), "side", n_side)
    mine = all_sum(mine, "col", n_col)
    got = [mine] + [lax.ppermute(mine, "side", shift_pairs(n_side, k)) for k in range(1, n_side)]
    stacked = jnp.stack(got)
    ordered = jnp.take(stacked, (side - jnp.arange(n_side)) % n_side, axis=0)
    return ordered.reshape(parts.shape)


def all_sum(x, axis, n):
    total = x
    for k in range(1, n):
        total = total + lax.ppermute(x, axis, shift_pairs(n, k))
    return total


def scatter_matmul(x, weights, axis, n):
    idx = lax.axis_index(axis)
    chunk = weights[0].shape[1] // n

    def block(j):
        parts = [
            jnp.dot(
                x,
                lax.dynamic_slice_in_dim(w, j * chunk, chunk, 1),
                preferred_element_type=jnp.float32,
            ).astype(jnp.bfloat16)
            for w in weights
        ]
        return jnp.concatenate(parts, axis=1)

    total = None
    for k in range(1, n):
        got = lax.ppermute(block((idx + k) % n), axis, shift_pairs(n, k)).astype(jnp.float32)
        total = got if total is None else total + got
    own = block(idx).astype(jnp.float32)
    return own if total is None else own + total


def gather_matmul(x, w, axis, n):
    idx = lax.axis_index(axis)
    chunk = x.shape[1]
    acc = jnp.dot(
        x, lax.dynamic_slice_in_dim(w, idx * chunk, chunk, 0), preferred_element_type=jnp.float32
    )
    for k in range(1, n):
        got = lax.ppermute(x, axis, shift_pairs(n, k))
        rows = lax.dynamic_slice_in_dim(w, ((idx - k) % n) * chunk, chunk, 0)
        acc = acc + jnp.dot(got, rows, preferred_element_type=jnp.float32)
    return acc


def local(
    tokens,
    attn_gain,
    w_qkv,
    w_out,
    ffn_gain,
    w_gate,
    w_up,
    w_down,
    kv_cache,
    lengths,
    request_slot,
    row_request,
):
    n_pool = lax.axis_size("pool")
    n_cs = lax.axis_size(CS)
    pool_index = lax.axis_index("pool")
    per_owner = kv_cache.shape[0]
    per_group = H // KVH
    rows_here = tokens.shape[0]
    rows_total = rows_here * n_cs
    my_start = pool_index * per_owner
    every = jnp.arange(rows_total, dtype=row_request.dtype)
    slot_of_row = pick(every, row_request, request_slot)
    row_of_slot = pick(slot_of_row, every, every)
    positions = pick(request_slot, my_start + jnp.arange(per_owner, dtype=row_request.dtype), lengths)

    residual = tokens.astype(jnp.float32)
    squares = all_sum(jnp.sum(residual * residual, axis=1), "pool", n_pool)
    normed = (residual * lax.rsqrt(squares / D + epsilon)[:, None] * attn_gain[None, :]).astype(
        jnp.bfloat16
    )
    by_slot = gather_rows(normed, CS, n_cs, row_of_slot)
    qkv_part = jnp.einsum(
        "rf,fgc->rgc", by_slot, w_qkv, preferred_element_type=jnp.float32
    ).reshape(rows_total, -1)
    qkv_part, kv_cache = lax.optimization_barrier((qkv_part, kv_cache))
    summed = scatter_sum(qkv_part.reshape(n_pool, per_owner, -1), "pool", n_pool)
    rotated = rope_rows(summed, positions, per_group, HD)
    attended = attend(rotated, kv_cache, positions, per_group, HD)
    by_row = gather_rows(attended, "pool", n_pool, slot_of_row)
    out_part = jnp.dot(by_row, w_out, preferred_element_type=jnp.float32)
    cs_index = lax.axis_index(CS)
    out_part = lax.dynamic_update_slice_in_dim(
        out_part,
        lax.dynamic_slice_in_dim(out_part, cs_index * rows_here, rows_here, 0) + residual,
        cs_index * rows_here,
        0,
    )
    resid_all = all_sum_cs(out_part)
    residual = lax.dynamic_slice_in_dim(resid_all, cs_index * rows_here, rows_here, 0)

    squares_mid = all_sum(jnp.sum(resid_all * resid_all, axis=1), "pool", n_pool)
    ffn_all = (
        resid_all * lax.rsqrt(squares_mid / D + epsilon)[:, None] * ffn_gain[None, :]
    ).astype(jnp.bfloat16)
    both = scatter_matmul(ffn_all, (w_gate, w_up), "pool", n_pool)
    chunk = w_gate.shape[1] // n_pool
    gate_total = both[:, :chunk]
    up_total = both[:, chunk:]
    hidden = (jax.nn.silu(gate_total) * up_total).astype(jnp.bfloat16)
    down_part = gather_matmul(hidden, w_down, "pool", n_pool)
    return residual + scatter_sum_cs(down_part.reshape(n_cs, rows_here, -1))


def solution(mesh):
    return jax.shard_map(
        local,
        mesh=mesh,
        in_specs=(
            P(("groups", "col", "side"), "pool"),
            P("pool"),
            P("pool", ("col", "side"), None),
            P(("col", "side"), "pool"),
            P("pool"),
            P("pool", ("col", "side")),
            P("pool", ("col", "side")),
            P(("col", "side"), "pool"),
            P(("groups", "pool"), None, None, ("col", "side"), None),
            P("groups"),
            P("groups"),
            P("groups"),
        ),
        out_specs=P(("groups", "col", "side"), "pool"),
        check_vma=False,
    )
```

```python
import math

import jax
import jax.numpy as jnp
from jax import lax
from jax.sharding import PartitionSpec as P

D = 8192
H = 64
KVH = 8
HD = 128


epsilon = 1e-05
rope_base = 500000.0
CS = ("col", "side")


def rotate(heads_in, positions):
    half_width = heads_in.shape[-1] // 2
    frequency = 1.0 / rope_base ** (
        jnp.arange(half_width, dtype=jnp.float32) * 2.0 / heads_in.shape[-1]
    )
    angles = positions.astype(jnp.float32)[:, None] * frequency[None, :]
    cosine_part = jnp.cos(angles)[:, None, :]
    sine_part = jnp.sin(angles)[:, None, :]
    first_half = heads_in[..., :half_width]
    second_half = heads_in[..., half_width:]
    return jnp.concatenate(
        [
            first_half * cosine_part - second_half * sine_part,
            second_half * cosine_part + first_half * sine_part,
        ],
        axis=-1,
    )


def rope_rows(qkv_sum, positions, per_group, head_dim):
    row_count = qkv_sum.shape[0]
    shaped = qkv_sum.reshape(row_count, -1, per_group + 2, head_dim)
    group_count = shaped.shape[1]
    turned = rotate(
        shaped[:, :, : per_group + 1].reshape(row_count, group_count * (per_group + 1), head_dim),
        positions,
    )
    turned = turned.reshape(row_count, group_count, per_group + 1, head_dim)
    return (
        jnp.concatenate([turned, shaped[:, :, per_group + 1 :]], axis=2)
        .reshape(row_count, -1)
        .astype(jnp.bfloat16)
    )


def attend(qkv_rot, kv_block, seen_count, per_group, head_dim):
    slot_count = qkv_rot.shape[0]
    cache_keys = kv_block[:, :, 0]
    values_all = kv_block[:, :, 1]
    shaped = qkv_rot.reshape(slot_count, cache_keys.shape[2], per_group + 2, head_dim)
    queries = shaped[:, :, :per_group]
    own_key = shaped[:, :, per_group]
    own_value = shaped[:, :, per_group + 1]
    score_scale = 1.0 / math.sqrt(head_dim)
    scores = (
        jnp.einsum("sgqd,stgd->sgqt", queries, cache_keys, preferred_element_type=jnp.float32)
        * score_scale
    )
    own_score = (
        jnp.einsum("sgqd,sgd->sgq", queries, own_key, preferred_element_type=jnp.float32)
        * score_scale
    )
    live_mask = (jnp.arange(cache_keys.shape[1], dtype=jnp.int32)[None, :] < seen_count[:, None])[
        :, None, None, :
    ]
    peak_score = jnp.maximum(jnp.max(jnp.where(live_mask, scores, -jnp.inf), axis=-1), own_score)
    weights = jnp.where(live_mask, jnp.exp(scores - peak_score[..., None]), 0.0)
    own_weight = jnp.exp(own_score - peak_score)
    denominator = jnp.sum(weights, axis=-1) + own_weight
    prob_weights = (weights / denominator[..., None]).astype(jnp.bfloat16)
    own_prob = (own_weight / denominator).astype(jnp.bfloat16)
    mixture = jnp.einsum(
        "sgqt,stgd->sgqd", prob_weights, values_all, preferred_element_type=jnp.float32
    )
    mixture = (
        mixture
        + own_prob.astype(jnp.float32)[..., None] * own_value.astype(jnp.float32)[:, :, None, :]
    )
    return mixture.reshape(slot_count, -1).astype(jnp.bfloat16)


def shift_pairs(n, k):
    return [(i, (i + k) % n) for i in range(n)]


def gather_rows(x, axis, n, want):
    idx = lax.axis_index(axis)
    per = x.shape[0]
    got = [x] + [lax.ppermute(x, axis, shift_pairs(n, k)) for k in range(1, n)]
    stacked = jnp.concatenate(got, axis=0)
    arrival = ((idx - want // per) % n) * per + want % per
    return jnp.take(stacked, arrival, axis=0)


def pick(keys, wanted, values):
    hit = keys[None, :] == wanted[:, None]
    return jnp.sum(jnp.where(hit, values[None, :], 0), axis=1)


def scatter_sum(blocks, axis, n):
    idx = lax.axis_index(axis)
    total = jnp.take(blocks, idx, axis=0).astype(jnp.float32)
    for k in range(1, n):
        piece = jnp.take(blocks, (idx + k) % n, axis=0)
        total = total + lax.ppermute(piece, axis, shift_pairs(n, k)).astype(jnp.float32)
    return total


def scatter_sum_cs(blocks):
    n_col = lax.axis_size("col")
    n_side = lax.axis_size("side")
    shaped = blocks.reshape((n_col, n_side) + blocks.shape[1:])
    per_col = scatter_sum(jnp.swapaxes(shaped, 0, 1), "side", n_side)
    return scatter_sum(per_col, "col", n_col)


def all_sum_cs(parts):
    n_col = lax.axis_size("col")
    n_side = lax.axis_size("side")
    side = lax.axis_index("side")
    mine = scatter_sum(parts.reshape((n_side, -1) + parts.shape[1:]), "side", n_side)
    mine = all_sum(mine, "col", n_col)
    got = [mine] + [lax.ppermute(mine, "side", shift_pairs(n_side, k)) for k in range(1, n_side)]
    stacked = jnp.stack(got)
    ordered = jnp.take(stacked, (side - jnp.arange(n_side)) % n_side, axis=0)
    return ordered.reshape(parts.shape)


def all_sum(x, axis, n):
    if n & (n - 1) == 0:
        step = 1
        while step < n:
            x = x + lax.ppermute(x, axis, [(i, i ^ step) for i in range(n)])
            step *= 2
        return x
    total = x
    for k in range(1, n):
        total = total + lax.ppermute(x, axis, shift_pairs(n, k))
    return total


def scatter_matmul(x, weights, axis, n):
    idx = lax.axis_index(axis)
    chunk = weights[0].shape[1] // n

    def block(j):
        parts = [
            jnp.dot(
                x,
                lax.dynamic_slice_in_dim(w, j * chunk, chunk, 1),
                preferred_element_type=jnp.float32,
            ).astype(jnp.bfloat16)
            for w in weights
        ]
        return jnp.concatenate(parts, axis=1)

    total = None
    for k in range(1, n):
        got = lax.ppermute(block((idx + k) % n), axis, shift_pairs(n, k)).astype(jnp.float32)
        total = got if total is None else total + got
    own = block(idx).astype(jnp.float32)
    return own if total is None else own + total


def gather_matmul(x, w, axis, n):
    idx = lax.axis_index(axis)
    chunk = x.shape[1]
    acc = jnp.dot(
        x, lax.dynamic_slice_in_dim(w, idx * chunk, chunk, 0), preferred_element_type=jnp.float32
    )
    for k in range(1, n):
        got = lax.ppermute(x, axis, shift_pairs(n, k))
        rows = lax.dynamic_slice_in_dim(w, ((idx - k) % n) * chunk, chunk, 0)
        acc = acc + jnp.dot(got, rows, preferred_element_type=jnp.float32)
    return acc


def local(
    tokens,
    attn_gain,
    w_qkv,
    w_out,
    ffn_gain,
    w_gate,
    w_up,
    w_down,
    kv_cache,
    lengths,
    request_slot,
    row_request,
):
    n_pool = lax.axis_size("pool")
    n_cs = lax.axis_size(CS)
    pool_index = lax.axis_index("pool")
    per_owner = kv_cache.shape[0]
    per_group = H // KVH
    rows_here = tokens.shape[0]
    rows_total = rows_here * n_cs
    my_start = pool_index * per_owner
    every = jnp.arange(rows_total, dtype=row_request.dtype)
    slot_of_row = pick(every, row_request, request_slot)
    row_of_slot = pick(slot_of_row, every, every)
    positions = pick(request_slot, my_start + jnp.arange(per_owner, dtype=row_request.dtype), lengths)

    residual = tokens.astype(jnp.float32)
    squares = all_sum(jnp.sum(residual * residual, axis=1), "pool", n_pool)
    normed = (residual * lax.rsqrt(squares / D + epsilon)[:, None] * attn_gain[None, :]).astype(
        jnp.bfloat16
    )
    by_slot = gather_rows(normed, CS, n_cs, row_of_slot)
    qkv_part = jnp.einsum(
        "rf,fgc->rgc", by_slot, w_qkv, preferred_element_type=jnp.float32
    ).reshape(rows_total, -1)
    qkv_part, kv_cache = lax.optimization_barrier((qkv_part, kv_cache))
    summed = scatter_sum(qkv_part.reshape(n_pool, per_owner, -1), "pool", n_pool)
    rotated = rope_rows(summed, positions, per_group, HD)
    attended = attend(rotated, kv_cache, positions, per_group, HD)
    by_row = gather_rows(attended, "pool", n_pool, slot_of_row)
    out_part = jnp.dot(by_row, w_out, preferred_element_type=jnp.float32)
    cs_index = lax.axis_index(CS)
    out_part = lax.dynamic_update_slice_in_dim(
        out_part,
        lax.dynamic_slice_in_dim(out_part, cs_index * rows_here, rows_here, 0) + residual,
        cs_index * rows_here,
        0,
    )
    resid_all = all_sum_cs(out_part)
    residual = lax.dynamic_slice_in_dim(resid_all, cs_index * rows_here, rows_here, 0)

    squares_mid = all_sum(jnp.sum(resid_all * resid_all, axis=1), "pool", n_pool)
    ffn_all = (
        resid_all * lax.rsqrt(squares_mid / D + epsilon)[:, None] * ffn_gain[None, :]
    ).astype(jnp.bfloat16)
    both = scatter_matmul(ffn_all, (w_gate, w_up), "pool", n_pool)
    chunk = w_gate.shape[1] // n_pool
    gate_total = both[:, :chunk]
    up_total = both[:, chunk:]
    hidden = (jax.nn.silu(gate_total) * up_total).astype(jnp.bfloat16)
    down_part = gather_matmul(hidden, w_down, "pool", n_pool)
    return residual + scatter_sum_cs(down_part.reshape(n_cs, rows_here, -1))


def solution(mesh):
    return jax.shard_map(
        local,
        mesh=mesh,
        in_specs=(
            P(("groups", "col", "side"), "pool"),
            P("pool"),
            P("pool", ("col", "side"), None),
            P(("col", "side"), "pool"),
            P("pool"),
            P("pool", ("col", "side")),
            P("pool", ("col", "side")),
            P(("col", "side"), "pool"),
            P(("groups", "pool"), None, None, ("col", "side"), None),
            P("groups"),
            P("groups"),
            P("groups"),
        ),
        out_specs=P(("groups", "col", "side"), "pool"),
        check_vma=False,
    )
```

```python
import math

import jax
import jax.numpy as jnp
from jax import lax
from jax.sharding import PartitionSpec as P

D = 8192
H = 64
KVH = 8
HD = 128


epsilon = 1e-05
rope_base = 500000.0
CS = ("col", "side")


def rotate(heads_in, positions):
    half_width = heads_in.shape[-1] // 2
    frequency = 1.0 / rope_base ** (
        jnp.arange(half_width, dtype=jnp.float32) * 2.0 / heads_in.shape[-1]
    )
    angles = positions.astype(jnp.float32)[:, None] * frequency[None, :]
    cosine_part = jnp.cos(angles)[:, None, :]
    sine_part = jnp.sin(angles)[:, None, :]
    first_half = heads_in[..., :half_width]
    second_half = heads_in[..., half_width:]
    return jnp.concatenate(
        [
            first_half * cosine_part - second_half * sine_part,
            second_half * cosine_part + first_half * sine_part,
        ],
        axis=-1,
    )


def rope_rows(qkv_sum, positions, per_group, head_dim):
    row_count = qkv_sum.shape[0]
    shaped = qkv_sum.reshape(row_count, -1, per_group + 2, head_dim)
    group_count = shaped.shape[1]
    turned = rotate(
        shaped[:, :, : per_group + 1].reshape(row_count, group_count * (per_group + 1), head_dim),
        positions,
    )
    turned = turned.reshape(row_count, group_count, per_group + 1, head_dim)
    return (
        jnp.concatenate([turned, shaped[:, :, per_group + 1 :]], axis=2)
        .reshape(row_count, -1)
        .astype(jnp.bfloat16)
    )


def attend(qkv_rot, kv_block, seen_count, per_group, head_dim):
    slot_count = qkv_rot.shape[0]
    cache_keys = kv_block[:, :, 0]
    values_all = kv_block[:, :, 1]
    shaped = qkv_rot.reshape(slot_count, cache_keys.shape[2], per_group + 2, head_dim)
    queries = shaped[:, :, :per_group]
    own_key = shaped[:, :, per_group]
    own_value = shaped[:, :, per_group + 1]
    score_scale = 1.0 / math.sqrt(head_dim)
    scores = (
        jnp.einsum("sgqd,stgd->sgqt", queries, cache_keys, preferred_element_type=jnp.float32)
        * score_scale
    )
    own_score = (
        jnp.einsum("sgqd,sgd->sgq", queries, own_key, preferred_element_type=jnp.float32)
        * score_scale
    )
    live_mask = (jnp.arange(cache_keys.shape[1], dtype=jnp.int32)[None, :] < seen_count[:, None])[
        :, None, None, :
    ]
    peak_score = jnp.maximum(jnp.max(jnp.where(live_mask, scores, -jnp.inf), axis=-1), own_score)
    weights = jnp.where(live_mask, jnp.exp(scores - peak_score[..., None]), 0.0)
    own_weight = jnp.exp(own_score - peak_score)
    denominator = jnp.sum(weights, axis=-1) + own_weight
    prob_weights = (weights / denominator[..., None]).astype(jnp.bfloat16)
    own_prob = (own_weight / denominator).astype(jnp.bfloat16)
    mixture = jnp.einsum(
        "sgqt,stgd->sgqd", prob_weights, values_all, preferred_element_type=jnp.float32
    )
    mixture = (
        mixture
        + own_prob.astype(jnp.float32)[..., None] * own_value.astype(jnp.float32)[:, :, None, :]
    )
    return mixture.reshape(slot_count, -1).astype(jnp.bfloat16)


def shift_pairs(n, k):
    return [(i, (i + k) % n) for i in range(n)]


def gather_rows(x, axis, n, want):
    idx = lax.axis_index(axis)
    per = x.shape[0]
    got = [x] + [lax.ppermute(x, axis, shift_pairs(n, k)) for k in range(1, n)]
    stacked = jnp.concatenate(got, axis=0)
    arrival = ((idx - want // per) % n) * per + want % per
    return jnp.take(stacked, arrival, axis=0)


def pick(keys, wanted, values):
    hit = keys[None, :] == wanted[:, None]
    return jnp.sum(jnp.where(hit, values[None, :], 0), axis=1)


def scatter_sum(blocks, axis, n):
    idx = lax.axis_index(axis)
    total = jnp.take(blocks, idx, axis=0).astype(jnp.float32)
    for k in range(1, n):
        piece = jnp.take(blocks, (idx + k) % n, axis=0)
        total = total + lax.ppermute(piece, axis, shift_pairs(n, k)).astype(jnp.float32)
    return total


def scatter_sum_cs(blocks):
    n_col = lax.axis_size("col")
    n_side = lax.axis_size("side")
    shaped = blocks.reshape((n_col, n_side) + blocks.shape[1:])
    per_col = scatter_sum(jnp.swapaxes(shaped, 0, 1), "side", n_side)
    return scatter_sum(per_col, "col", n_col)


def all_sum_cs(parts):
    n_col = lax.axis_size("col")
    n_side = lax.axis_size("side")
    side = lax.axis_index("side")
    mine = scatter_sum(parts.reshape((n_side, -1) + parts.shape[1:]), "side", n_side)
    mine = all_sum(mine, "col", n_col)
    got = [mine] + [lax.ppermute(mine, "side", shift_pairs(n_side, k)) for k in range(1, n_side)]
    stacked = jnp.stack(got)
    ordered = jnp.take(stacked, (side - jnp.arange(n_side)) % n_side, axis=0)
    return ordered.reshape(parts.shape)


def all_sum(x, axis, n):
    total = x
    for k in range(1, n):
        total = total + lax.ppermute(x, axis, shift_pairs(n, k))
    return total


def scatter_matmul(x, weights, axis, n):
    idx = lax.axis_index(axis)
    chunk = weights[0].shape[1] // n

    def block(j):
        parts = [
            jnp.dot(
                x,
                lax.dynamic_slice_in_dim(w, j * chunk, chunk, 1),
                preferred_element_type=jnp.float32,
            ).astype(jnp.bfloat16)
            for w in weights
        ]
        return jnp.concatenate(parts, axis=1)

    pieces = [block((idx + k) % n) for k in range(1, n)]
    pieces, x = lax.optimization_barrier((pieces, x))
    total = None
    for k in range(1, n):
        got = lax.ppermute(pieces[k - 1], axis, shift_pairs(n, k)).astype(jnp.float32)
        total = got if total is None else total + got
    own = block(idx).astype(jnp.float32)
    return own if total is None else own + total


def gather_matmul(x, w, axis, n):
    idx = lax.axis_index(axis)
    chunk = x.shape[1]
    acc = jnp.dot(
        x, lax.dynamic_slice_in_dim(w, idx * chunk, chunk, 0), preferred_element_type=jnp.float32
    )
    for k in range(1, n):
        got = lax.ppermute(x, axis, shift_pairs(n, k))
        rows = lax.dynamic_slice_in_dim(w, ((idx - k) % n) * chunk, chunk, 0)
        acc = acc + jnp.dot(got, rows, preferred_element_type=jnp.float32)
    return acc


def local(
    tokens,
    attn_gain,
    w_qkv,
    w_out,
    ffn_gain,
    w_gate,
    w_up,
    w_down,
    kv_cache,
    lengths,
    request_slot,
    row_request,
):
    n_pool = lax.axis_size("pool")
    n_cs = lax.axis_size(CS)
    pool_index = lax.axis_index("pool")
    per_owner = kv_cache.shape[0]
    per_group = H // KVH
    rows_here = tokens.shape[0]
    rows_total = rows_here * n_cs
    my_start = pool_index * per_owner
    every = jnp.arange(rows_total, dtype=row_request.dtype)
    slot_of_row = pick(every, row_request, request_slot)
    row_of_slot = pick(slot_of_row, every, every)
    positions = pick(request_slot, my_start + jnp.arange(per_owner, dtype=row_request.dtype), lengths)

    residual = tokens.astype(jnp.float32)
    squares = all_sum(jnp.sum(residual * residual, axis=1), "pool", n_pool)
    normed = (residual * lax.rsqrt(squares / D + epsilon)[:, None] * attn_gain[None, :]).astype(
        jnp.bfloat16
    )
    by_slot = gather_rows(normed, CS, n_cs, row_of_slot)
    qkv_part = jnp.einsum(
        "rf,fgc->rgc", by_slot, w_qkv, preferred_element_type=jnp.float32
    ).reshape(rows_total, -1)
    qkv_part, kv_cache = lax.optimization_barrier((qkv_part, kv_cache))
    summed = scatter_sum(qkv_part.reshape(n_pool, per_owner, -1), "pool", n_pool)
    rotated = rope_rows(summed, positions, per_group, HD)
    attended = attend(rotated, kv_cache, positions, per_group, HD)
    by_row = gather_rows(attended, "pool", n_pool, slot_of_row)
    out_part = jnp.dot(by_row, w_out, preferred_element_type=jnp.float32)
    cs_index = lax.axis_index(CS)
    out_part = lax.dynamic_update_slice_in_dim(
        out_part,
        lax.dynamic_slice_in_dim(out_part, cs_index * rows_here, rows_here, 0) + residual,
        cs_index * rows_here,
        0,
    )
    resid_all = all_sum_cs(out_part)
    residual = lax.dynamic_slice_in_dim(resid_all, cs_index * rows_here, rows_here, 0)

    squares_mid = all_sum(jnp.sum(resid_all * resid_all, axis=1), "pool", n_pool)
    ffn_all = (
        resid_all * lax.rsqrt(squares_mid / D + epsilon)[:, None] * ffn_gain[None, :]
    ).astype(jnp.bfloat16)
    both = scatter_matmul(ffn_all, (w_gate, w_up), "pool", n_pool)
    chunk = w_gate.shape[1] // n_pool
    gate_total = both[:, :chunk]
    up_total = both[:, chunk:]
    hidden = (jax.nn.silu(gate_total) * up_total).astype(jnp.bfloat16)
    down_part = gather_matmul(hidden, w_down, "pool", n_pool)
    return residual + scatter_sum_cs(down_part.reshape(n_cs, rows_here, -1))


def solution(mesh):
    return jax.shard_map(
        local,
        mesh=mesh,
        in_specs=(
            P(("groups", "col", "side"), "pool"),
            P("pool"),
            P("pool", ("col", "side"), None),
            P(("col", "side"), "pool"),
            P("pool"),
            P("pool", ("col", "side")),
            P("pool", ("col", "side")),
            P(("col", "side"), "pool"),
            P(("groups", "pool"), None, None, ("col", "side"), None),
            P("groups"),
            P("groups"),
            P("groups"),
        ),
        out_specs=P(("groups", "col", "side"), "pool"),
        check_vma=False,
    )
```

```python
import math

import jax
import jax.numpy as jnp
from jax import lax
from jax.sharding import PartitionSpec as P

D = 8192
H = 64
KVH = 8
HD = 128


epsilon = 1e-05
rope_base = 500000.0
CS = ("col", "side")


def rotate(heads_in, positions):
    half_width = heads_in.shape[-1] // 2
    frequency = 1.0 / rope_base ** (
        jnp.arange(half_width, dtype=jnp.float32) * 2.0 / heads_in.shape[-1]
    )
    angles = positions.astype(jnp.float32)[:, None] * frequency[None, :]
    cosine_part = jnp.cos(angles)[:, None, :]
    sine_part = jnp.sin(angles)[:, None, :]
    first_half = heads_in[..., :half_width]
    second_half = heads_in[..., half_width:]
    return jnp.concatenate(
        [
            first_half * cosine_part - second_half * sine_part,
            second_half * cosine_part + first_half * sine_part,
        ],
        axis=-1,
    )


def rope_rows(qkv_sum, positions, per_group, head_dim):
    row_count = qkv_sum.shape[0]
    shaped = qkv_sum.reshape(row_count, -1, per_group + 2, head_dim)
    group_count = shaped.shape[1]
    turned = rotate(
        shaped[:, :, : per_group + 1].reshape(row_count, group_count * (per_group + 1), head_dim),
        positions,
    )
    turned = turned.reshape(row_count, group_count, per_group + 1, head_dim)
    return (
        jnp.concatenate([turned, shaped[:, :, per_group + 1 :]], axis=2)
        .reshape(row_count, -1)
        .astype(jnp.bfloat16)
    )


def attend(qkv_rot, kv_block, seen_count, per_group, head_dim):
    slot_count = qkv_rot.shape[0]
    cache_keys = kv_block[:, :, 0]
    values_all = kv_block[:, :, 1]
    shaped = qkv_rot.reshape(slot_count, cache_keys.shape[2], per_group + 2, head_dim)
    queries = shaped[:, :, :per_group]
    own_key = shaped[:, :, per_group]
    own_value = shaped[:, :, per_group + 1]
    score_scale = 1.0 / math.sqrt(head_dim)
    scores = (
        jnp.einsum("sgqd,stgd->sgqt", queries, cache_keys, preferred_element_type=jnp.float32)
        * score_scale
    )
    own_score = (
        jnp.einsum("sgqd,sgd->sgq", queries, own_key, preferred_element_type=jnp.float32)
        * score_scale
    )
    live_mask = (jnp.arange(cache_keys.shape[1], dtype=jnp.int32)[None, :] < seen_count[:, None])[
        :, None, None, :
    ]
    peak_score = jnp.maximum(jnp.max(jnp.where(live_mask, scores, -jnp.inf), axis=-1), own_score)
    weights = jnp.where(live_mask, jnp.exp(scores - peak_score[..., None]), 0.0)
    own_weight = jnp.exp(own_score - peak_score)
    denominator = jnp.sum(weights, axis=-1) + own_weight
    prob_weights = (weights / denominator[..., None]).astype(jnp.bfloat16)
    own_prob = (own_weight / denominator).astype(jnp.bfloat16)
    mixture = jnp.einsum(
        "sgqt,stgd->sgqd", prob_weights, values_all, preferred_element_type=jnp.float32
    )
    mixture = (
        mixture
        + own_prob.astype(jnp.float32)[..., None] * own_value.astype(jnp.float32)[:, :, None, :]
    )
    return mixture.reshape(slot_count, -1).astype(jnp.bfloat16)


def shift_pairs(n, k):
    return [(i, (i + k) % n) for i in range(n)]


def gather_rows(x, axis, n, want):
    idx = lax.axis_index(axis)
    per = x.shape[0]
    got = [x] + [lax.ppermute(x, axis, shift_pairs(n, k)) for k in range(1, n)]
    stacked = jnp.concatenate(got, axis=0)
    arrival = ((idx - want // per) % n) * per + want % per
    chooser = (arrival[:, None] == jnp.arange(n * per, dtype=arrival.dtype)[None, :]).astype(x.dtype)
    return jnp.dot(chooser, stacked, preferred_element_type=jnp.float32).astype(x.dtype)


def pick(keys, wanted, values):
    hit = keys[None, :] == wanted[:, None]
    return jnp.sum(jnp.where(hit, values[None, :], 0), axis=1)


def scatter_sum(blocks, axis, n):
    idx = lax.axis_index(axis)
    total = jnp.take(blocks, idx, axis=0).astype(jnp.float32)
    for k in range(1, n):
        piece = jnp.take(blocks, (idx + k) % n, axis=0)
        total = total + lax.ppermute(piece, axis, shift_pairs(n, k)).astype(jnp.float32)
    return total


def scatter_sum_cs(blocks):
    n_col = lax.axis_size("col")
    n_side = lax.axis_size("side")
    shaped = blocks.reshape((n_col, n_side) + blocks.shape[1:])
    per_col = scatter_sum(jnp.swapaxes(shaped, 0, 1), "side", n_side)
    return scatter_sum(per_col, "col", n_col)


def all_sum_cs(parts):
    n_col = lax.axis_size("col")
    n_side = lax.axis_size("side")
    side = lax.axis_index("side")
    mine = scatter_sum(parts.reshape((n_side, -1) + parts.shape[1:]), "side", n_side)
    mine = all_sum(mine, "col", n_col)
    got = [mine] + [lax.ppermute(mine, "side", shift_pairs(n_side, k)) for k in range(1, n_side)]
    ordered = [lax.select_n((side - j) % n_side, *got) for j in range(n_side)]
    return jnp.stack(ordered).reshape(parts.shape)


def all_sum(x, axis, n):
    total = x
    for k in range(1, n):
        total = total + lax.ppermute(x, axis, shift_pairs(n, k))
    return total


def scatter_matmul(x, weights, axis, n):
    idx = lax.axis_index(axis)
    chunk = weights[0].shape[1] // n

    def block(j):
        parts = [
            jnp.dot(
                x,
                lax.dynamic_slice_in_dim(w, j * chunk, chunk, 1),
                preferred_element_type=jnp.float32,
            ).astype(jnp.bfloat16)
            for w in weights
        ]
        return jnp.concatenate(parts, axis=1)

    pieces = [block((idx + k) % n) for k in range(1, n)]
    pieces, x = lax.optimization_barrier((pieces, x))
    total = None
    for k in range(1, n):
        got = lax.ppermute(pieces[k - 1], axis, shift_pairs(n, k)).astype(jnp.float32)
        total = got if total is None else total + got
    own = block(idx).astype(jnp.float32)
    return own if total is None else own + total


def gather_matmul(x, w, axis, n):
    idx = lax.axis_index(axis)
    chunk = x.shape[1]
    acc = jnp.dot(
        x, lax.dynamic_slice_in_dim(w, idx * chunk, chunk, 0), preferred_element_type=jnp.float32
    )
    for k in range(1, n):
        got = lax.ppermute(x, axis, shift_pairs(n, k))
        rows = lax.dynamic_slice_in_dim(w, ((idx - k) % n) * chunk, chunk, 0)
        acc = acc + jnp.dot(got, rows, preferred_element_type=jnp.float32)
    return acc


def local(
    tokens,
    attn_gain,
    w_qkv,
    w_out,
    ffn_gain,
    w_gate,
    w_up,
    w_down,
    kv_cache,
    lengths,
    request_slot,
    row_request,
):
    n_pool = lax.axis_size("pool")
    n_cs = lax.axis_size(CS)
    pool_index = lax.axis_index("pool")
    per_owner = kv_cache.shape[0]
    per_group = H // KVH
    rows_here = tokens.shape[0]
    rows_total = rows_here * n_cs
    my_start = pool_index * per_owner
    every = jnp.arange(rows_total, dtype=row_request.dtype)
    slot_of_row = pick(every, row_request, request_slot)
    row_of_slot = pick(slot_of_row, every, every)
    positions = pick(request_slot, my_start + jnp.arange(per_owner, dtype=row_request.dtype), lengths)

    residual = tokens.astype(jnp.float32)
    squares = all_sum(jnp.sum(residual * residual, axis=1), "pool", n_pool)
    normed = (residual * lax.rsqrt(squares / D + epsilon)[:, None] * attn_gain[None, :]).astype(
        jnp.bfloat16
    )
    by_slot = gather_rows(normed, CS, n_cs, row_of_slot)
    qkv_part = jnp.einsum(
        "rf,fgc->rgc", by_slot, w_qkv, preferred_element_type=jnp.float32
    ).reshape(rows_total, -1)
    qkv_part, kv_cache = lax.optimization_barrier((qkv_part, kv_cache))
    summed = scatter_sum(qkv_part.reshape(n_pool, per_owner, -1), "pool", n_pool)
    rotated = rope_rows(summed, positions, per_group, HD)
    attended = attend(rotated, kv_cache, positions, per_group, HD)
    by_row = gather_rows(attended, "pool", n_pool, slot_of_row)
    out_part = jnp.dot(by_row, w_out, preferred_element_type=jnp.float32)
    cs_index = lax.axis_index(CS)
    out_part = lax.dynamic_update_slice_in_dim(
        out_part,
        lax.dynamic_slice_in_dim(out_part, cs_index * rows_here, rows_here, 0) + residual,
        cs_index * rows_here,
        0,
    )
    resid_all = all_sum_cs(out_part)
    residual = lax.dynamic_slice_in_dim(resid_all, cs_index * rows_here, rows_here, 0)

    squares_mid = all_sum(jnp.sum(resid_all * resid_all, axis=1), "pool", n_pool)
    ffn_all = (
        resid_all * lax.rsqrt(squares_mid / D + epsilon)[:, None] * ffn_gain[None, :]
    ).astype(jnp.bfloat16)
    both = scatter_matmul(ffn_all, (w_gate, w_up), "pool", n_pool)
    chunk = w_gate.shape[1] // n_pool
    gate_total = both[:, :chunk]
    up_total = both[:, chunk:]
    hidden = (jax.nn.silu(gate_total) * up_total).astype(jnp.bfloat16)
    down_part = gather_matmul(hidden, w_down, "pool", n_pool)
    return residual + scatter_sum_cs(down_part.reshape(n_cs, rows_here, -1))


def solution(mesh):
    return jax.shard_map(
        local,
        mesh=mesh,
        in_specs=(
            P(("groups", "col", "side"), "pool"),
            P("pool"),
            P("pool", ("col", "side"), None),
            P(("col", "side"), "pool"),
            P("pool"),
            P("pool", ("col", "side")),
            P("pool", ("col", "side")),
            P(("col", "side"), "pool"),
            P(("groups", "pool"), None, None, ("col", "side"), None),
            P("groups"),
            P("groups"),
            P("groups"),
        ),
        out_specs=P(("groups", "col", "side"), "pool"),
        check_vma=False,
    )
```

```python
import math

import jax
import jax.numpy as jnp
from jax import lax
from jax.sharding import PartitionSpec as P

D = 8192
H = 64
KVH = 8
HD = 128


epsilon = 1e-05
rope_base = 500000.0
CS = ("col", "side")


def rotate(heads_in, positions):
    half_width = heads_in.shape[-1] // 2
    frequency = 1.0 / rope_base ** (
        jnp.arange(half_width, dtype=jnp.float32) * 2.0 / heads_in.shape[-1]
    )
    angles = positions.astype(jnp.float32)[:, None] * frequency[None, :]
    cosine_part = jnp.cos(angles)[:, None, :]
    sine_part = jnp.sin(angles)[:, None, :]
    first_half = heads_in[..., :half_width]
    second_half = heads_in[..., half_width:]
    return jnp.concatenate(
        [
            first_half * cosine_part - second_half * sine_part,
            second_half * cosine_part + first_half * sine_part,
        ],
        axis=-1,
    )


def rope_rows(qkv_sum, positions, per_group, head_dim):
    row_count = qkv_sum.shape[0]
    shaped = qkv_sum.reshape(row_count, -1, per_group + 2, head_dim)
    group_count = shaped.shape[1]
    turned = rotate(
        shaped[:, :, : per_group + 1].reshape(row_count, group_count * (per_group + 1), head_dim),
        positions,
    )
    turned = turned.reshape(row_count, group_count, per_group + 1, head_dim)
    return (
        jnp.concatenate([turned, shaped[:, :, per_group + 1 :]], axis=2)
        .reshape(row_count, -1)
        .astype(jnp.bfloat16)
    )


def attend(qkv_rot, kv_block, seen_count, per_group, head_dim):
    slot_count = qkv_rot.shape[0]
    cache_keys = kv_block[:, :, 0]
    values_all = kv_block[:, :, 1]
    shaped = qkv_rot.reshape(slot_count, cache_keys.shape[2], per_group + 2, head_dim)
    queries = shaped[:, :, :per_group]
    own_key = shaped[:, :, per_group]
    own_value = shaped[:, :, per_group + 1]
    score_scale = 1.0 / math.sqrt(head_dim)
    scores = (
        jnp.einsum("sgqd,stgd->sgqt", queries, cache_keys, preferred_element_type=jnp.float32)
        * score_scale
    )
    own_score = (
        jnp.einsum("sgqd,sgd->sgq", queries, own_key, preferred_element_type=jnp.float32)
        * score_scale
    )
    live_mask = (jnp.arange(cache_keys.shape[1], dtype=jnp.int32)[None, :] < seen_count[:, None])[
        :, None, None, :
    ]
    peak_score = jnp.maximum(jnp.max(jnp.where(live_mask, scores, -jnp.inf), axis=-1), own_score)
    weights = jnp.where(live_mask, jnp.exp(scores - peak_score[..., None]), 0.0)
    own_weight = jnp.exp(own_score - peak_score)
    denominator = jnp.sum(weights, axis=-1) + own_weight
    prob_weights = (weights / denominator[..., None]).astype(jnp.bfloat16)
    own_prob = (own_weight / denominator).astype(jnp.bfloat16)
    mixture = jnp.einsum(
        "sgqt,stgd->sgqd", prob_weights, values_all, preferred_element_type=jnp.float32
    )
    mixture = (
        mixture
        + own_prob.astype(jnp.float32)[..., None] * own_value.astype(jnp.float32)[:, :, None, :]
    )
    return mixture.reshape(slot_count, -1).astype(jnp.bfloat16)


def shift_pairs(n, k):
    return [(i, (i + k) % n) for i in range(n)]


def gather_rows(x, axis, n, want):
    idx = lax.axis_index(axis)
    per = x.shape[0]
    got = [x] + [lax.ppermute(x, axis, shift_pairs(n, k)) for k in range(1, n)]
    stacked = jnp.concatenate(got, axis=0)
    arrival = ((idx - want // per) % n) * per + want % per
    chooser = (arrival[:, None] == jnp.arange(n * per, dtype=arrival.dtype)[None, :]).astype(x.dtype)
    return jnp.dot(chooser, stacked, preferred_element_type=jnp.float32).astype(x.dtype)


def pick(keys, wanted, values):
    hit = keys[None, :] == wanted[:, None]
    return jnp.sum(jnp.where(hit, values[None, :], 0), axis=1)


def scatter_sum(blocks, axis, n):
    idx = lax.axis_index(axis)
    total = jnp.take(blocks, idx, axis=0).astype(jnp.float32)
    for k in range(1, n):
        piece = jnp.take(blocks, (idx + k) % n, axis=0)
        total = total + lax.ppermute(piece, axis, shift_pairs(n, k)).astype(jnp.float32)
    return total


def scatter_sum_cs(blocks):
    n_col = lax.axis_size("col")
    n_side = lax.axis_size("side")
    shaped = blocks.reshape((n_col, n_side) + blocks.shape[1:])
    per_col = scatter_sum(jnp.swapaxes(shaped, 0, 1), "side", n_side)
    return scatter_sum(per_col, "col", n_col)


def all_sum_cs(parts):
    n_col = lax.axis_size("col")
    n_side = lax.axis_size("side")
    n_pool = lax.axis_size("pool")
    side = lax.axis_index("side")
    mine = scatter_sum(parts.reshape((n_side, -1) + parts.shape[1:]), "side", n_side)
    mine = all_sum(mine, "col", n_col)
    squares = all_sum(jnp.sum(mine * mine, axis=1), "pool", n_pool)
    got = [mine] + [lax.ppermute(mine, "side", shift_pairs(n_side, k)) for k in range(1, n_side)]
    got_sq = [squares] + [
        lax.ppermute(squares, "side", shift_pairs(n_side, k)) for k in range(1, n_side)
    ]
    ordered = [lax.select_n((side - j) % n_side, *got) for j in range(n_side)]
    ordered_sq = [lax.select_n((side - j) % n_side, *got_sq) for j in range(n_side)]
    return jnp.stack(ordered).reshape(parts.shape), jnp.concatenate(ordered_sq)


def all_sum(x, axis, n):
    total = x
    for k in range(1, n):
        total = total + lax.ppermute(x, axis, shift_pairs(n, k))
    return total


def scatter_matmul(x, weights, axis, n):
    idx = lax.axis_index(axis)
    chunk = weights[0].shape[1] // n

    def block(j):
        parts = [
            jnp.dot(
                x,
                lax.dynamic_slice_in_dim(w, j * chunk, chunk, 1),
                preferred_element_type=jnp.float32,
            ).astype(jnp.bfloat16)
            for w in weights
        ]
        return jnp.concatenate(parts, axis=1)

    pieces = [block((idx + k) % n) for k in range(1, n)]
    pieces, x = lax.optimization_barrier((pieces, x))
    total = None
    for k in range(1, n):
        got = lax.ppermute(pieces[k - 1], axis, shift_pairs(n, k)).astype(jnp.float32)
        total = got if total is None else total + got
    own = block(idx).astype(jnp.float32)
    return own if total is None else own + total


def gather_matmul(x, w, axis, n):
    idx = lax.axis_index(axis)
    chunk = x.shape[1]
    acc = jnp.dot(
        x, lax.dynamic_slice_in_dim(w, idx * chunk, chunk, 0), preferred_element_type=jnp.float32
    )
    for k in range(1, n):
        got = lax.ppermute(x, axis, shift_pairs(n, k))
        rows = lax.dynamic_slice_in_dim(w, ((idx - k) % n) * chunk, chunk, 0)
        acc = acc + jnp.dot(got, rows, preferred_element_type=jnp.float32)
    return acc


def local(
    tokens,
    attn_gain,
    w_qkv,
    w_out,
    ffn_gain,
    w_gate,
    w_up,
    w_down,
    kv_cache,
    lengths,
    request_slot,
    row_request,
):
    n_pool = lax.axis_size("pool")
    n_cs = lax.axis_size(CS)
    pool_index = lax.axis_index("pool")
    per_owner = kv_cache.shape[0]
    per_group = H // KVH
    rows_here = tokens.shape[0]
    rows_total = rows_here * n_cs
    my_start = pool_index * per_owner
    every = jnp.arange(rows_total, dtype=row_request.dtype)
    slot_of_row = pick(every, row_request, request_slot)
    row_of_slot = pick(slot_of_row, every, every)
    positions = pick(request_slot, my_start + jnp.arange(per_owner, dtype=row_request.dtype), lengths)

    residual = tokens.astype(jnp.float32)
    squares = all_sum(jnp.sum(residual * residual, axis=1), "pool", n_pool)
    normed = (residual * lax.rsqrt(squares / D + epsilon)[:, None] * attn_gain[None, :]).astype(
        jnp.bfloat16
    )
    by_slot = gather_rows(normed, CS, n_cs, row_of_slot)
    qkv_part = jnp.einsum(
        "rf,fgc->rgc", by_slot, w_qkv, preferred_element_type=jnp.float32
    ).reshape(rows_total, -1)
    qkv_part, kv_cache = lax.optimization_barrier((qkv_part, kv_cache))
    summed = scatter_sum(qkv_part.reshape(n_pool, per_owner, -1), "pool", n_pool)
    rotated = rope_rows(summed, positions, per_group, HD)
    attended = attend(rotated, kv_cache, positions, per_group, HD)
    by_row = gather_rows(attended, "pool", n_pool, slot_of_row)
    out_part = jnp.dot(by_row, w_out, preferred_element_type=jnp.float32)
    cs_index = lax.axis_index(CS)
    out_part = lax.dynamic_update_slice_in_dim(
        out_part,
        lax.dynamic_slice_in_dim(out_part, cs_index * rows_here, rows_here, 0) + residual,
        cs_index * rows_here,
        0,
    )
    resid_all, squares_mid = all_sum_cs(out_part)
    residual = lax.dynamic_slice_in_dim(resid_all, cs_index * rows_here, rows_here, 0)

    ffn_all = (
        resid_all * lax.rsqrt(squares_mid / D + epsilon)[:, None] * ffn_gain[None, :]
    ).astype(jnp.bfloat16)
    both = scatter_matmul(ffn_all, (w_gate, w_up), "pool", n_pool)
    chunk = w_gate.shape[1] // n_pool
    gate_total = both[:, :chunk]
    up_total = both[:, chunk:]
    hidden = (jax.nn.silu(gate_total) * up_total).astype(jnp.bfloat16)
    down_part = gather_matmul(hidden, w_down, "pool", n_pool)
    return residual + scatter_sum_cs(down_part.reshape(n_cs, rows_here, -1))


def solution(mesh):
    return jax.shard_map(
        local,
        mesh=mesh,
        in_specs=(
            P(("groups", "col", "side"), "pool"),
            P("pool"),
            P("pool", ("col", "side"), None),
            P(("col", "side"), "pool"),
            P("pool"),
            P("pool", ("col", "side")),
            P("pool", ("col", "side")),
            P(("col", "side"), "pool"),
            P(("groups", "pool"), None, None, ("col", "side"), None),
            P("groups"),
            P("groups"),
            P("groups"),
        ),
        out_specs=P(("groups", "col", "side"), "pool"),
        check_vma=False,
    )
```

```python
import math

import jax
import jax.numpy as jnp
from jax import lax
from jax.sharding import PartitionSpec as P

D = 8192
H = 64
KVH = 8
HD = 128


epsilon = 1e-05
rope_base = 500000.0
CS = ("col", "side")


def rotate(heads_in, positions):
    half_width = heads_in.shape[-1] // 2
    frequency = 1.0 / rope_base ** (
        jnp.arange(half_width, dtype=jnp.float32) * 2.0 / heads_in.shape[-1]
    )
    angles = positions.astype(jnp.float32)[:, None] * frequency[None, :]
    cosine_part = jnp.cos(angles)[:, None, :]
    sine_part = jnp.sin(angles)[:, None, :]
    first_half = heads_in[..., :half_width]
    second_half = heads_in[..., half_width:]
    return jnp.concatenate(
        [
            first_half * cosine_part - second_half * sine_part,
            second_half * cosine_part + first_half * sine_part,
        ],
        axis=-1,
    )


def rope_rows(qkv_sum, positions, per_group, head_dim):
    row_count = qkv_sum.shape[0]
    shaped = qkv_sum.reshape(row_count, -1, per_group + 2, head_dim)
    group_count = shaped.shape[1]
    turned = rotate(
        shaped[:, :, : per_group + 1].reshape(row_count, group_count * (per_group + 1), head_dim),
        positions,
    )
    turned = turned.reshape(row_count, group_count, per_group + 1, head_dim)
    return (
        jnp.concatenate([turned, shaped[:, :, per_group + 1 :]], axis=2)
        .reshape(row_count, -1)
        .astype(jnp.bfloat16)
    )


def attend(qkv_rot, kv_block, seen_count, per_group, head_dim):
    slot_count = qkv_rot.shape[0]
    cache_keys = kv_block[:, :, 0]
    values_all = kv_block[:, :, 1]
    shaped = qkv_rot.reshape(slot_count, cache_keys.shape[2], per_group + 2, head_dim)
    queries = shaped[:, :, :per_group]
    own_key = shaped[:, :, per_group]
    own_value = shaped[:, :, per_group + 1]
    score_scale = 1.0 / math.sqrt(head_dim)
    scores = (
        jnp.einsum("sgqd,stgd->sgqt", queries, cache_keys, preferred_element_type=jnp.float32)
        * score_scale
    )
    own_score = (
        jnp.einsum("sgqd,sgd->sgq", queries, own_key, preferred_element_type=jnp.float32)
        * score_scale
    )
    live_mask = (jnp.arange(cache_keys.shape[1], dtype=jnp.int32)[None, :] < seen_count[:, None])[
        :, None, None, :
    ]
    peak_score = jnp.maximum(jnp.max(jnp.where(live_mask, scores, -jnp.inf), axis=-1), own_score)
    weights = jnp.where(live_mask, jnp.exp(scores - peak_score[..., None]), 0.0)
    own_weight = jnp.exp(own_score - peak_score)
    denominator = jnp.sum(weights, axis=-1) + own_weight
    prob_weights = (weights / denominator[..., None]).astype(jnp.bfloat16)
    own_prob = (own_weight / denominator).astype(jnp.bfloat16)
    mixture = jnp.einsum(
        "sgqt,stgd->sgqd", prob_weights, values_all, preferred_element_type=jnp.float32
    )
    mixture = (
        mixture
        + own_prob.astype(jnp.float32)[..., None] * own_value.astype(jnp.float32)[:, :, None, :]
    )
    return mixture.reshape(slot_count, -1).astype(jnp.bfloat16)


def shift_pairs(n, k):
    return [(i, (i + k) % n) for i in range(n)]


def gather_rows(x, axis, n, want):
    idx = lax.axis_index(axis)
    per = x.shape[0]
    got = [x] + [lax.ppermute(x, axis, shift_pairs(n, k)) for k in range(1, n)]
    stacked = jnp.concatenate(got, axis=0)
    arrival = ((idx - want // per) % n) * per + want % per
    chooser = (arrival[:, None] == jnp.arange(n * per, dtype=arrival.dtype)[None, :]).astype(x.dtype)
    return jnp.dot(chooser, stacked, preferred_element_type=jnp.float32).astype(x.dtype)


def pick(keys, wanted, values):
    hit = keys[None, :] == wanted[:, None]
    return jnp.sum(jnp.where(hit, values[None, :], 0), axis=1)


def scatter_sum(blocks, axis, n):
    idx = lax.axis_index(axis)
    total = jnp.take(blocks, idx, axis=0).astype(jnp.float32)
    for k in range(1, n):
        piece = jnp.take(blocks, (idx + k) % n, axis=0)
        total = total + lax.ppermute(piece, axis, shift_pairs(n, k)).astype(jnp.float32)
    return total


def scatter_sum_cs(blocks):
    n_col = lax.axis_size("col")
    n_side = lax.axis_size("side")
    shaped = blocks.reshape((n_col, n_side) + blocks.shape[1:])
    per_col = scatter_sum(jnp.swapaxes(shaped, 0, 1), "side", n_side)
    return scatter_sum(per_col, "col", n_col)


def all_sum_cs(parts):
    n_col = lax.axis_size("col")
    n_side = lax.axis_size("side")
    side = lax.axis_index("side")
    mine = scatter_sum(parts.reshape((n_side, -1) + parts.shape[1:]), "side", n_side)
    mine = all_sum(mine, "col", n_col)
    got = [mine] + [lax.ppermute(mine, "side", shift_pairs(n_side, k)) for k in range(1, n_side)]
    ordered = [lax.select_n((side - j) % n_side, *got) for j in range(n_side)]
    return jnp.stack(ordered).reshape(parts.shape)


def all_sum(x, axis, n):
    total = x
    for k in range(1, n):
        total = total + lax.ppermute(x, axis, shift_pairs(n, k))
    return total


def scatter_matmul(x, weights, axis, n):
    idx = lax.axis_index(axis)
    chunk = weights[0].shape[1] // n

    def block(j):
        parts = [
            jnp.dot(
                x,
                lax.dynamic_slice_in_dim(w, j * chunk, chunk, 1),
                preferred_element_type=jnp.float32,
            ).astype(jnp.bfloat16)
            for w in weights
        ]
        return jnp.concatenate(parts, axis=1)

    pieces = [block((idx + k) % n) for k in range(1, n)]
    pieces, x = lax.optimization_barrier((pieces, x))
    total = None
    for k in range(1, n):
        got = lax.ppermute(pieces[k - 1], axis, shift_pairs(n, k)).astype(jnp.float32)
        total = got if total is None else total + got
    own = block(idx).astype(jnp.float32)
    return own if total is None else own + total


def gather_matmul(x, w, axis, n):
    idx = lax.axis_index(axis)
    chunk = x.shape[1]
    acc = jnp.dot(
        x, lax.dynamic_slice_in_dim(w, idx * chunk, chunk, 0), preferred_element_type=jnp.float32
    )
    for k in range(1, n):
        got = lax.ppermute(x, axis, shift_pairs(n, k))
        rows = lax.dynamic_slice_in_dim(w, ((idx - k) % n) * chunk, chunk, 0)
        acc = acc + jnp.dot(got, rows, preferred_element_type=jnp.float32)
    return acc


def local(
    tokens,
    attn_gain,
    w_qkv,
    w_out,
    ffn_gain,
    w_gate,
    w_up,
    w_down,
    kv_cache,
    lengths,
    request_slot,
    row_request,
):
    n_pool = lax.axis_size("pool")
    n_cs = lax.axis_size(CS)
    pool_index = lax.axis_index("pool")
    per_owner = kv_cache.shape[0]
    per_group = H // KVH
    rows_here = tokens.shape[0]
    rows_total = rows_here * n_cs
    my_start = pool_index * per_owner
    every = jnp.arange(rows_total, dtype=row_request.dtype)
    slot_of_row = pick(every, row_request, request_slot)
    row_of_slot = pick(slot_of_row, every, every)
    positions = pick(request_slot, my_start + jnp.arange(per_owner, dtype=row_request.dtype), lengths)

    residual = tokens.astype(jnp.float32)
    squares = all_sum(jnp.sum(residual * residual, axis=1), "pool", n_pool)
    tokens_by_slot = gather_rows(tokens, CS, n_cs, row_of_slot)
    cs_index = lax.axis_index(CS)
    squares_got = jnp.concatenate(
        [squares] + [lax.ppermute(squares, CS, shift_pairs(n_cs, k)) for k in range(1, n_cs)]
    )
    squares_by_slot = jnp.take(
        squares_got,
        ((cs_index - row_of_slot // rows_here) % n_cs) * rows_here + row_of_slot % rows_here,
    )[:, None]
    by_slot = (
        tokens_by_slot.astype(jnp.float32)
        * lax.rsqrt(squares_by_slot / D + epsilon)
        * attn_gain[None, :]
    ).astype(jnp.bfloat16)
    qkv_part = jnp.einsum(
        "rf,fgc->rgc", by_slot, w_qkv, preferred_element_type=jnp.float32
    ).reshape(rows_total, -1)
    qkv_part, kv_cache = lax.optimization_barrier((qkv_part, kv_cache))
    summed = scatter_sum(qkv_part.reshape(n_pool, per_owner, -1), "pool", n_pool)
    rotated = rope_rows(summed, positions, per_group, HD)
    attended = attend(rotated, kv_cache, positions, per_group, HD)
    by_row = gather_rows(attended, "pool", n_pool, slot_of_row)
    out_part = jnp.dot(by_row, w_out, preferred_element_type=jnp.float32)
    out_part = lax.dynamic_update_slice_in_dim(
        out_part,
        lax.dynamic_slice_in_dim(out_part, cs_index * rows_here, rows_here, 0) + residual,
        cs_index * rows_here,
        0,
    )
    resid_all = all_sum_cs(out_part)
    residual = lax.dynamic_slice_in_dim(resid_all, cs_index * rows_here, rows_here, 0)

    squares_mid = all_sum(jnp.sum(resid_all * resid_all, axis=1), "pool", n_pool)
    ffn_all = (
        resid_all * lax.rsqrt(squares_mid / D + epsilon)[:, None] * ffn_gain[None, :]
    ).astype(jnp.bfloat16)
    both = scatter_matmul(ffn_all, (w_gate, w_up), "pool", n_pool)
    chunk = w_gate.shape[1] // n_pool
    gate_total = both[:, :chunk]
    up_total = both[:, chunk:]
    hidden = (jax.nn.silu(gate_total) * up_total).astype(jnp.bfloat16)
    down_part = gather_matmul(hidden, w_down, "pool", n_pool)
    return residual + scatter_sum_cs(down_part.reshape(n_cs, rows_here, -1))


def solution(mesh):
    return jax.shard_map(
        local,
        mesh=mesh,
        in_specs=(
            P(("groups", "col", "side"), "pool"),
            P("pool"),
            P("pool", ("col", "side"), None),
            P(("col", "side"), "pool"),
            P("pool"),
            P("pool", ("col", "side")),
            P("pool", ("col", "side")),
            P(("col", "side"), "pool"),
            P(("groups", "pool"), None, None, ("col", "side"), None),
            P("groups"),
            P("groups"),
            P("groups"),
        ),
        out_specs=P(("groups", "col", "side"), "pool"),
        check_vma=False,
    )
```

```python
import math

import jax
import jax.numpy as jnp
from jax import lax
from jax.sharding import PartitionSpec as P

D = 8192
H = 64
KVH = 8
HD = 128


epsilon = 1e-05
rope_base = 500000.0
CS = ("col", "side")


def rotate(heads_in, positions):
    half_width = heads_in.shape[-1] // 2
    frequency = 1.0 / rope_base ** (
        jnp.arange(half_width, dtype=jnp.float32) * 2.0 / heads_in.shape[-1]
    )
    angles = positions.astype(jnp.float32)[:, None] * frequency[None, :]
    cosine_part = jnp.cos(angles)[:, None, :]
    sine_part = jnp.sin(angles)[:, None, :]
    first_half = heads_in[..., :half_width]
    second_half = heads_in[..., half_width:]
    return jnp.concatenate(
        [
            first_half * cosine_part - second_half * sine_part,
            second_half * cosine_part + first_half * sine_part,
        ],
        axis=-1,
    )


def rope_rows(qkv_sum, positions, per_group, head_dim):
    row_count = qkv_sum.shape[0]
    shaped = qkv_sum.reshape(row_count, -1, per_group + 2, head_dim)
    group_count = shaped.shape[1]
    turned = rotate(
        shaped[:, :, : per_group + 1].reshape(row_count, group_count * (per_group + 1), head_dim),
        positions,
    )
    turned = turned.reshape(row_count, group_count, per_group + 1, head_dim)
    return (
        jnp.concatenate([turned, shaped[:, :, per_group + 1 :]], axis=2)
        .reshape(row_count, -1)
        .astype(jnp.bfloat16)
    )


def attend(qkv_rot, kv_block, seen_count, per_group, head_dim):
    slot_count = qkv_rot.shape[0]
    cache_keys = kv_block[:, :, 0]
    values_all = kv_block[:, :, 1]
    shaped = qkv_rot.reshape(slot_count, cache_keys.shape[2], per_group + 2, head_dim)
    queries = shaped[:, :, :per_group]
    own_key = shaped[:, :, per_group]
    own_value = shaped[:, :, per_group + 1]
    score_scale = 1.0 / math.sqrt(head_dim)
    scores = (
        jnp.einsum("sgqd,stgd->sgqt", queries, cache_keys, preferred_element_type=jnp.float32)
        * score_scale
    )
    own_score = (
        jnp.einsum("sgqd,sgd->sgq", queries, own_key, preferred_element_type=jnp.float32)
        * score_scale
    )
    live_mask = (jnp.arange(cache_keys.shape[1], dtype=jnp.int32)[None, :] < seen_count[:, None])[
        :, None, None, :
    ]
    peak_score = jnp.maximum(jnp.max(jnp.where(live_mask, scores, -jnp.inf), axis=-1), own_score)
    weights = jnp.where(live_mask, jnp.exp(scores - peak_score[..., None]), 0.0)
    own_weight = jnp.exp(own_score - peak_score)
    denominator = jnp.sum(weights, axis=-1) + own_weight
    prob_weights = (weights / denominator[..., None]).astype(jnp.bfloat16)
    own_prob = (own_weight / denominator).astype(jnp.bfloat16)
    mixture = jnp.einsum(
        "sgqt,stgd->sgqd", prob_weights, values_all, preferred_element_type=jnp.float32
    )
    mixture = (
        mixture
        + own_prob.astype(jnp.float32)[..., None] * own_value.astype(jnp.float32)[:, :, None, :]
    )
    return mixture.reshape(slot_count, -1).astype(jnp.bfloat16)


def send_order(n):
    return sorted(range(1, n), key=lambda k: -min(k, n - k))


def shift_pairs(n, k):
    return [(i, (i + k) % n) for i in range(n)]


def gather_rows(x, axis, n, want):
    idx = lax.axis_index(axis)
    per = x.shape[0]
    sent = {k: lax.ppermute(x, axis, shift_pairs(n, k)) for k in send_order(n)}
    stacked = jnp.concatenate([x] + [sent[k] for k in range(1, n)], axis=0)
    arrival = ((idx - want // per) % n) * per + want % per
    chooser = (arrival[:, None] == jnp.arange(n * per, dtype=arrival.dtype)[None, :]).astype(x.dtype)
    return jnp.dot(chooser, stacked, preferred_element_type=jnp.float32).astype(x.dtype)


def pick(keys, wanted, values):
    hit = keys[None, :] == wanted[:, None]
    return jnp.sum(jnp.where(hit, values[None, :], 0), axis=1)


def scatter_sum(blocks, axis, n):
    idx = lax.axis_index(axis)
    total = jnp.take(blocks, idx, axis=0).astype(jnp.float32)
    for k in send_order(n):
        piece = jnp.take(blocks, (idx + k) % n, axis=0)
        total = total + lax.ppermute(piece, axis, shift_pairs(n, k)).astype(jnp.float32)
    return total


def scatter_sum_cs(blocks):
    n_col = lax.axis_size("col")
    n_side = lax.axis_size("side")
    shaped = blocks.reshape((n_col, n_side) + blocks.shape[1:])
    per_col = scatter_sum(jnp.swapaxes(shaped, 0, 1), "side", n_side)
    return scatter_sum(per_col, "col", n_col)


def all_sum_cs(parts):
    n_col = lax.axis_size("col")
    n_side = lax.axis_size("side")
    side = lax.axis_index("side")
    mine = scatter_sum(parts.reshape((n_side, -1) + parts.shape[1:]), "side", n_side)
    mine = all_sum(mine, "col", n_col)
    got = [mine] + [lax.ppermute(mine, "side", shift_pairs(n_side, k)) for k in range(1, n_side)]
    ordered = [lax.select_n((side - j) % n_side, *got) for j in range(n_side)]
    return jnp.stack(ordered).reshape(parts.shape)


def all_sum(x, axis, n):
    total = x
    for k in range(1, n):
        total = total + lax.ppermute(x, axis, shift_pairs(n, k))
    return total


def scatter_matmul(x, weights, axis, n):
    idx = lax.axis_index(axis)
    chunk = weights[0].shape[1] // n

    def block(j):
        parts = [
            jnp.dot(
                x,
                lax.dynamic_slice_in_dim(w, j * chunk, chunk, 1),
                preferred_element_type=jnp.float32,
            ).astype(jnp.bfloat16)
            for w in weights
        ]
        return jnp.concatenate(parts, axis=1)

    order = send_order(n)
    pieces = [block((idx + k) % n) for k in order]
    pieces, x = lax.optimization_barrier((pieces, x))
    total = None
    for k, piece in zip(order, pieces):
        got = lax.ppermute(piece, axis, shift_pairs(n, k)).astype(jnp.float32)
        total = got if total is None else total + got
    own = block(idx).astype(jnp.float32)
    return own if total is None else own + total


def gather_matmul(x, w, axis, n):
    idx = lax.axis_index(axis)
    chunk = x.shape[1]
    acc = jnp.dot(
        x, lax.dynamic_slice_in_dim(w, idx * chunk, chunk, 0), preferred_element_type=jnp.float32
    )
    for k in send_order(n):
        got = lax.ppermute(x, axis, shift_pairs(n, k))
        rows = lax.dynamic_slice_in_dim(w, ((idx - k) % n) * chunk, chunk, 0)
        acc = acc + jnp.dot(got, rows, preferred_element_type=jnp.float32)
    return acc


def local(
    tokens,
    attn_gain,
    w_qkv,
    w_out,
    ffn_gain,
    w_gate,
    w_up,
    w_down,
    kv_cache,
    lengths,
    request_slot,
    row_request,
):
    n_pool = lax.axis_size("pool")
    n_cs = lax.axis_size(CS)
    pool_index = lax.axis_index("pool")
    per_owner = kv_cache.shape[0]
    per_group = H // KVH
    rows_here = tokens.shape[0]
    rows_total = rows_here * n_cs
    my_start = pool_index * per_owner
    every = jnp.arange(rows_total, dtype=row_request.dtype)
    slot_of_row = pick(every, row_request, request_slot)
    row_of_slot = pick(slot_of_row, every, every)
    positions = pick(request_slot, my_start + jnp.arange(per_owner, dtype=row_request.dtype), lengths)

    residual = tokens.astype(jnp.float32)
    squares = all_sum(jnp.sum(residual * residual, axis=1), "pool", n_pool)
    normed = (residual * lax.rsqrt(squares / D + epsilon)[:, None] * attn_gain[None, :]).astype(
        jnp.bfloat16
    )
    by_slot = gather_rows(normed, CS, n_cs, row_of_slot)
    qkv_part = jnp.einsum(
        "rf,fgc->rgc", by_slot, w_qkv, preferred_element_type=jnp.float32
    ).reshape(rows_total, -1)
    qkv_part, kv_cache = lax.optimization_barrier((qkv_part, kv_cache))
    summed = scatter_sum(qkv_part.reshape(n_pool, per_owner, -1), "pool", n_pool)
    rotated = rope_rows(summed, positions, per_group, HD)
    attended = attend(rotated, kv_cache, positions, per_group, HD)
    by_row = gather_rows(attended, "pool", n_pool, slot_of_row)
    out_part = jnp.dot(by_row, w_out, preferred_element_type=jnp.float32)
    cs_index = lax.axis_index(CS)
    out_part = lax.dynamic_update_slice_in_dim(
        out_part,
        lax.dynamic_slice_in_dim(out_part, cs_index * rows_here, rows_here, 0) + residual,
        cs_index * rows_here,
        0,
    )
    resid_all = all_sum_cs(out_part)
    residual = lax.dynamic_slice_in_dim(resid_all, cs_index * rows_here, rows_here, 0)

    squares_mid = all_sum(jnp.sum(resid_all * resid_all, axis=1), "pool", n_pool)
    ffn_all = (
        resid_all * lax.rsqrt(squares_mid / D + epsilon)[:, None] * ffn_gain[None, :]
    ).astype(jnp.bfloat16)
    both = scatter_matmul(ffn_all, (w_gate, w_up), "pool", n_pool)
    chunk = w_gate.shape[1] // n_pool
    gate_total = both[:, :chunk]
    up_total = both[:, chunk:]
    hidden = (jax.nn.silu(gate_total) * up_total).astype(jnp.bfloat16)
    down_part = gather_matmul(hidden, w_down, "pool", n_pool)
    return residual + scatter_sum_cs(down_part.reshape(n_cs, rows_here, -1))


def solution(mesh):
    return jax.shard_map(
        local,
        mesh=mesh,
        in_specs=(
            P(("groups", "col", "side"), "pool"),
            P("pool"),
            P("pool", ("col", "side"), None),
            P(("col", "side"), "pool"),
            P("pool"),
            P("pool", ("col", "side")),
            P("pool", ("col", "side")),
            P(("col", "side"), "pool"),
            P(("groups", "pool"), None, None, ("col", "side"), None),
            P("groups"),
            P("groups"),
            P("groups"),
        ),
        out_specs=P(("groups", "col", "side"), "pool"),
        check_vma=False,
    )
```

```python
import math

import jax
import jax.numpy as jnp
from jax import lax
from jax.sharding import PartitionSpec as P

D = 8192
H = 64
KVH = 8
HD = 128


epsilon = 1e-05
rope_base = 500000.0
CS = ("col", "side")


def rotate(heads_in, positions):
    half_width = heads_in.shape[-1] // 2
    frequency = 1.0 / rope_base ** (
        jnp.arange(half_width, dtype=jnp.float32) * 2.0 / heads_in.shape[-1]
    )
    angles = positions.astype(jnp.float32)[:, None] * frequency[None, :]
    cosine_part = jnp.cos(angles)[:, None, :]
    sine_part = jnp.sin(angles)[:, None, :]
    first_half = heads_in[..., :half_width]
    second_half = heads_in[..., half_width:]
    return jnp.concatenate(
        [
            first_half * cosine_part - second_half * sine_part,
            second_half * cosine_part + first_half * sine_part,
        ],
        axis=-1,
    )


def rope_rows(qkv_sum, positions, per_group, head_dim):
    row_count = qkv_sum.shape[0]
    shaped = qkv_sum.reshape(row_count, -1, per_group + 2, head_dim)
    group_count = shaped.shape[1]
    turned = rotate(
        shaped[:, :, : per_group + 1].reshape(row_count, group_count * (per_group + 1), head_dim),
        positions,
    )
    turned = turned.reshape(row_count, group_count, per_group + 1, head_dim)
    return (
        jnp.concatenate([turned, shaped[:, :, per_group + 1 :]], axis=2)
        .reshape(row_count, -1)
        .astype(jnp.bfloat16)
    )


def attend(qkv_rot, kv_block, seen_count, per_group, head_dim):
    slot_count = qkv_rot.shape[0]
    cache_keys = kv_block[:, :, 0]
    values_all = kv_block[:, :, 1]
    shaped = qkv_rot.reshape(slot_count, cache_keys.shape[2], per_group + 2, head_dim)
    queries = shaped[:, :, :per_group]
    own_key = shaped[:, :, per_group]
    own_value = shaped[:, :, per_group + 1]
    score_scale = 1.0 / math.sqrt(head_dim)
    scores = (
        jnp.einsum("sgqd,stgd->sgqt", queries, cache_keys, preferred_element_type=jnp.float32)
        * score_scale
    )
    own_score = (
        jnp.einsum("sgqd,sgd->sgq", queries, own_key, preferred_element_type=jnp.float32)
        * score_scale
    )
    live_mask = (jnp.arange(cache_keys.shape[1], dtype=jnp.int32)[None, :] < seen_count[:, None])[
        :, None, None, :
    ]
    peak_score = jnp.maximum(jnp.max(jnp.where(live_mask, scores, -jnp.inf), axis=-1), own_score)
    weights = jnp.where(live_mask, jnp.exp(scores - peak_score[..., None]), 0.0)
    own_weight = jnp.exp(own_score - peak_score)
    denominator = jnp.sum(weights, axis=-1) + own_weight
    prob_weights = (weights / denominator[..., None]).astype(jnp.bfloat16)
    own_prob = (own_weight / denominator).astype(jnp.bfloat16)
    mixture = jnp.einsum(
        "sgqt,stgd->sgqd", prob_weights, values_all, preferred_element_type=jnp.float32
    )
    mixture = (
        mixture
        + own_prob.astype(jnp.float32)[..., None] * own_value.astype(jnp.float32)[:, :, None, :]
    )
    return mixture.reshape(slot_count, -1).astype(jnp.bfloat16)


def send_order(n):
    return sorted(range(1, n), key=lambda k: -min(k, n - k))


def shift_pairs(n, k):
    return [(i, (i + k) % n) for i in range(n)]


def gather_rows(x, axis, n, want):
    idx = lax.axis_index(axis)
    per = x.shape[0]
    sent = {k: lax.ppermute(x, axis, shift_pairs(n, k)) for k in send_order(n)}
    stacked = jnp.concatenate([x] + [sent[k] for k in range(1, n)], axis=0)
    arrival = ((idx - want // per) % n) * per + want % per
    chooser = (arrival[:, None] == jnp.arange(n * per, dtype=arrival.dtype)[None, :]).astype(x.dtype)
    return jnp.dot(chooser, stacked, preferred_element_type=jnp.float32).astype(x.dtype)


def pick(keys, wanted, values):
    hit = keys[None, :] == wanted[:, None]
    return jnp.sum(jnp.where(hit, values[None, :], 0), axis=1)


def scatter_sum(blocks, axis, n):
    idx = lax.axis_index(axis)
    total = jnp.take(blocks, idx, axis=0).astype(jnp.float32)
    for k in send_order(n):
        piece = jnp.take(blocks, (idx + k) % n, axis=0)
        total = total + lax.ppermute(piece, axis, shift_pairs(n, k)).astype(jnp.float32)
    return total


def scatter_sum_cs(blocks):
    n_col = lax.axis_size("col")
    n_side = lax.axis_size("side")
    shaped = blocks.reshape((n_col, n_side) + blocks.shape[1:])
    per_col = scatter_sum(jnp.swapaxes(shaped, 0, 1), "side", n_side)
    return scatter_sum(per_col, "col", n_col)


def all_sum_cs(parts):
    n_col = lax.axis_size("col")
    n_side = lax.axis_size("side")
    side = lax.axis_index("side")
    mine = scatter_sum(parts.reshape((n_side, -1) + parts.shape[1:]), "side", n_side)
    mine = all_sum(mine, "col", n_col)
    got = [mine] + [lax.ppermute(mine, "side", shift_pairs(n_side, k)) for k in range(1, n_side)]
    ordered = [lax.select_n((side - j) % n_side, *got) for j in range(n_side)]
    return jnp.stack(ordered).reshape(parts.shape)


def all_sum(x, axis, n):
    total = x
    for k in send_order(n):
        total = total + lax.ppermute(x, axis, shift_pairs(n, k))
    return total


def scatter_matmul(x, weights, axis, n):
    idx = lax.axis_index(axis)
    chunk = weights[0].shape[1] // n

    def block(j):
        parts = [
            jnp.dot(
                x,
                lax.dynamic_slice_in_dim(w, j * chunk, chunk, 1),
                preferred_element_type=jnp.float32,
            ).astype(jnp.bfloat16)
            for w in weights
        ]
        return jnp.concatenate(parts, axis=1)

    order = send_order(n)
    pieces = [block((idx + k) % n) for k in order]
    pieces, x = lax.optimization_barrier((pieces, x))
    total = None
    for k, piece in zip(order, pieces):
        got = lax.ppermute(piece, axis, shift_pairs(n, k)).astype(jnp.float32)
        total = got if total is None else total + got
    own = block(idx).astype(jnp.float32)
    return own if total is None else own + total


def gather_matmul(x, w, axis, n):
    idx = lax.axis_index(axis)
    chunk = x.shape[1]
    acc = jnp.dot(
        x, lax.dynamic_slice_in_dim(w, idx * chunk, chunk, 0), preferred_element_type=jnp.float32
    )
    for k in send_order(n):
        got = lax.ppermute(x, axis, shift_pairs(n, k))
        rows = lax.dynamic_slice_in_dim(w, ((idx - k) % n) * chunk, chunk, 0)
        acc = acc + jnp.dot(got, rows, preferred_element_type=jnp.float32)
    return acc


def local(
    tokens,
    attn_gain,
    w_qkv,
    w_out,
    ffn_gain,
    w_gate,
    w_up,
    w_down,
    kv_cache,
    lengths,
    request_slot,
    row_request,
):
    n_pool = lax.axis_size("pool")
    n_cs = lax.axis_size(CS)
    pool_index = lax.axis_index("pool")
    per_owner = kv_cache.shape[0]
    per_group = H // KVH
    rows_here = tokens.shape[0]
    rows_total = rows_here * n_cs
    my_start = pool_index * per_owner
    every = jnp.arange(rows_total, dtype=row_request.dtype)
    slot_of_row = pick(every, row_request, request_slot)
    row_of_slot = pick(slot_of_row, every, every)
    positions = pick(request_slot, my_start + jnp.arange(per_owner, dtype=row_request.dtype), lengths)

    residual = tokens.astype(jnp.float32)
    squares = all_sum(jnp.sum(residual * residual, axis=1), "pool", n_pool)
    normed = (residual * lax.rsqrt(squares / D + epsilon)[:, None] * attn_gain[None, :]).astype(
        jnp.bfloat16
    )
    by_slot = gather_rows(normed, CS, n_cs, row_of_slot)
    qkv_part = jnp.einsum(
        "rf,fgc->rgc", by_slot, w_qkv, preferred_element_type=jnp.float32
    ).reshape(rows_total, -1)
    qkv_part, kv_cache = lax.optimization_barrier((qkv_part, kv_cache))
    summed = scatter_sum(qkv_part.reshape(n_pool, per_owner, -1), "pool", n_pool)
    rotated = rope_rows(summed, positions, per_group, HD)
    attended = attend(rotated, kv_cache, positions, per_group, HD)
    by_row = gather_rows(attended, "pool", n_pool, slot_of_row)
    out_part = jnp.dot(by_row, w_out, preferred_element_type=jnp.float32)
    cs_index = lax.axis_index(CS)
    out_part = lax.dynamic_update_slice_in_dim(
        out_part,
        lax.dynamic_slice_in_dim(out_part, cs_index * rows_here, rows_here, 0) + residual,
        cs_index * rows_here,
        0,
    )
    resid_all = all_sum_cs(out_part)
    residual = lax.dynamic_slice_in_dim(resid_all, cs_index * rows_here, rows_here, 0)

    squares_mid = all_sum(jnp.sum(resid_all * resid_all, axis=1), "pool", n_pool)
    ffn_all = (
        resid_all * lax.rsqrt(squares_mid / D + epsilon)[:, None] * ffn_gain[None, :]
    ).astype(jnp.bfloat16)
    both = scatter_matmul(ffn_all, (w_gate, w_up), "pool", n_pool)
    chunk = w_gate.shape[1] // n_pool
    gate_total = both[:, :chunk]
    up_total = both[:, chunk:]
    hidden = (jax.nn.silu(gate_total) * up_total).astype(jnp.bfloat16)
    down_part = gather_matmul(hidden, w_down, "pool", n_pool)
    return residual + scatter_sum_cs(down_part.reshape(n_cs, rows_here, -1))


def solution(mesh):
    return jax.shard_map(
        local,
        mesh=mesh,
        in_specs=(
            P(("groups", "col", "side"), "pool"),
            P("pool"),
            P("pool", ("col", "side"), None),
            P(("col", "side"), "pool"),
            P("pool"),
            P("pool", ("col", "side")),
            P("pool", ("col", "side")),
            P(("col", "side"), "pool"),
            P(("groups", "pool"), None, None, ("col", "side"), None),
            P("groups"),
            P("groups"),
            P("groups"),
        ),
        out_specs=P(("groups", "col", "side"), "pool"),
        check_vma=False,
    )
```

```python
import math

import jax
import jax.numpy as jnp
from jax import lax
from jax.sharding import PartitionSpec as P

D = 8192
H = 64
KVH = 8
HD = 128


epsilon = 1e-05
rope_base = 500000.0
CS = ("col", "side")


def rotate(heads_in, positions):
    half_width = heads_in.shape[-1] // 2
    frequency = 1.0 / rope_base ** (
        jnp.arange(half_width, dtype=jnp.float32) * 2.0 / heads_in.shape[-1]
    )
    angles = positions.astype(jnp.float32)[:, None] * frequency[None, :]
    cosine_part = jnp.cos(angles)[:, None, :]
    sine_part = jnp.sin(angles)[:, None, :]
    first_half = heads_in[..., :half_width]
    second_half = heads_in[..., half_width:]
    return jnp.concatenate(
        [
            first_half * cosine_part - second_half * sine_part,
            second_half * cosine_part + first_half * sine_part,
        ],
        axis=-1,
    )


def rope_rows(qkv_sum, positions, per_group, head_dim):
    row_count = qkv_sum.shape[0]
    shaped = qkv_sum.reshape(row_count, -1, per_group + 2, head_dim)
    group_count = shaped.shape[1]
    turned = rotate(
        shaped[:, :, : per_group + 1].reshape(row_count, group_count * (per_group + 1), head_dim),
        positions,
    )
    turned = turned.reshape(row_count, group_count, per_group + 1, head_dim)
    return (
        jnp.concatenate([turned, shaped[:, :, per_group + 1 :]], axis=2)
        .reshape(row_count, -1)
        .astype(jnp.bfloat16)
    )


def attend(qkv_rot, kv_block, seen_count, per_group, head_dim):
    slot_count = qkv_rot.shape[0]
    cache_keys = kv_block[:, :, 0]
    values_all = kv_block[:, :, 1]
    shaped = qkv_rot.reshape(slot_count, cache_keys.shape[2], per_group + 2, head_dim)
    queries = shaped[:, :, :per_group]
    own_key = shaped[:, :, per_group]
    own_value = shaped[:, :, per_group + 1]
    score_scale = 1.0 / math.sqrt(head_dim)
    scores = (
        jnp.einsum("sgqd,stgd->sgqt", queries, cache_keys, preferred_element_type=jnp.float32)
        * score_scale
    )
    own_score = (
        jnp.einsum("sgqd,sgd->sgq", queries, own_key, preferred_element_type=jnp.float32)
        * score_scale
    )
    live_mask = (jnp.arange(cache_keys.shape[1], dtype=jnp.int32)[None, :] < seen_count[:, None])[
        :, None, None, :
    ]
    peak_score = jnp.maximum(jnp.max(jnp.where(live_mask, scores, -jnp.inf), axis=-1), own_score)
    weights = jnp.where(live_mask, jnp.exp(scores - peak_score[..., None]), 0.0)
    own_weight = jnp.exp(own_score - peak_score)
    denominator = jnp.sum(weights, axis=-1) + own_weight
    prob_weights = (weights / denominator[..., None]).astype(jnp.bfloat16)
    own_prob = (own_weight / denominator).astype(jnp.bfloat16)
    mixture = jnp.einsum(
        "sgqt,stgd->sgqd", prob_weights, values_all, preferred_element_type=jnp.float32
    )
    mixture = (
        mixture
        + own_prob.astype(jnp.float32)[..., None] * own_value.astype(jnp.float32)[:, :, None, :]
    )
    return mixture.reshape(slot_count, -1).astype(jnp.bfloat16)


def send_order(n):
    return sorted(range(1, n), key=lambda k: -min(k, n - k))


def shift_pairs(n, k):
    return [(i, (i + k) % n) for i in range(n)]


def gather_rows(x, axis, n, want):
    idx = lax.axis_index(axis)
    per = x.shape[0]
    sent = {k: lax.ppermute(x, axis, shift_pairs(n, k)) for k in send_order(n)}
    stacked = jnp.concatenate([x] + [sent[k] for k in range(1, n)], axis=0)
    arrival = ((idx - want // per) % n) * per + want % per
    chooser = (arrival[:, None] == jnp.arange(n * per, dtype=arrival.dtype)[None, :]).astype(x.dtype)
    return jnp.dot(chooser, stacked, preferred_element_type=jnp.float32).astype(x.dtype)


def pick(keys, wanted, values):
    hit = keys[None, :] == wanted[:, None]
    return jnp.sum(jnp.where(hit, values[None, :], 0), axis=1)


def scatter_sum(blocks, axis, n):
    idx = lax.axis_index(axis)
    total = jnp.take(blocks, idx, axis=0).astype(jnp.float32)
    sent = {
        k: lax.ppermute(jnp.take(blocks, (idx + k) % n, axis=0), axis, shift_pairs(n, k))
        for k in send_order(n)
    }
    for k in reversed(send_order(n)):
        total = total + sent[k].astype(jnp.float32)
    return total


def scatter_sum_cs(blocks):
    n_col = lax.axis_size("col")
    n_side = lax.axis_size("side")
    shaped = blocks.reshape((n_col, n_side) + blocks.shape[1:])
    per_col = scatter_sum(jnp.swapaxes(shaped, 0, 1), "side", n_side)
    return scatter_sum(per_col, "col", n_col)


def all_sum_cs(parts):
    n_col = lax.axis_size("col")
    n_side = lax.axis_size("side")
    side = lax.axis_index("side")
    mine = scatter_sum(parts.reshape((n_side, -1) + parts.shape[1:]), "side", n_side)
    mine = all_sum(mine, "col", n_col)
    got = [mine] + [lax.ppermute(mine, "side", shift_pairs(n_side, k)) for k in range(1, n_side)]
    ordered = [lax.select_n((side - j) % n_side, *got) for j in range(n_side)]
    return jnp.stack(ordered).reshape(parts.shape)


def all_sum(x, axis, n):
    total = x
    for k in range(1, n):
        total = total + lax.ppermute(x, axis, shift_pairs(n, k))
    return total


def scatter_matmul(x, weights, axis, n):
    idx = lax.axis_index(axis)
    chunk = weights[0].shape[1] // n

    def block(j):
        parts = [
            jnp.dot(
                x,
                lax.dynamic_slice_in_dim(w, j * chunk, chunk, 1),
                preferred_element_type=jnp.float32,
            ).astype(jnp.bfloat16)
            for w in weights
        ]
        return jnp.concatenate(parts, axis=1)

    order = send_order(n)
    pieces = [block((idx + k) % n) for k in order]
    pieces, x = lax.optimization_barrier((pieces, x))
    total = None
    for k, piece in zip(order, pieces):
        got = lax.ppermute(piece, axis, shift_pairs(n, k)).astype(jnp.float32)
        total = got if total is None else total + got
    own = block(idx).astype(jnp.float32)
    return own if total is None else own + total


def gather_matmul(x, w, axis, n):
    idx = lax.axis_index(axis)
    chunk = x.shape[1]
    acc = jnp.dot(
        x, lax.dynamic_slice_in_dim(w, idx * chunk, chunk, 0), preferred_element_type=jnp.float32
    )
    sent = {k: lax.ppermute(x, axis, shift_pairs(n, k)) for k in send_order(n)}
    for k in reversed(send_order(n)):
        rows = lax.dynamic_slice_in_dim(w, ((idx - k) % n) * chunk, chunk, 0)
        acc = acc + jnp.dot(sent[k], rows, preferred_element_type=jnp.float32)
    return acc


def local(
    tokens,
    attn_gain,
    w_qkv,
    w_out,
    ffn_gain,
    w_gate,
    w_up,
    w_down,
    kv_cache,
    lengths,
    request_slot,
    row_request,
):
    n_pool = lax.axis_size("pool")
    n_cs = lax.axis_size(CS)
    pool_index = lax.axis_index("pool")
    per_owner = kv_cache.shape[0]
    per_group = H // KVH
    rows_here = tokens.shape[0]
    rows_total = rows_here * n_cs
    my_start = pool_index * per_owner
    every = jnp.arange(rows_total, dtype=row_request.dtype)
    slot_of_row = pick(every, row_request, request_slot)
    row_of_slot = pick(slot_of_row, every, every)
    positions = pick(request_slot, my_start + jnp.arange(per_owner, dtype=row_request.dtype), lengths)

    residual = tokens.astype(jnp.float32)
    squares = all_sum(jnp.sum(residual * residual, axis=1), "pool", n_pool)
    normed = (residual * lax.rsqrt(squares / D + epsilon)[:, None] * attn_gain[None, :]).astype(
        jnp.bfloat16
    )
    by_slot = gather_rows(normed, CS, n_cs, row_of_slot)
    qkv_part = jnp.einsum(
        "rf,fgc->rgc", by_slot, w_qkv, preferred_element_type=jnp.float32
    ).reshape(rows_total, -1)
    qkv_part, kv_cache = lax.optimization_barrier((qkv_part, kv_cache))
    summed = scatter_sum(qkv_part.reshape(n_pool, per_owner, -1), "pool", n_pool)
    rotated = rope_rows(summed, positions, per_group, HD)
    attended = attend(rotated, kv_cache, positions, per_group, HD)
    by_row = gather_rows(attended, "pool", n_pool, slot_of_row)
    out_part = jnp.dot(by_row, w_out, preferred_element_type=jnp.float32)
    cs_index = lax.axis_index(CS)
    out_part = lax.dynamic_update_slice_in_dim(
        out_part,
        lax.dynamic_slice_in_dim(out_part, cs_index * rows_here, rows_here, 0) + residual,
        cs_index * rows_here,
        0,
    )
    resid_all = all_sum_cs(out_part)
    residual = lax.dynamic_slice_in_dim(resid_all, cs_index * rows_here, rows_here, 0)

    squares_mid = all_sum(jnp.sum(resid_all * resid_all, axis=1), "pool", n_pool)
    ffn_all = (
        resid_all * lax.rsqrt(squares_mid / D + epsilon)[:, None] * ffn_gain[None, :]
    ).astype(jnp.bfloat16)
    both = scatter_matmul(ffn_all, (w_gate, w_up), "pool", n_pool)
    chunk = w_gate.shape[1] // n_pool
    gate_total = both[:, :chunk]
    up_total = both[:, chunk:]
    hidden = (jax.nn.silu(gate_total) * up_total).astype(jnp.bfloat16)
    down_part = gather_matmul(hidden, w_down, "pool", n_pool)
    return residual + scatter_sum_cs(down_part.reshape(n_cs, rows_here, -1))


def solution(mesh):
    return jax.shard_map(
        local,
        mesh=mesh,
        in_specs=(
            P(("groups", "col", "side"), "pool"),
            P("pool"),
            P("pool", ("col", "side"), None),
            P(("col", "side"), "pool"),
            P("pool"),
            P("pool", ("col", "side")),
            P("pool", ("col", "side")),
            P(("col", "side"), "pool"),
            P(("groups", "pool"), None, None, ("col", "side"), None),
            P("groups"),
            P("groups"),
            P("groups"),
        ),
        out_specs=P(("groups", "col", "side"), "pool"),
        check_vma=False,
    )
```

```python
import math

import jax
import jax.numpy as jnp
from jax import lax
from jax.sharding import PartitionSpec as P

D = 8192
H = 64
KVH = 8
HD = 128


epsilon = 1e-05
rope_base = 500000.0
CS = ("col", "side")


def rotate(heads_in, positions):
    half_width = heads_in.shape[-1] // 2
    frequency = 1.0 / rope_base ** (
        jnp.arange(half_width, dtype=jnp.float32) * 2.0 / heads_in.shape[-1]
    )
    angles = positions.astype(jnp.float32)[:, None] * frequency[None, :]
    cosine_part = jnp.cos(angles)[:, None, :]
    sine_part = jnp.sin(angles)[:, None, :]
    first_half = heads_in[..., :half_width]
    second_half = heads_in[..., half_width:]
    return jnp.concatenate(
        [
            first_half * cosine_part - second_half * sine_part,
            second_half * cosine_part + first_half * sine_part,
        ],
        axis=-1,
    )


def rope_rows(qkv_sum, positions, per_group, head_dim):
    row_count = qkv_sum.shape[0]
    shaped = qkv_sum.reshape(row_count, -1, per_group + 2, head_dim)
    group_count = shaped.shape[1]
    turned = rotate(
        shaped[:, :, : per_group + 1].reshape(row_count, group_count * (per_group + 1), head_dim),
        positions,
    )
    turned = turned.reshape(row_count, group_count, per_group + 1, head_dim)
    return (
        jnp.concatenate([turned, shaped[:, :, per_group + 1 :]], axis=2)
        .reshape(row_count, -1)
        .astype(jnp.bfloat16)
    )


def attend(qkv_rot, kv_block, seen_count, per_group, head_dim):
    slot_count = qkv_rot.shape[0]
    cache_keys = kv_block[:, :, 0]
    values_all = kv_block[:, :, 1]
    shaped = qkv_rot.reshape(slot_count, cache_keys.shape[2], per_group + 2, head_dim)
    queries = shaped[:, :, :per_group]
    own_key = shaped[:, :, per_group]
    own_value = shaped[:, :, per_group + 1]
    score_scale = 1.0 / math.sqrt(head_dim)
    scores = (
        jnp.einsum("sgqd,stgd->sgqt", queries, cache_keys, preferred_element_type=jnp.float32)
        * score_scale
    )
    own_score = (
        jnp.einsum("sgqd,sgd->sgq", queries, own_key, preferred_element_type=jnp.float32)
        * score_scale
    )
    live_mask = (jnp.arange(cache_keys.shape[1], dtype=jnp.int32)[None, :] < seen_count[:, None])[
        :, None, None, :
    ]
    peak_score = jnp.maximum(jnp.max(jnp.where(live_mask, scores, -jnp.inf), axis=-1), own_score)
    weights = jnp.where(live_mask, jnp.exp(scores - peak_score[..., None]), 0.0)
    own_weight = jnp.exp(own_score - peak_score)
    denominator = jnp.sum(weights, axis=-1) + own_weight
    prob_weights = (weights / denominator[..., None]).astype(jnp.bfloat16)
    own_prob = (own_weight / denominator).astype(jnp.bfloat16)
    mixture = jnp.einsum(
        "sgqt,stgd->sgqd", prob_weights, values_all, preferred_element_type=jnp.float32
    )
    mixture = (
        mixture
        + own_prob.astype(jnp.float32)[..., None] * own_value.astype(jnp.float32)[:, :, None, :]
    )
    return mixture.reshape(slot_count, -1).astype(jnp.bfloat16)


def send_order(n):
    return sorted(range(1, n), key=lambda k: -min(k, n - k))


def shift_pairs(n, k):
    return [(i, (i + k) % n) for i in range(n)]


def gather_rows(x, axis, n, want):
    idx = lax.axis_index(axis)
    per = x.shape[0]
    sent = {k: lax.ppermute(x, axis, shift_pairs(n, k)) for k in send_order(n)}
    stacked = jnp.concatenate([x] + [sent[k] for k in range(1, n)], axis=0)
    arrival = ((idx - want // per) % n) * per + want % per
    chooser = (arrival[:, None] == jnp.arange(n * per, dtype=arrival.dtype)[None, :]).astype(x.dtype)
    return jnp.dot(chooser, stacked, preferred_element_type=jnp.float32).astype(x.dtype)


def pick(keys, wanted, values):
    hit = keys[None, :] == wanted[:, None]
    return jnp.sum(jnp.where(hit, values[None, :], 0), axis=1)


def scatter_sum(blocks, axis, n):
    idx = lax.axis_index(axis)
    total = jnp.take(blocks, idx, axis=0).astype(jnp.float32)
    sent = {
        k: lax.ppermute(jnp.take(blocks, (idx + k) % n, axis=0), axis, shift_pairs(n, k))
        for k in send_order(n)
    }
    for k in reversed(send_order(n)):
        total = total + sent[k].astype(jnp.float32)
    return total


def scatter_sum_cs(blocks):
    n_col = lax.axis_size("col")
    n_side = lax.axis_size("side")
    shaped = blocks.reshape((n_col, n_side) + blocks.shape[1:])
    per_col = scatter_sum(jnp.swapaxes(shaped, 0, 1), "side", n_side)
    return scatter_sum(per_col, "col", n_col)


def all_sum_cs(parts):
    n_col = lax.axis_size("col")
    n_side = lax.axis_size("side")
    side = lax.axis_index("side")
    mine = scatter_sum(parts.reshape((n_side, -1) + parts.shape[1:]), "side", n_side)
    mine = all_sum(mine, "col", n_col)
    got = [mine] + [lax.ppermute(mine, "side", shift_pairs(n_side, k)) for k in range(1, n_side)]
    ordered = [lax.select_n((side - j) % n_side, *got) for j in range(n_side)]
    return jnp.stack(ordered).reshape(parts.shape)


def all_sum(x, axis, n):
    total = x
    for k in range(1, n):
        total = total + lax.ppermute(x, axis, shift_pairs(n, k))
    return total


def scatter_matmul(x, weights, axis, n):
    idx = lax.axis_index(axis)
    chunk = weights[0].shape[1] // n

    def block(j):
        parts = [
            jnp.dot(
                x,
                lax.dynamic_slice_in_dim(w, j * chunk, chunk, 1),
                preferred_element_type=jnp.float32,
            ).astype(jnp.bfloat16)
            for w in weights
        ]
        return jnp.concatenate(parts, axis=1)

    order = send_order(n)
    pieces = [block((idx + k) % n) for k in order]
    pieces, x = lax.optimization_barrier((pieces, x))
    sent = {k: lax.ppermute(piece, axis, shift_pairs(n, k)) for k, piece in zip(order, pieces)}
    total = None
    for k in reversed(order):
        got = sent[k].astype(jnp.float32)
        total = got if total is None else total + got
    own = block(idx).astype(jnp.float32)
    return own if total is None else own + total


def gather_matmul(x, w, axis, n):
    idx = lax.axis_index(axis)
    chunk = x.shape[1]
    acc = jnp.dot(
        x, lax.dynamic_slice_in_dim(w, idx * chunk, chunk, 0), preferred_element_type=jnp.float32
    )
    sent = {k: lax.ppermute(x, axis, shift_pairs(n, k)) for k in send_order(n)}
    for k in reversed(send_order(n)):
        rows = lax.dynamic_slice_in_dim(w, ((idx - k) % n) * chunk, chunk, 0)
        acc = acc + jnp.dot(sent[k], rows, preferred_element_type=jnp.float32)
    return acc


def local(
    tokens,
    attn_gain,
    w_qkv,
    w_out,
    ffn_gain,
    w_gate,
    w_up,
    w_down,
    kv_cache,
    lengths,
    request_slot,
    row_request,
):
    n_pool = lax.axis_size("pool")
    n_cs = lax.axis_size(CS)
    pool_index = lax.axis_index("pool")
    per_owner = kv_cache.shape[0]
    per_group = H // KVH
    rows_here = tokens.shape[0]
    rows_total = rows_here * n_cs
    my_start = pool_index * per_owner
    every = jnp.arange(rows_total, dtype=row_request.dtype)
    slot_of_row = pick(every, row_request, request_slot)
    row_of_slot = pick(slot_of_row, every, every)
    positions = pick(request_slot, my_start + jnp.arange(per_owner, dtype=row_request.dtype), lengths)

    residual = tokens.astype(jnp.float32)
    squares = all_sum(jnp.sum(residual * residual, axis=1), "pool", n_pool)
    normed = (residual * lax.rsqrt(squares / D + epsilon)[:, None] * attn_gain[None, :]).astype(
        jnp.bfloat16
    )
    by_slot = gather_rows(normed, CS, n_cs, row_of_slot)
    qkv_part = jnp.einsum(
        "rf,fgc->rgc", by_slot, w_qkv, preferred_element_type=jnp.float32
    ).reshape(rows_total, -1)
    qkv_part, kv_cache = lax.optimization_barrier((qkv_part, kv_cache))
    summed = scatter_sum(qkv_part.reshape(n_pool, per_owner, -1), "pool", n_pool)
    rotated = rope_rows(summed, positions, per_group, HD)
    attended = attend(rotated, kv_cache, positions, per_group, HD)
    by_row = gather_rows(attended, "pool", n_pool, slot_of_row)
    out_part = jnp.dot(by_row, w_out, preferred_element_type=jnp.float32)
    cs_index = lax.axis_index(CS)
    out_part = lax.dynamic_update_slice_in_dim(
        out_part,
        lax.dynamic_slice_in_dim(out_part, cs_index * rows_here, rows_here, 0) + residual,
        cs_index * rows_here,
        0,
    )
    resid_all = all_sum_cs(out_part)
    residual = lax.dynamic_slice_in_dim(resid_all, cs_index * rows_here, rows_here, 0)

    squares_mid = all_sum(jnp.sum(resid_all * resid_all, axis=1), "pool", n_pool)
    ffn_all = (
        resid_all * lax.rsqrt(squares_mid / D + epsilon)[:, None] * ffn_gain[None, :]
    ).astype(jnp.bfloat16)
    both = scatter_matmul(ffn_all, (w_gate, w_up), "pool", n_pool)
    chunk = w_gate.shape[1] // n_pool
    gate_total = both[:, :chunk]
    up_total = both[:, chunk:]
    hidden = (jax.nn.silu(gate_total) * up_total).astype(jnp.bfloat16)
    down_part = gather_matmul(hidden, w_down, "pool", n_pool)
    return residual + scatter_sum_cs(down_part.reshape(n_cs, rows_here, -1))


def solution(mesh):
    return jax.shard_map(
        local,
        mesh=mesh,
        in_specs=(
            P(("groups", "col", "side"), "pool"),
            P("pool"),
            P("pool", ("col", "side"), None),
            P(("col", "side"), "pool"),
            P("pool"),
            P("pool", ("col", "side")),
            P("pool", ("col", "side")),
            P(("col", "side"), "pool"),
            P(("groups", "pool"), None, None, ("col", "side"), None),
            P("groups"),
            P("groups"),
            P("groups"),
        ),
        out_specs=P(("groups", "col", "side"), "pool"),
        check_vma=False,
    )
```
